32 devices in a mesh: tok: 2 (over x), voc: 4 (over y, core), wid: 4 (over z).
Axes of the slice: x: 2, y: 2, z: 4, core: 2. Of those that a mesh axis runs over, the one named last changes fastest.
Arguments:
- hidden: bfloat16 [512, 8192], P('tok', 'wid'), may hold values from -1500 to 1500
- proj: bfloat16 [3584, 8192], P('voc', 'wid'), may hold values from -0.0625 to 0.0625
- table: bfloat16 [19456, 3584], P(('voc', 'wid'), 'tok'), may hold values from -10 to 10
- targets: int32 [512], P('tok'), may hold values from 0 to 19455
- valid: int32 [512], P('tok'), may hold values from 0 to 1, as said below
Outputs:
- grad_proj: float32 [3584, 8192], P('voc', 'wid')
- loss: float32 [], replicated
The draws below stay inside these ranges and needn't reach their ends.
Inputs may be any that keep to these rules, and one draw needn't show every extreme that they name: `valid`: position 0 is always scored.
All inputs are finite; a program needn't handle non-finite values.
Results may differ from the reference program's by a relative error of at most 0.008.
Values may be sent and summed in bfloat16 or wider, within the bound.
No kernel may reach another device: no remote copies, remote signals or barrier semaphores. Data moves between devices by JAX's collectives and lax.ppermute only.
A program may use at most 128 MiB of HBM per device.

```python
import math
import jax
import jax.numpy as jnp
from jax import lax

DIN = 8192
DOUT = 3584
VB = 1216
TOKENS = 512
VOCAB = 19456


def draw_hidden(key, part):
    key_base = jax.random.fold_in(key, 31)
    key_pick = jax.random.fold_in(key, 32)
    key_size = jax.random.fold_in(key, 33)
    base_part = jnp.clip(jax.random.normal(key_base, (TOKENS, DIN), jnp.float32), -6.0, 6.0)
    position = jnp.arange(TOKENS, dtype=jnp.int32)
    rolled = jax.random.randint(key_pick, (TOKENS,), 0, 64)
    strong = (rolled == 0) | (position == TOKENS // 2)
    boost = 600.0 / math.sqrt(DOUT) * jnp.exp(jax.random.uniform(key_size, (TOKENS,), jnp.float32, 0.0, math.log(4.0)))
    factor = jnp.where(strong, boost, 1.0)
    return jnp.clip(base_part * factor[:, None], -1500.0, 1500.0).astype(jnp.bfloat16)


def draw_table(key, part):
    key_base = jax.random.fold_in(key, 11)
    normal_part = jnp.clip(jax.random.normal(key_base, (VOCAB, DOUT), jnp.float32), -4.0, 4.0) * 0.05
    return normal_part.astype(jnp.bfloat16)


def draw_valid(key, part):
    position = jnp.arange(TOKENS, dtype=jnp.int32)
    chance = 250 + 600 * position // TOKENS
    rolled = jax.random.randint(jax.random.fold_in(key, 21), (TOKENS,), 0, 1000)
    scored = jnp.where(rolled < chance, 1, 0)
    scored = jnp.where(position == 0, 1, scored)
    return scored.astype(jnp.int32)


def with_ends(drawn, own_key, smallest, top_value):
    spot = [jax.random.randint(jax.random.fold_in(own_key, axis), (), 0, length) for axis, length in enumerate(drawn.shape)]
    main_axis = drawn.shape.index(max(drawn.shape))
    neighbour = spot[:main_axis] + [(spot[main_axis] + 1) % drawn.shape[main_axis]] + spot[main_axis + 1:]
    return drawn.at[tuple(spot)].set(smallest).at[tuple(neighbour)].set(top_value)


def block_scale(key, shape, pieces, least, high):
    level, own = 1.0, jax.random.fold_in(key, 6)
    for axis_at, parts in pieces:
        heights = jnp.exp(jax.random.uniform(jax.random.fold_in(own, axis_at), (parts,), jnp.float32, least / len(pieces), high / len(pieces)))
        level = level * jnp.repeat(heights, shape[axis_at] // parts).reshape([-1 if axis == axis_at else 1 for axis in range(len(shape))])
    return level


def bell_draw(own_key, shape, spread, bound, cuts=(), held_as=jnp.bfloat16):
    level = block_scale(own_key, shape, cuts, -0.22, 0.18) if cuts else 1.0
    result = jax.random.normal(own_key, shape, jnp.float32) * spread * level
    return jnp.minimum(jnp.maximum(result, -bound), bound).astype(held_as)


def setup_inputs(seed: int = 0) -> dict:
    key_of = jax.random.split(jax.random.key(seed), 6)
    hidden = draw_hidden(jax.random.fold_in(key_of[5], 71), 0)
    proj = bell_draw(key_of[1], (DOUT, DIN), DIN ** -0.5, 0.0625, ((0, 4), (1, 4)))
    table = draw_table(jax.random.fold_in(key_of[5], 71), 0)
    targets = with_ends(jax.random.randint(key_of[3], (TOKENS,), 0, VOCAB), jax.random.fold_in(key_of[3], 1), 0, VOCAB - 1).astype(jnp.int32)
    valid = draw_valid(jax.random.fold_in(key_of[5], 71), 0)
    return dict(hidden=hidden, proj=proj, table=table, targets=targets, valid=valid)


def reference(hidden, proj, table, targets, valid):
    projected = lax.dot_general(hidden, proj, (((1,), (1,)), ((), ())), preferred_element_type=jnp.float32).astype(jnp.bfloat16)
    count_blocks = VOCAB // VB
    blocks = table.reshape(count_blocks, VB, DOUT)

    def scores(block_rows):
        return jnp.dot(projected, block_rows.T, preferred_element_type=jnp.float32)

    logits = lax.map(scores, blocks)
    row_peak = jnp.max(logits, axis=(0, 2))
    row_total = jnp.sum(jnp.exp(logits - row_peak[None, :, None]), axis=(0, 2))
    log_total = row_peak + jnp.log(row_total)
    block_of = (targets // VB).astype(jnp.int32)
    inside = (targets % VB).astype(jnp.int32)
    position = jnp.arange(TOKENS, dtype=jnp.int32)
    picked = logits[block_of, position, inside]
    weight = valid.astype(jnp.float32)
    loss = jnp.sum(weight * (log_total - picked)) / jnp.sum(weight)
    softened = weight[None, :, None] * jnp.exp(logits - log_total[None, :, None])
    softened = softened.at[block_of, position, inside].add(-weight)
    dlogits = softened.astype(jnp.bfloat16)

    def accumulate(running, entries):
        piece_grad, block_rows = entries
        return running + jnp.dot(piece_grad, block_rows, preferred_element_type=jnp.float32), None

    grad_rows, _ = lax.scan(accumulate, jnp.zeros((TOKENS, DOUT), jnp.float32), (dlogits, blocks))
    grad_proj = jnp.dot(grad_rows.astype(jnp.bfloat16).T, hidden, preferred_element_type=jnp.float32)
    return grad_proj, loss
```

```python
import jax
import jax.numpy as jnp
from jax import lax
from jax.sharding import PartitionSpec as P


def tok_pieces(x, n_tok):
    pieces = [x]
    for k in range(1, n_tok):
        perm = [(i, (i + k) % n_tok) for i in range(n_tok)]
        pieces.append(lax.ppermute(x, "tok", perm))
    return pieces


def on_device(hidden, proj, table, targets, valid):
    tok_rows = hidden.shape[0]
    block_rows = table.shape[0]
    n_tok = lax.axis_size("tok")
    t = lax.axis_index("tok")
    d_cols = table.shape[1]

    table_pieces = tok_pieces(table, n_tok)
    if n_tok == 2:
        hidden_other = lax.ppermute(hidden, "tok", [(0, 1), (1, 0)])

    partial_value = lax.dot_general(
        hidden, proj, (((1,), (1,)), ((), ())), preferred_element_type=jnp.float32
    )
    summed = lax.psum(partial_value, "wid")
    projected = lax.all_gather(summed.astype(jnp.bfloat16), "voc", axis=1, tiled=True)

    logits = None
    for k, piece in enumerate(table_pieces):
        cols = lax.dynamic_slice_in_dim(projected, ((t - k) % n_tok) * d_cols, d_cols, axis=1)
        part = lax.dot_general(
            cols, piece, (((1,), (1,)), ((), ())), preferred_element_type=jnp.float32
        )
        logits = part if logits is None else logits + part

    block_base = (lax.axis_index("voc") * lax.axis_size("wid") + lax.axis_index("wid")) * block_rows
    local_ids = targets - block_base
    is_target = local_ids[:, None] == lax.broadcasted_iota(jnp.int32, (tok_rows, block_rows), 1)
    picked_here = jnp.sum(jnp.where(is_target, logits, 0.0), axis=1)
    peak_here = jnp.max(logits, axis=1)
    exp_here = jnp.sum(jnp.exp(logits - peak_here[:, None]), axis=1)
    weight = valid.astype(jnp.float32)

    stats = jnp.stack([peak_here, exp_here, picked_here, weight])
    gathered = lax.all_gather(stats, ("tok", "voc", "wid"))
    gathered = gathered.reshape(n_tok, -1, 4, tok_rows)
    peaks = gathered[:, :, 0]
    row_peak_all = jnp.max(peaks, axis=1)
    row_total_all = jnp.sum(gathered[:, :, 1] * jnp.exp(peaks - row_peak_all[:, None]), axis=1)
    log_total_all = row_peak_all + jnp.log(row_total_all)
    picked_all = jnp.sum(gathered[:, :, 2], axis=1)
    weight_all = gathered[:, 0, 3]
    loss = jnp.sum(weight_all * (log_total_all - picked_all)) / jnp.sum(weight_all)
    log_total = lax.dynamic_index_in_dim(log_total_all, t, axis=0, keepdims=False)

    dlogits = (
        weight[:, None] * (jnp.exp(logits - log_total[:, None]) - is_target.astype(jnp.float32))
    ).astype(jnp.bfloat16)

    full_rows = jnp.zeros((d_cols * n_tok, tok_rows), jnp.float32)
    for k, piece in enumerate(table_pieces):
        part = lax.dot_general(
            piece, dlogits, (((0,), (1,)), ((), ())), preferred_element_type=jnp.float32
        )
        full_rows = lax.dynamic_update_slice_in_dim(full_rows, part, ((t - k) % n_tok) * d_cols, axis=0)
    reduced = lax.psum_scatter(full_rows, "voc", scatter_dimension=0, tiled=True)
    grad_rows_t = lax.psum(reduced, "wid").astype(jnp.bfloat16)

    if n_tok == 2:
        grad_other = lax.ppermute(grad_rows_t, "tok", [(0, 1), (1, 0)])
        first = t == 0
        grad_all = jnp.where(
            first,
            jnp.concatenate([grad_rows_t, grad_other], axis=1),
            jnp.concatenate([grad_other, grad_rows_t], axis=1),
        )
        hidden_all = jnp.where(
            first,
            jnp.concatenate([hidden, hidden_other], axis=0),
            jnp.concatenate([hidden_other, hidden], axis=0),
        )
        grad_proj = jnp.dot(grad_all, hidden_all, preferred_element_type=jnp.float32)
    else:
        grad_all = lax.all_gather(grad_rows_t, "tok", axis=1, tiled=True)
        hidden_all = lax.all_gather(hidden, "tok", axis=0, tiled=True)
        grad_proj = jnp.dot(grad_all, hidden_all, preferred_element_type=jnp.float32)
    return (grad_proj, loss)


def solution(mesh):
    return jax.shard_map(
        on_device,
        mesh=mesh,
        in_specs=(P("tok", "wid"), P("voc", "wid"), P(("voc", "wid"), "tok"), P("tok"), P("tok")),
        out_specs=(P("voc", "wid"), P()),
        check_vma=False,
    )
```

```python
import jax
import jax.numpy as jnp
from jax import lax
from jax.sharding import PartitionSpec as P


def tok_pieces(x, n_tok):
    pieces = [x]
    for k in range(1, n_tok):
        perm = [(i, (i + k) % n_tok) for i in range(n_tok)]
        pieces.append(lax.ppermute(x, "tok", perm))
    return pieces


def combine(a, b):
    peak = jnp.maximum(a[0], b[0])
    total = a[1] * jnp.exp(a[0] - peak) + b[1] * jnp.exp(b[0] - peak)
    return jnp.stack([peak, total, a[2] + b[2]])


def butterfly(stats, axes):
    for ax in axes:
        n = lax.axis_size(ax)
        if n & (n - 1):
            gathered = lax.all_gather(stats, ax)
            out = gathered[0]
            for i in range(1, n):
                out = combine(out, gathered[i])
            stats = out
            continue
        b = 1
        while b < n:
            other = lax.ppermute(stats, ax, [(i, i ^ b) for i in range(n)])
            stats = combine(stats, other)
            b *= 2
    return stats


def tree_sum(x, ax):
    n = lax.axis_size(ax)
    if n & (n - 1):
        return lax.psum(x, ax)
    b = 1
    while b < n:
        x = x + lax.ppermute(x, ax, [(i, i ^ b) for i in range(n)])
        b *= 2
    return x


def on_device(hidden, proj, table, targets, valid):
    tok_rows = hidden.shape[0]
    block_rows = table.shape[0]
    n_tok = lax.axis_size("tok")
    t = lax.axis_index("tok")
    d_cols = table.shape[1]

    table_pieces = tok_pieces(table, n_tok)
    if n_tok == 2:
        hidden_other = lax.ppermute(hidden, "tok", [(0, 1), (1, 0)])

    partial_value = lax.dot_general(
        hidden, proj, (((1,), (1,)), ((), ())), preferred_element_type=jnp.float32
    )
    summed = lax.psum(partial_value, "wid")
    projected = lax.all_gather(summed.astype(jnp.bfloat16), "voc", axis=1, tiled=True)

    logits = None
    for k, piece in enumerate(table_pieces):
        cols = lax.dynamic_slice_in_dim(projected, ((t - k) % n_tok) * d_cols, d_cols, axis=1)
        part = lax.dot_general(
            cols, piece, (((1,), (1,)), ((), ())), preferred_element_type=jnp.float32
        )
        logits = part if logits is None else logits + part

    block_base = (lax.axis_index("voc") * lax.axis_size("wid") + lax.axis_index("wid")) * block_rows
    local_ids = targets - block_base
    is_target = local_ids[:, None] == lax.broadcasted_iota(jnp.int32, (tok_rows, block_rows), 1)
    picked_here = jnp.sum(jnp.where(is_target, logits, 0.0), axis=1)
    peak_here = jnp.max(logits, axis=1)
    exp_here = jnp.sum(jnp.exp(logits - peak_here[:, None]), axis=1)
    weight = valid.astype(jnp.float32)

    stats = jnp.stack([peak_here, exp_here, picked_here])
    stats = butterfly(stats, ("voc", "wid"))
    log_total = stats[0] + jnp.log(stats[1])
    picked = stats[2]
    sums = jnp.stack([jnp.sum(weight * (log_total - picked)), jnp.sum(weight)])
    sums = tree_sum(sums, "tok")
    loss = sums[0] / sums[1]

    dlogits = (
        weight[:, None] * (jnp.exp(logits - log_total[:, None]) - is_target.astype(jnp.float32))
    ).astype(jnp.bfloat16)

    full_rows = jnp.zeros((d_cols * n_tok, tok_rows), jnp.float32)
    for k, piece in enumerate(table_pieces):
        part = lax.dot_general(
            piece, dlogits, (((0,), (1,)), ((), ())), preferred_element_type=jnp.float32
        )
        full_rows = lax.dynamic_update_slice_in_dim(full_rows, part, ((t - k) % n_tok) * d_cols, axis=0)
    reduced = lax.psum_scatter(full_rows, "voc", scatter_dimension=0, tiled=True)
    grad_rows_t = lax.psum(reduced, "wid").astype(jnp.bfloat16)

    if n_tok == 2:
        grad_other = lax.ppermute(grad_rows_t, "tok", [(0, 1), (1, 0)])
        first = t == 0
        grad_all = jnp.where(
            first,
            jnp.concatenate([grad_rows_t, grad_other], axis=1),
            jnp.concatenate([grad_other, grad_rows_t], axis=1),
        )
        hidden_all = jnp.where(
            first,
            jnp.concatenate([hidden, hidden_other], axis=0),
            jnp.concatenate([hidden_other, hidden], axis=0),
        )
        grad_proj = jnp.dot(grad_all, hidden_all, preferred_element_type=jnp.float32)
    else:
        grad_all = lax.all_gather(grad_rows_t, "tok", axis=1, tiled=True)
        hidden_all = lax.all_gather(hidden, "tok", axis=0, tiled=True)
        grad_proj = jnp.dot(grad_all, hidden_all, preferred_element_type=jnp.float32)
    return (grad_proj, loss)


def solution(mesh):
    return jax.shard_map(
        on_device,
        mesh=mesh,
        in_specs=(P("tok", "wid"), P("voc", "wid"), P(("voc", "wid"), "tok"), P("tok"), P("tok")),
        out_specs=(P("voc", "wid"), P()),
        check_vma=False,
    )
```

```python
import jax
import jax.numpy as jnp
from jax import lax
from jax.sharding import PartitionSpec as P


def tok_pieces(x, n_tok):
    pieces = [x]
    for k in range(1, n_tok):
        perm = [(i, (i + k) % n_tok) for i in range(n_tok)]
        pieces.append(lax.ppermute(x, "tok", perm))
    return pieces


def combine(a, b):
    peak = jnp.maximum(a[0], b[0])
    total = a[1] * jnp.exp(a[0] - peak) + b[1] * jnp.exp(b[0] - peak)
    return jnp.stack([peak, total, a[2] + b[2]])


def butterfly(stats, axes):
    for ax in axes:
        n = lax.axis_size(ax)
        if n & (n - 1):
            gathered = lax.all_gather(stats, ax)
            out = gathered[0]
            for i in range(1, n):
                out = combine(out, gathered[i])
            stats = out
            continue
        b = 1
        while b < n:
            other = lax.ppermute(stats, ax, [(i, i ^ b) for i in range(n)])
            stats = combine(stats, other)
            b *= 2
    return stats


def tree_sum(x, ax):
    n = lax.axis_size(ax)
    if n & (n - 1):
        return lax.psum(x, ax)
    b = 1
    while b < n:
        x = x + lax.ppermute(x, ax, [(i, i ^ b) for i in range(n)])
        b *= 2
    return x


def is_pow2(n):
    return n & (n - 1) == 0


def halving_scatter(x, axes):
    for ax in axes:
        n = lax.axis_size(ax)
        i = lax.axis_index(ax)
        b = 1
        while b < n:
            m = x.shape[0]
            x = x.reshape((m // 2, 2) + x.shape[1:])
            bit = (i // b) % 2
            keep = lax.dynamic_index_in_dim(x, bit, axis=1, keepdims=False)
            send = lax.dynamic_index_in_dim(x, 1 - bit, axis=1, keepdims=False)
            x = keep + lax.ppermute(send, ax, [(k, k ^ b) for k in range(n)])
            b *= 2
        x = x[0]
    return x


def doubling_gather(x, ax):
    n = lax.axis_size(ax)
    i = lax.axis_index(ax)
    b = n // 2
    lead = 0
    while b >= 1:
        other = lax.ppermute(x, ax, [(k, k ^ b) for k in range(n)])
        bit = (i // b) % 2
        x = jnp.where(bit == 0, jnp.stack([x, other], axis=lead), jnp.stack([other, x], axis=lead))
        lead += 1
        b //= 2
    return x.reshape((n,) + x.shape[lead:])


def on_device(hidden, proj, table, targets, valid):
    tok_rows = hidden.shape[0]
    block_rows = table.shape[0]
    n_tok = lax.axis_size("tok")
    t = lax.axis_index("tok")
    d_cols = table.shape[1]

    table_pieces = tok_pieces(table, n_tok)
    if n_tok == 2:
        hidden_other = lax.ppermute(hidden, "tok", [(0, 1), (1, 0)])

    partial_value = lax.dot_general(
        hidden, proj, (((1,), (1,)), ((), ())), preferred_element_type=jnp.float32
    )
    summed = lax.psum(partial_value, "wid")
    projected = lax.all_gather(summed.astype(jnp.bfloat16), "voc", axis=1, tiled=True)

    logits = None
    for k, piece in enumerate(table_pieces):
        cols = lax.dynamic_slice_in_dim(projected, ((t - k) % n_tok) * d_cols, d_cols, axis=1)
        part = lax.dot_general(
            cols, piece, (((1,), (1,)), ((), ())), preferred_element_type=jnp.float32
        )
        logits = part if logits is None else logits + part

    block_base = (lax.axis_index("voc") * lax.axis_size("wid") + lax.axis_index("wid")) * block_rows
    local_ids = targets - block_base
    is_target = local_ids[:, None] == lax.broadcasted_iota(jnp.int32, (tok_rows, block_rows), 1)
    picked_here = jnp.sum(jnp.where(is_target, logits, 0.0), axis=1)
    peak_here = jnp.max(logits, axis=1)
    exp_here = jnp.sum(jnp.exp(logits - peak_here[:, None]), axis=1)
    weight = valid.astype(jnp.float32)

    stats = jnp.stack([peak_here, exp_here, picked_here])
    stats = butterfly(stats, ("voc", "wid"))
    log_total = stats[0] + jnp.log(stats[1])
    picked = stats[2]
    sums = jnp.stack([jnp.sum(weight * (log_total - picked)), jnp.sum(weight)])
    sums = tree_sum(sums, "tok")
    loss = sums[0] / sums[1]

    dlogits = (
        weight[:, None] * (jnp.exp(logits - log_total[:, None]) - is_target.astype(jnp.float32))
    ).astype(jnp.bfloat16)

    full_rows = jnp.zeros((d_cols * n_tok, tok_rows), jnp.float32)
    for k, piece in enumerate(table_pieces):
        part = lax.dot_general(
            piece, dlogits, (((0,), (1,)), ((), ())), preferred_element_type=jnp.float32
        )
        full_rows = lax.dynamic_update_slice_in_dim(full_rows, part, ((t - k) % n_tok) * d_cols, axis=0)
    if all(is_pow2(lax.axis_size(ax)) for ax in ("voc", "wid")):
        n_voc, n_wid = lax.axis_size("voc"), lax.axis_size("wid")
        blocks = full_rows.reshape((n_voc, n_wid, -1, tok_rows))
        mine = halving_scatter(blocks, ("voc", "wid")).astype(jnp.bfloat16)
        grad_rows_t = doubling_gather(mine, "wid")
        grad_rows_t = grad_rows_t.reshape((-1, tok_rows))
    else:
        reduced = lax.psum_scatter(full_rows, "voc", scatter_dimension=0, tiled=True)
        grad_rows_t = lax.psum(reduced, "wid").astype(jnp.bfloat16)

    if n_tok == 2:
        grad_other = lax.ppermute(grad_rows_t, "tok", [(0, 1), (1, 0)])
        first = t == 0
        grad_all = jnp.where(
            first,
            jnp.concatenate([grad_rows_t, grad_other], axis=1),
            jnp.concatenate([grad_other, grad_rows_t], axis=1),
        )
        hidden_all = jnp.where(
            first,
            jnp.concatenate([hidden, hidden_other], axis=0),
            jnp.concatenate([hidden_other, hidden], axis=0),
        )
        grad_proj = jnp.dot(grad_all, hidden_all, preferred_element_type=jnp.float32)
    else:
        grad_all = lax.all_gather(grad_rows_t, "tok", axis=1, tiled=True)
        hidden_all = lax.all_gather(hidden, "tok", axis=0, tiled=True)
        grad_proj = jnp.dot(grad_all, hidden_all, preferred_element_type=jnp.float32)
    return (grad_proj, loss)


def solution(mesh):
    return jax.shard_map(
        on_device,
        mesh=mesh,
        in_specs=(P("tok", "wid"), P("voc", "wid"), P(("voc", "wid"), "tok"), P("tok"), P("tok")),
        out_specs=(P("voc", "wid"), P()),
        check_vma=False,
    )
```

```python
import jax
import jax.numpy as jnp
from jax import lax
from jax.sharding import PartitionSpec as P


def tok_pieces(x, n_tok):
    pieces = [x]
    for k in range(1, n_tok):
        perm = [(i, (i + k) % n_tok) for i in range(n_tok)]
        pieces.append(lax.ppermute(x, "tok", perm))
    return pieces


def combine(a, b):
    peak = jnp.maximum(a[0], b[0])
    total = a[1] * jnp.exp(a[0] - peak) + b[1] * jnp.exp(b[0] - peak)
    return jnp.stack([peak, total, a[2] + b[2]])


def butterfly(stats, axes):
    for ax in axes:
        n = lax.axis_size(ax)
        if n & (n - 1):
            gathered = lax.all_gather(stats, ax)
            out = gathered[0]
            for i in range(1, n):
                out = combine(out, gathered[i])
            stats = out
            continue
        b = 1
        while b < n:
            other = lax.ppermute(stats, ax, [(i, i ^ b) for i in range(n)])
            stats = combine(stats, other)
            b *= 2
    return stats


def tree_sum(x, ax):
    n = lax.axis_size(ax)
    if n & (n - 1):
        return lax.psum(x, ax)
    b = 1
    while b < n:
        x = x + lax.ppermute(x, ax, [(i, i ^ b) for i in range(n)])
        b *= 2
    return x


def is_pow2(n):
    return n & (n - 1) == 0


def bit_list(ax, n):
    out = []
    b = 1
    while b < n:
        out.append((ax, b))
        b *= 2
    return out


def halving_steps(x, dims, order):
    dims = list(dims)
    for ax, b in order:
        pos = dims.index((ax, b))
        n = lax.axis_size(ax)
        bit = (lax.axis_index(ax) // b) % 2
        keep = lax.dynamic_index_in_dim(x, bit, axis=pos, keepdims=False)
        send = lax.dynamic_index_in_dim(x, 1 - bit, axis=pos, keepdims=False)
        x = keep + lax.ppermute(send, ax, [(k, k ^ b) for k in range(n)])
        dims.pop(pos)
    return x


def doubling_gather(x, ax):
    n = lax.axis_size(ax)
    i = lax.axis_index(ax)
    b = n // 2
    lead = 0
    while b >= 1:
        other = lax.ppermute(x, ax, [(k, k ^ b) for k in range(n)])
        bit = (i // b) % 2
        x = jnp.where(bit == 0, jnp.stack([x, other], axis=lead), jnp.stack([other, x], axis=lead))
        lead += 1
        b //= 2
    return x.reshape((n,) + x.shape[lead:])


def on_device(hidden, proj, table, targets, valid):
    tok_rows = hidden.shape[0]
    block_rows = table.shape[0]
    n_tok = lax.axis_size("tok")
    t = lax.axis_index("tok")
    d_cols = table.shape[1]

    table_pieces = tok_pieces(table, n_tok)
    if n_tok == 2:
        hidden_other = lax.ppermute(hidden, "tok", [(0, 1), (1, 0)])

    partial_value = lax.dot_general(
        hidden, proj, (((1,), (1,)), ((), ())), preferred_element_type=jnp.float32
    )
    summed = lax.psum(partial_value, "wid")
    projected = lax.all_gather(summed.astype(jnp.bfloat16), "voc", axis=1, tiled=True)

    logits = None
    for k, piece in enumerate(table_pieces):
        cols = lax.dynamic_slice_in_dim(projected, ((t - k) % n_tok) * d_cols, d_cols, axis=1)
        part = lax.dot_general(
            cols, piece, (((1,), (1,)), ((), ())), preferred_element_type=jnp.float32
        )
        logits = part if logits is None else logits + part

    block_base = (lax.axis_index("voc") * lax.axis_size("wid") + lax.axis_index("wid")) * block_rows
    local_ids = targets - block_base
    is_target = local_ids[:, None] == lax.broadcasted_iota(jnp.int32, (tok_rows, block_rows), 1)
    picked_here = jnp.sum(jnp.where(is_target, logits, 0.0), axis=1)
    peak_here = jnp.max(logits, axis=1)
    exp_here = jnp.sum(jnp.exp(logits - peak_here[:, None]), axis=1)
    weight = valid.astype(jnp.float32)

    stats = jnp.stack([peak_here, exp_here, picked_here])
    stats = butterfly(stats, ("voc", "wid"))
    log_total = stats[0] + jnp.log(stats[1])
    picked = stats[2]
    sums = jnp.stack([jnp.sum(weight * (log_total - picked)), jnp.sum(weight)])
    sums = tree_sum(sums, "tok")
    loss = sums[0] / sums[1]

    dlogits = (
        weight[:, None] * (jnp.exp(logits - log_total[:, None]) - is_target.astype(jnp.float32))
    ).astype(jnp.bfloat16)

    parts = []
    for k, piece in enumerate(table_pieces):
        parts.append(
            lax.dot_general(piece, dlogits, (((0,), (1,)), ((), ())), preferred_element_type=jnp.float32)
        )
    if n_tok == 2:
        full_rows = jnp.where(
            t == 0, jnp.concatenate(parts, axis=0), jnp.concatenate(parts[::-1], axis=0)
        )
    else:
        full_rows = jnp.zeros((d_cols * n_tok, tok_rows), jnp.float32)
        for k, part in enumerate(parts):
            full_rows = lax.dynamic_update_slice_in_dim(
                full_rows, part, ((t - k) % n_tok) * d_cols, axis=0
            )
    n_voc, n_wid = lax.axis_size("voc"), lax.axis_size("wid")
    if is_pow2(n_voc) and is_pow2(n_wid) and n_voc > 1 and tok_rows % 2 == 0:
        voc_bits = bit_list("voc", n_voc)
        wid_bits = bit_list("wid", n_wid)
        dims = voc_bits[::-1] + wid_bits[::-1]
        blocks = full_rows.reshape(tuple(2 for _ in dims) + (-1, tok_rows))
        first = voc_bits[0]
        blocks = halving_steps(blocks, dims, [first])
        dims = [d for d in dims if d != first]
        half = tok_rows // 2
        part_a = halving_steps(blocks[..., :half], dims, voc_bits[1:] + wid_bits)
        part_b = halving_steps(blocks[..., half:], dims, wid_bits + voc_bits[1:])
        mine = jnp.concatenate([part_a, part_b], axis=-1).astype(jnp.bfloat16)
        grad_rows_t = doubling_gather(mine, "wid").reshape((-1, tok_rows))
    else:
        reduced = lax.psum_scatter(full_rows, "voc", scatter_dimension=0, tiled=True)
        grad_rows_t = lax.psum(reduced, "wid").astype(jnp.bfloat16)

    if n_tok == 2:
        grad_other = lax.ppermute(grad_rows_t, "tok", [(0, 1), (1, 0)])
        first = t == 0
        grad_all = jnp.where(
            first,
            jnp.concatenate([grad_rows_t, grad_other], axis=1),
            jnp.concatenate([grad_other, grad_rows_t], axis=1),
        )
        hidden_all = jnp.where(
            first,
            jnp.concatenate([hidden, hidden_other], axis=0),
            jnp.concatenate([hidden_other, hidden], axis=0),
        )
        grad_proj = jnp.dot(grad_all, hidden_all, preferred_element_type=jnp.float32)
    else:
        grad_all = lax.all_gather(grad_rows_t, "tok", axis=1, tiled=True)
        hidden_all = lax.all_gather(hidden, "tok", axis=0, tiled=True)
        grad_proj = jnp.dot(grad_all, hidden_all, preferred_element_type=jnp.float32)
    return (grad_proj, loss)


def solution(mesh):
    return jax.shard_map(
        on_device,
        mesh=mesh,
        in_specs=(P("tok", "wid"), P("voc", "wid"), P(("voc", "wid"), "tok"), P("tok"), P("tok")),
        out_specs=(P("voc", "wid"), P()),
        check_vma=False,
    )
```

```python
import jax
import jax.numpy as jnp
from jax import lax
from jax.sharding import PartitionSpec as P


def tok_pieces(x, n_tok):
    pieces = [x]
    for k in range(1, n_tok):
        perm = [(i, (i + k) % n_tok) for i in range(n_tok)]
        pieces.append(lax.ppermute(x, "tok", perm))
    return pieces


def combine(a, b):
    peak = jnp.maximum(a[0], b[0])
    total = a[1] * jnp.exp(a[0] - peak) + b[1] * jnp.exp(b[0] - peak)
    return jnp.stack([peak, total, a[2] + b[2]])


def butterfly(stats, axes):
    for ax in axes:
        n = lax.axis_size(ax)
        if n & (n - 1):
            gathered = lax.all_gather(stats, ax)
            out = gathered[0]
            for i in range(1, n):
                out = combine(out, gathered[i])
            stats = out
            continue
        b = 1
        while b < n:
            other = lax.ppermute(stats, ax, [(i, i ^ b) for i in range(n)])
            stats = combine(stats, other)
            b *= 2
    return stats


def tree_sum(x, ax):
    n = lax.axis_size(ax)
    if n & (n - 1):
        return lax.psum(x, ax)
    b = 1
    while b < n:
        x = x + lax.ppermute(x, ax, [(i, i ^ b) for i in range(n)])
        b *= 2
    return x


def is_pow2(n):
    return n & (n - 1) == 0


def bit_list(ax, n):
    out = []
    b = 1
    while b < n:
        out.append((ax, b))
        b *= 2
    return out


def halving_steps(x, dims, order, bits=None):
    dims = list(dims)
    for ax, b in order:
        pos = dims.index((ax, b))
        n = lax.axis_size(ax)
        bit = (lax.axis_index(ax) // b) % 2 if bits is None else bits[(ax, b)]
        keep = lax.dynamic_index_in_dim(x, bit, axis=pos, keepdims=False)
        send = lax.dynamic_index_in_dim(x, 1 - bit, axis=pos, keepdims=False)
        x = keep + lax.ppermute(send, ax, [(k, k ^ b) for k in range(n)])
        dims.pop(pos)
    return x


def doubling_gather(x, ax):
    n = lax.axis_size(ax)
    i = lax.axis_index(ax)
    b = n // 2
    lead = 0
    while b >= 1:
        other = lax.ppermute(x, ax, [(k, k ^ b) for k in range(n)])
        bit = (i // b) % 2
        x = jnp.where(bit == 0, jnp.stack([x, other], axis=lead), jnp.stack([other, x], axis=lead))
        lead += 1
        b //= 2
    return x.reshape((n,) + x.shape[lead:])


def on_device(hidden, proj, table, targets, valid):
    tok_rows = hidden.shape[0]
    block_rows = table.shape[0]
    n_tok = lax.axis_size("tok")
    t = lax.axis_index("tok")
    d_cols = table.shape[1]

    table_pieces = tok_pieces(table, n_tok)
    if n_tok == 2:
        hidden_other = lax.ppermute(hidden, "tok", [(0, 1), (1, 0)])

    partial_value = lax.dot_general(
        hidden, proj, (((1,), (1,)), ((), ())), preferred_element_type=jnp.float32
    )
    summed = lax.psum(partial_value, "wid")
    projected = lax.all_gather(summed.astype(jnp.bfloat16), "voc", axis=1, tiled=True)

    logits = None
    for k, piece in enumerate(table_pieces):
        cols = lax.dynamic_slice_in_dim(projected, ((t - k) % n_tok) * d_cols, d_cols, axis=1)
        part = lax.dot_general(
            cols, piece, (((1,), (1,)), ((), ())), preferred_element_type=jnp.float32
        )
        logits = part if logits is None else logits + part

    block_base = (lax.axis_index("voc") * lax.axis_size("wid") + lax.axis_index("wid")) * block_rows
    local_ids = targets - block_base
    is_target = local_ids[:, None] == lax.broadcasted_iota(jnp.int32, (tok_rows, block_rows), 1)
    picked_here = jnp.sum(jnp.where(is_target, logits, 0.0), axis=1)
    peak_here = jnp.max(logits, axis=1)
    exp_here = jnp.sum(jnp.exp(logits - peak_here[:, None]), axis=1)
    weight = valid.astype(jnp.float32)

    stats = jnp.stack([peak_here, exp_here, picked_here])
    stats = butterfly(stats, ("voc", "wid"))
    log_total = stats[0] + jnp.log(stats[1])
    picked = stats[2]
    sums = jnp.stack([jnp.sum(weight * (log_total - picked)), jnp.sum(weight)])
    sums = tree_sum(sums, "tok")
    loss = sums[0] / sums[1]

    dlogits = (
        weight[:, None] * (jnp.exp(logits - log_total[:, None]) - is_target.astype(jnp.float32))
    ).astype(jnp.bfloat16)

    n_voc, n_wid = lax.axis_size("voc"), lax.axis_size("wid")
    grad_rows_pos = None
    if (
        n_tok == 2
        and n_voc >= 2
        and is_pow2(n_voc)
        and is_pow2(n_wid)
        and tok_rows % (2 * n_wid) == 0
        and d_cols % (n_voc // 2) == 0
    ):
        per_piece = n_voc // 2
        q_cols = d_cols // per_piece
        stacked = jnp.stack(
            [
                jnp.stack(
                    [
                        jnp.dot(dlogits, piece[:, i * q_cols : (i + 1) * q_cols], preferred_element_type=jnp.float32)
                        for i in range(per_piece)
                    ]
                )
                for piece in table_pieces
            ]
        )
        voc_bits = bit_list("voc", n_voc)
        wid_bits = bit_list("wid", n_wid)
        v = lax.axis_index("voc")
        bits = {key: (v // key[1]) % 2 for key in voc_bits}
        bits[voc_bits[-1]] = ((v // per_piece) % 2) ^ t
        for key in wid_bits:
            bits[key] = (lax.axis_index("wid") // key[1]) % 2
        dims = [voc_bits[-1]] + voc_bits[:-1][::-1] + wid_bits[::-1]
        blocks = stacked.reshape(tuple(2 for _ in dims) + (tok_rows // n_wid, q_cols))
        first = voc_bits[0]
        blocks = halving_steps(blocks, dims, [first], bits)
        dims = [d for d in dims if d != first]
        half = tok_rows // n_wid // 2
        rest_voc = voc_bits[1:]
        part_a = halving_steps(blocks[..., :half, :], dims, rest_voc + wid_bits, bits)
        part_b = halving_steps(blocks[..., half:, :], dims, wid_bits + rest_voc, bits)
        mine = jnp.concatenate([part_a, part_b], axis=0).astype(jnp.bfloat16)
        grad_rows_pos = doubling_gather(mine, "wid").reshape((tok_rows, q_cols))
    else:
        parts = []
        for k, piece in enumerate(table_pieces):
            parts.append(
                lax.dot_general(piece, dlogits, (((0,), (1,)), ((), ())), preferred_element_type=jnp.float32)
            )
        full_rows = jnp.zeros((d_cols * n_tok, tok_rows), jnp.float32)
        for k, part in enumerate(parts):
            full_rows = lax.dynamic_update_slice_in_dim(
                full_rows, part, ((t - k) % n_tok) * d_cols, axis=0
            )
        reduced = lax.psum_scatter(full_rows, "voc", scatter_dimension=0, tiled=True)
        grad_rows_t = lax.psum(reduced, "wid").astype(jnp.bfloat16)

    if grad_rows_pos is not None:
        grad_other = lax.ppermute(grad_rows_pos, "tok", [(0, 1), (1, 0)])
        first = t == 0
        grad_all = jnp.where(
            first,
            jnp.concatenate([grad_rows_pos, grad_other], axis=0),
            jnp.concatenate([grad_other, grad_rows_pos], axis=0),
        )
        hidden_all = jnp.where(
            first,
            jnp.concatenate([hidden, hidden_other], axis=0),
            jnp.concatenate([hidden_other, hidden], axis=0),
        )
        grad_proj = lax.dot_general(
            grad_all, hidden_all, (((0,), (0,)), ((), ())), preferred_element_type=jnp.float32
        )
    elif n_tok == 2:
        grad_other = lax.ppermute(grad_rows_t, "tok", [(0, 1), (1, 0)])
        first = t == 0
        grad_all = jnp.where(
            first,
            jnp.concatenate([grad_rows_t, grad_other], axis=1),
            jnp.concatenate([grad_other, grad_rows_t], axis=1),
        )
        hidden_all = jnp.where(
            first,
            jnp.concatenate([hidden, hidden_other], axis=0),
            jnp.concatenate([hidden_other, hidden], axis=0),
        )
        grad_proj = jnp.dot(grad_all, hidden_all, preferred_element_type=jnp.float32)
    else:
        grad_all = lax.all_gather(grad_rows_t, "tok", axis=1, tiled=True)
        hidden_all = lax.all_gather(hidden, "tok", axis=0, tiled=True)
        grad_proj = jnp.dot(grad_all, hidden_all, preferred_element_type=jnp.float32)
    return (grad_proj, loss)


def solution(mesh):
    return jax.shard_map(
        on_device,
        mesh=mesh,
        in_specs=(P("tok", "wid"), P("voc", "wid"), P(("voc", "wid"), "tok"), P("tok"), P("tok")),
        out_specs=(P("voc", "wid"), P()),
        check_vma=False,
    )
```

```python
import jax
import jax.numpy as jnp
from jax import lax
from jax.sharding import PartitionSpec as P


def tok_pieces(x, n_tok):
    pieces = [x]
    for k in range(1, n_tok):
        perm = [(i, (i + k) % n_tok) for i in range(n_tok)]
        pieces.append(lax.ppermute(x, "tok", perm))
    return pieces


def combine(a, b):
    peak = jnp.maximum(a[0], b[0])
    total = a[1] * jnp.exp(a[0] - peak) + b[1] * jnp.exp(b[0] - peak)
    return jnp.stack([peak, total, a[2] + b[2]])


def butterfly(stats, axes):
    for ax in axes:
        n = lax.axis_size(ax)
        if n & (n - 1):
            gathered = lax.all_gather(stats, ax)
            out = gathered[0]
            for i in range(1, n):
                out = combine(out, gathered[i])
            stats = out
            continue
        b = 1
        while b < n:
            other = lax.ppermute(stats, ax, [(i, i ^ b) for i in range(n)])
            stats = combine(stats, other)
            b *= 2
    return stats


def tree_sum(x, ax):
    n = lax.axis_size(ax)
    if n & (n - 1):
        return lax.psum(x, ax)
    b = 1
    while b < n:
        x = x + lax.ppermute(x, ax, [(i, i ^ b) for i in range(n)])
        b *= 2
    return x


def is_pow2(n):
    return n & (n - 1) == 0


def bit_list(ax, n):
    out = []
    b = 1
    while b < n:
        out.append((ax, b))
        b *= 2
    return out


def halving_steps(x, dims, order, bits=None):
    dims = list(dims)
    for ax, b in order:
        pos = dims.index((ax, b))
        n = lax.axis_size(ax)
        bit = (lax.axis_index(ax) // b) % 2 if bits is None else bits[(ax, b)]
        keep = lax.dynamic_index_in_dim(x, bit, axis=pos, keepdims=False)
        send = lax.dynamic_index_in_dim(x, 1 - bit, axis=pos, keepdims=False)
        x = keep + lax.ppermute(send, ax, [(k, k ^ b) for k in range(n)])
        dims.pop(pos)
    return x


def doubling_gather(x, ax):
    n = lax.axis_size(ax)
    i = lax.axis_index(ax)
    b = n // 2
    lead = 0
    while b >= 1:
        other = lax.ppermute(x, ax, [(k, k ^ b) for k in range(n)])
        bit = (i // b) % 2
        x = jnp.where(bit == 0, jnp.stack([x, other], axis=lead), jnp.stack([other, x], axis=lead))
        lead += 1
        b //= 2
    return x.reshape((n,) + x.shape[lead:])


def on_device(hidden, proj, table, targets, valid):
    tok_rows = hidden.shape[0]
    block_rows = table.shape[0]
    n_tok = lax.axis_size("tok")
    t = lax.axis_index("tok")
    d_cols = table.shape[1]

    table_pieces = tok_pieces(table, n_tok)
    if n_tok == 2:
        hidden_other = lax.ppermute(hidden, "tok", [(0, 1), (1, 0)])

    partial_value = lax.dot_general(
        hidden, proj, (((1,), (1,)), ((), ())), preferred_element_type=jnp.float32
    )
    summed = lax.psum(partial_value, "wid")
    projected = lax.all_gather(summed.astype(jnp.bfloat16), "voc", axis=1, tiled=True)

    logits = None
    for k, piece in enumerate(table_pieces):
        cols = lax.dynamic_slice_in_dim(projected, ((t - k) % n_tok) * d_cols, d_cols, axis=1)
        part = lax.dot_general(
            cols, piece, (((1,), (1,)), ((), ())), preferred_element_type=jnp.float32
        )
        logits = part if logits is None else logits + part

    block_base = (lax.axis_index("voc") * lax.axis_size("wid") + lax.axis_index("wid")) * block_rows
    local_ids = targets - block_base
    is_target = local_ids[:, None] == lax.broadcasted_iota(jnp.int32, (tok_rows, block_rows), 1)
    picked_here = jnp.sum(jnp.where(is_target, logits, 0.0), axis=1)
    peak_here = jnp.max(logits, axis=1)
    exp_here = jnp.sum(jnp.exp(logits - peak_here[:, None]), axis=1)
    weight = valid.astype(jnp.float32)

    stats = jnp.stack([peak_here, exp_here, picked_here])
    stats = butterfly(stats, ("voc", "wid"))
    log_total = stats[0] + jnp.log(stats[1])
    picked = stats[2]
    sums = jnp.stack([jnp.sum(weight * (log_total - picked)), jnp.sum(weight)])
    sums = tree_sum(sums, "tok")
    loss = sums[0] / sums[1]

    dlogits = (
        weight[:, None] * (jnp.exp(logits - log_total[:, None]) - is_target.astype(jnp.float32))
    ).astype(jnp.bfloat16)

    n_voc, n_wid = lax.axis_size("voc"), lax.axis_size("wid")
    grad_rows_pos = None
    grad_path = (
        n_tok == 2
        and n_voc >= 2
        and is_pow2(n_voc)
        and is_pow2(n_wid)
        and tok_rows % (2 * n_wid) == 0
        and d_cols % (n_voc // 2) == 0
    )
    per_piece = 0
    if grad_path:
        per_piece = n_voc // 2
        q_cols = d_cols // per_piece
    if grad_path and per_piece == 2:
        c = lax.axis_index("voc") % 2

        def quarter_dots(sel):
            return jnp.stack(
                [
                    jnp.dot(
                        dlogits,
                        lax.dynamic_slice_in_dim(piece, sel * q_cols, q_cols, axis=1),
                        preferred_element_type=jnp.float32,
                    )
                    for piece in table_pieces
                ]
            )

        sent = quarter_dots(1 - c)
        received = lax.ppermute(sent, "voc", [(k, k ^ 1) for k in range(n_voc)])
        blocks = quarter_dots(c) + received
        voc_bits = bit_list("voc", n_voc)
        wid_bits = bit_list("wid", n_wid)
        v = lax.axis_index("voc")
        bits = {voc_bits[-1]: ((v // per_piece) % 2) ^ t}
        for key in wid_bits:
            bits[key] = (lax.axis_index("wid") // key[1]) % 2
        dims = [voc_bits[-1]] + wid_bits[::-1]
        blocks = blocks.reshape(tuple(2 for _ in dims) + (tok_rows // n_wid, q_cols))
        half = tok_rows // n_wid // 2
        rest_voc = voc_bits[1:]
        part_a = halving_steps(blocks[..., :half, :], dims, rest_voc + wid_bits, bits)
        part_b = halving_steps(blocks[..., half:, :], dims, wid_bits + rest_voc, bits)
        mine = jnp.concatenate([part_a, part_b], axis=0).astype(jnp.bfloat16)
        grad_rows_pos = doubling_gather(mine, "wid").reshape((tok_rows, q_cols))
    elif grad_path:
        stacked = jnp.stack(
            [
                jnp.stack(
                    [
                        jnp.dot(dlogits, piece[:, i * q_cols : (i + 1) * q_cols], preferred_element_type=jnp.float32)
                        for i in range(per_piece)
                    ]
                )
                for piece in table_pieces
            ]
        )
        voc_bits = bit_list("voc", n_voc)
        wid_bits = bit_list("wid", n_wid)
        v = lax.axis_index("voc")
        bits = {key: (v // key[1]) % 2 for key in voc_bits}
        bits[voc_bits[-1]] = ((v // per_piece) % 2) ^ t
        for key in wid_bits:
            bits[key] = (lax.axis_index("wid") // key[1]) % 2
        dims = [voc_bits[-1]] + voc_bits[:-1][::-1] + wid_bits[::-1]
        blocks = stacked.reshape(tuple(2 for _ in dims) + (tok_rows // n_wid, q_cols))
        first = voc_bits[0]
        blocks = halving_steps(blocks, dims, [first], bits)
        dims = [d for d in dims if d != first]
        half = tok_rows // n_wid // 2
        rest_voc = voc_bits[1:]
        part_a = halving_steps(blocks[..., :half, :], dims, rest_voc + wid_bits, bits)
        part_b = halving_steps(blocks[..., half:, :], dims, wid_bits + rest_voc, bits)
        mine = jnp.concatenate([part_a, part_b], axis=0).astype(jnp.bfloat16)
        grad_rows_pos = doubling_gather(mine, "wid").reshape((tok_rows, q_cols))
    else:
        parts = []
        for k, piece in enumerate(table_pieces):
            parts.append(
                lax.dot_general(piece, dlogits, (((0,), (1,)), ((), ())), preferred_element_type=jnp.float32)
            )
        full_rows = jnp.zeros((d_cols * n_tok, tok_rows), jnp.float32)
        for k, part in enumerate(parts):
            full_rows = lax.dynamic_update_slice_in_dim(
                full_rows, part, ((t - k) % n_tok) * d_cols, axis=0
            )
        reduced = lax.psum_scatter(full_rows, "voc", scatter_dimension=0, tiled=True)
        grad_rows_t = lax.psum(reduced, "wid").astype(jnp.bfloat16)

    if grad_rows_pos is not None:
        grad_other = lax.ppermute(grad_rows_pos, "tok", [(0, 1), (1, 0)])
        first = t == 0
        grad_all = jnp.where(
            first,
            jnp.concatenate([grad_rows_pos, grad_other], axis=0),
            jnp.concatenate([grad_other, grad_rows_pos], axis=0),
        )
        hidden_all = jnp.where(
            first,
            jnp.concatenate([hidden, hidden_other], axis=0),
            jnp.concatenate([hidden_other, hidden], axis=0),
        )
        grad_proj = lax.dot_general(
            grad_all, hidden_all, (((0,), (0,)), ((), ())), preferred_element_type=jnp.float32
        )
    elif n_tok == 2:
        grad_other = lax.ppermute(grad_rows_t, "tok", [(0, 1), (1, 0)])
        first = t == 0
        grad_all = jnp.where(
            first,
            jnp.concatenate([grad_rows_t, grad_other], axis=1),
            jnp.concatenate([grad_other, grad_rows_t], axis=1),
        )
        hidden_all = jnp.where(
            first,
            jnp.concatenate([hidden, hidden_other], axis=0),
            jnp.concatenate([hidden_other, hidden], axis=0),
        )
        grad_proj = jnp.dot(grad_all, hidden_all, preferred_element_type=jnp.float32)
    else:
        grad_all = lax.all_gather(grad_rows_t, "tok", axis=1, tiled=True)
        hidden_all = lax.all_gather(hidden, "tok", axis=0, tiled=True)
        grad_proj = jnp.dot(grad_all, hidden_all, preferred_element_type=jnp.float32)
    return (grad_proj, loss)


def solution(mesh):
    return jax.shard_map(
        on_device,
        mesh=mesh,
        in_specs=(P("tok", "wid"), P("voc", "wid"), P(("voc", "wid"), "tok"), P("tok"), P("tok")),
        out_specs=(P("voc", "wid"), P()),
        check_vma=False,
    )
```

```python
import jax
import jax.numpy as jnp
from jax import lax
from jax.sharding import PartitionSpec as P


def tok_pieces(x, n_tok):
    pieces = [x]
    for k in range(1, n_tok):
        perm = [(i, (i + k) % n_tok) for i in range(n_tok)]
        pieces.append(lax.ppermute(x, "tok", perm))
    return pieces


def combine(a, b):
    peak = jnp.maximum(a[0], b[0])
    total = a[1] * jnp.exp(a[0] - peak) + b[1] * jnp.exp(b[0] - peak)
    return jnp.stack([peak, total, a[2] + b[2]])


def butterfly(stats, axes):
    for ax in axes:
        n = lax.axis_size(ax)
        if n & (n - 1):
            gathered = lax.all_gather(stats, ax)
            out = gathered[0]
            for i in range(1, n):
                out = combine(out, gathered[i])
            stats = out
            continue
        b = 1
        while b < n:
            other = lax.ppermute(stats, ax, [(i, i ^ b) for i in range(n)])
            stats = combine(stats, other)
            b *= 2
    return stats


def tree_sum(x, ax):
    n = lax.axis_size(ax)
    if n & (n - 1):
        return lax.psum(x, ax)
    b = 1
    while b < n:
        x = x + lax.ppermute(x, ax, [(i, i ^ b) for i in range(n)])
        b *= 2
    return x


def is_pow2(n):
    return n & (n - 1) == 0


def bit_list(ax, n):
    out = []
    b = 1
    while b < n:
        out.append((ax, b))
        b *= 2
    return out


def halving_steps(x, dims, order, bits=None):
    dims = list(dims)
    for ax, b in order:
        pos = dims.index((ax, b))
        n = lax.axis_size(ax)
        bit = (lax.axis_index(ax) // b) % 2 if bits is None else bits[(ax, b)]
        keep = lax.dynamic_index_in_dim(x, bit, axis=pos, keepdims=False)
        send = lax.dynamic_index_in_dim(x, 1 - bit, axis=pos, keepdims=False)
        x = keep + lax.ppermute(send, ax, [(k, k ^ b) for k in range(n)])
        dims.pop(pos)
    return x


def doubling_gather(x, ax):
    n = lax.axis_size(ax)
    i = lax.axis_index(ax)
    b = n // 2
    lead = 0
    while b >= 1:
        other = lax.ppermute(x, ax, [(k, k ^ b) for k in range(n)])
        bit = (i // b) % 2
        x = jnp.where(bit == 0, jnp.stack([x, other], axis=lead), jnp.stack([other, x], axis=lead))
        lead += 1
        b //= 2
    return x.reshape((n,) + x.shape[lead:])


def on_device(hidden, proj, table, targets, valid):
    tok_rows = hidden.shape[0]
    block_rows = table.shape[0]
    n_tok = lax.axis_size("tok")
    t = lax.axis_index("tok")
    d_cols = table.shape[1]

    table_pieces = tok_pieces(table, n_tok)
    if n_tok == 2:
        hidden_other = lax.ppermute(hidden, "tok", [(0, 1), (1, 0)])

    partial_value = lax.dot_general(
        hidden, proj, (((1,), (1,)), ((), ())), preferred_element_type=jnp.float32
    )
    summed = lax.psum(partial_value, "wid")
    if is_pow2(lax.axis_size("voc")):
        quarters = doubling_gather(summed.astype(jnp.bfloat16), "voc")
        projected = quarters.transpose(1, 0, 2).reshape((tok_rows, -1))
    else:
        projected = lax.all_gather(summed.astype(jnp.bfloat16), "voc", axis=1, tiled=True)

    logits = None
    for k, piece in enumerate(table_pieces):
        cols = lax.dynamic_slice_in_dim(projected, ((t - k) % n_tok) * d_cols, d_cols, axis=1)
        part = lax.dot_general(
            cols, piece, (((1,), (1,)), ((), ())), preferred_element_type=jnp.float32
        )
        logits = part if logits is None else logits + part

    block_base = (lax.axis_index("voc") * lax.axis_size("wid") + lax.axis_index("wid")) * block_rows
    local_ids = targets - block_base
    is_target = local_ids[:, None] == lax.broadcasted_iota(jnp.int32, (tok_rows, block_rows), 1)
    picked_here = jnp.sum(jnp.where(is_target, logits, 0.0), axis=1)
    peak_here = jnp.max(logits, axis=1)
    exp_here = jnp.sum(jnp.exp(logits - peak_here[:, None]), axis=1)
    weight = valid.astype(jnp.float32)

    stats = jnp.stack([peak_here, exp_here, picked_here])
    stats = butterfly(stats, ("voc", "wid"))
    log_total = stats[0] + jnp.log(stats[1])
    picked = stats[2]
    sums = jnp.stack([jnp.sum(weight * (log_total - picked)), jnp.sum(weight)])
    sums = tree_sum(sums, "tok")
    loss = sums[0] / sums[1]

    dlogits = (
        weight[:, None] * (jnp.exp(logits - log_total[:, None]) - is_target.astype(jnp.float32))
    ).astype(jnp.bfloat16)

    n_voc, n_wid = lax.axis_size("voc"), lax.axis_size("wid")
    grad_rows_pos = None
    grad_path = (
        n_tok == 2
        and n_voc >= 2
        and is_pow2(n_voc)
        and is_pow2(n_wid)
        and tok_rows % (2 * n_wid) == 0
        and d_cols % (n_voc // 2) == 0
    )
    per_piece = 0
    if grad_path:
        per_piece = n_voc // 2
        q_cols = d_cols // per_piece
    if grad_path and per_piece == 2:
        c = lax.axis_index("voc") % 2

        def quarter_dots(sel):
            return jnp.stack(
                [
                    jnp.dot(
                        dlogits,
                        lax.dynamic_slice_in_dim(piece, sel * q_cols, q_cols, axis=1),
                        preferred_element_type=jnp.float32,
                    )
                    for piece in table_pieces
                ]
            )

        sent = quarter_dots(1 - c)
        received = lax.ppermute(sent, "voc", [(k, k ^ 1) for k in range(n_voc)])
        blocks = quarter_dots(c) + received
        voc_bits = bit_list("voc", n_voc)
        wid_bits = bit_list("wid", n_wid)
        v = lax.axis_index("voc")
        bits = {voc_bits[-1]: ((v // per_piece) % 2) ^ t}
        for key in wid_bits:
            bits[key] = (lax.axis_index("wid") // key[1]) % 2
        dims = [voc_bits[-1]] + wid_bits[::-1]
        blocks = blocks.reshape(tuple(2 for _ in dims) + (tok_rows // n_wid, q_cols))
        half = tok_rows // n_wid // 2
        rest_voc = voc_bits[1:]
        part_a = halving_steps(blocks[..., :half, :], dims, rest_voc + wid_bits, bits)
        part_b = halving_steps(blocks[..., half:, :], dims, wid_bits + rest_voc, bits)
        mine = jnp.concatenate([part_a, part_b], axis=0).astype(jnp.bfloat16)
        grad_rows_pos = doubling_gather(mine, "wid").reshape((tok_rows, q_cols))
    elif grad_path:
        stacked = jnp.stack(
            [
                jnp.stack(
                    [
                        jnp.dot(dlogits, piece[:, i * q_cols : (i + 1) * q_cols], preferred_element_type=jnp.float32)
                        for i in range(per_piece)
                    ]
                )
                for piece in table_pieces
            ]
        )
        voc_bits = bit_list("voc", n_voc)
        wid_bits = bit_list("wid", n_wid)
        v = lax.axis_index("voc")
        bits = {key: (v // key[1]) % 2 for key in voc_bits}
        bits[voc_bits[-1]] = ((v // per_piece) % 2) ^ t
        for key in wid_bits:
            bits[key] = (lax.axis_index("wid") // key[1]) % 2
        dims = [voc_bits[-1]] + voc_bits[:-1][::-1] + wid_bits[::-1]
        blocks = stacked.reshape(tuple(2 for _ in dims) + (tok_rows // n_wid, q_cols))
        first = voc_bits[0]
        blocks = halving_steps(blocks, dims, [first], bits)
        dims = [d for d in dims if d != first]
        half = tok_rows // n_wid // 2
        rest_voc = voc_bits[1:]
        part_a = halving_steps(blocks[..., :half, :], dims, rest_voc + wid_bits, bits)
        part_b = halving_steps(blocks[..., half:, :], dims, wid_bits + rest_voc, bits)
        mine = jnp.concatenate([part_a, part_b], axis=0).astype(jnp.bfloat16)
        grad_rows_pos = doubling_gather(mine, "wid").reshape((tok_rows, q_cols))
    else:
        parts = []
        for k, piece in enumerate(table_pieces):
            parts.append(
                lax.dot_general(piece, dlogits, (((0,), (1,)), ((), ())), preferred_element_type=jnp.float32)
            )
        full_rows = jnp.zeros((d_cols * n_tok, tok_rows), jnp.float32)
        for k, part in enumerate(parts):
            full_rows = lax.dynamic_update_slice_in_dim(
                full_rows, part, ((t - k) % n_tok) * d_cols, axis=0
            )
        reduced = lax.psum_scatter(full_rows, "voc", scatter_dimension=0, tiled=True)
        grad_rows_t = lax.psum(reduced, "wid").astype(jnp.bfloat16)

    if grad_rows_pos is not None:
        grad_other = lax.ppermute(grad_rows_pos, "tok", [(0, 1), (1, 0)])
        first = t == 0
        grad_all = jnp.where(
            first,
            jnp.concatenate([grad_rows_pos, grad_other], axis=0),
            jnp.concatenate([grad_other, grad_rows_pos], axis=0),
        )
        hidden_all = jnp.where(
            first,
            jnp.concatenate([hidden, hidden_other], axis=0),
            jnp.concatenate([hidden_other, hidden], axis=0),
        )
        grad_proj = lax.dot_general(
            grad_all, hidden_all, (((0,), (0,)), ((), ())), preferred_element_type=jnp.float32
        )
    elif n_tok == 2:
        grad_other = lax.ppermute(grad_rows_t, "tok", [(0, 1), (1, 0)])
        first = t == 0
        grad_all = jnp.where(
            first,
            jnp.concatenate([grad_rows_t, grad_other], axis=1),
            jnp.concatenate([grad_other, grad_rows_t], axis=1),
        )
        hidden_all = jnp.where(
            first,
            jnp.concatenate([hidden, hidden_other], axis=0),
            jnp.concatenate([hidden_other, hidden], axis=0),
        )
        grad_proj = jnp.dot(grad_all, hidden_all, preferred_element_type=jnp.float32)
    else:
        grad_all = lax.all_gather(grad_rows_t, "tok", axis=1, tiled=True)
        hidden_all = lax.all_gather(hidden, "tok", axis=0, tiled=True)
        grad_proj = jnp.dot(grad_all, hidden_all, preferred_element_type=jnp.float32)
    return (grad_proj, loss)


def solution(mesh):
    return jax.shard_map(
        on_device,
        mesh=mesh,
        in_specs=(P("tok", "wid"), P("voc", "wid"), P(("voc", "wid"), "tok"), P("tok"), P("tok")),
        out_specs=(P("voc", "wid"), P()),
        check_vma=False,
    )
```

```python
import jax
import jax.numpy as jnp
from jax import lax
from jax.sharding import PartitionSpec as P


def tok_pieces(x, n_tok):
    pieces = [x]
    for k in range(1, n_tok):
        perm = [(i, (i + k) % n_tok) for i in range(n_tok)]
        pieces.append(lax.ppermute(x, "tok", perm))
    return pieces


def combine(a, b):
    peak = jnp.maximum(a[0], b[0])
    total = a[1] * jnp.exp(a[0] - peak) + b[1] * jnp.exp(b[0] - peak)
    return jnp.stack([peak, total, a[2] + b[2]])


def butterfly(stats, axes):
    for ax in axes:
        n = lax.axis_size(ax)
        if n & (n - 1):
            gathered = lax.all_gather(stats, ax)
            out = gathered[0]
            for i in range(1, n):
                out = combine(out, gathered[i])
            stats = out
            continue
        b = 1
        while b < n:
            other = lax.ppermute(stats, ax, [(i, i ^ b) for i in range(n)])
            stats = combine(stats, other)
            b *= 2
    return stats


def tree_sum(x, ax):
    n = lax.axis_size(ax)
    if n & (n - 1):
        return lax.psum(x, ax)
    b = 1
    while b < n:
        x = x + lax.ppermute(x, ax, [(i, i ^ b) for i in range(n)])
        b *= 2
    return x


def is_pow2(n):
    return n & (n - 1) == 0


def bit_list(ax, n):
    out = []
    b = 1
    while b < n:
        out.append((ax, b))
        b *= 2
    return out


def halving_steps(x, dims, order, bits=None):
    dims = list(dims)
    for ax, b in order:
        pos = dims.index((ax, b))
        n = lax.axis_size(ax)
        bit = (lax.axis_index(ax) // b) % 2 if bits is None else bits[(ax, b)]
        keep = lax.dynamic_index_in_dim(x, bit, axis=pos, keepdims=False)
        send = lax.dynamic_index_in_dim(x, 1 - bit, axis=pos, keepdims=False)
        x = keep + lax.ppermute(send, ax, [(k, k ^ b) for k in range(n)])
        dims.pop(pos)
    return x


def doubling_gather(x, ax):
    n = lax.axis_size(ax)
    i = lax.axis_index(ax)
    b = n // 2
    lead = 0
    while b >= 1:
        other = lax.ppermute(x, ax, [(k, k ^ b) for k in range(n)])
        bit = (i // b) % 2
        x = jnp.where(bit == 0, jnp.stack([x, other], axis=lead), jnp.stack([other, x], axis=lead))
        lead += 1
        b //= 2
    return x.reshape((n,) + x.shape[lead:])


def on_device(hidden, proj, table, targets, valid):
    tok_rows = hidden.shape[0]
    block_rows = table.shape[0]
    n_tok = lax.axis_size("tok")
    t = lax.axis_index("tok")
    d_cols = table.shape[1]

    table_pieces = tok_pieces(table, n_tok)
    if n_tok == 2:
        hidden_other = lax.ppermute(hidden, "tok", [(0, 1), (1, 0)])

    partial_value = lax.dot_general(
        hidden, proj, (((1,), (1,)), ((), ())), preferred_element_type=jnp.float32
    )
    summed = lax.psum(partial_value, "wid")
    if is_pow2(lax.axis_size("voc")):
        quarters = doubling_gather(summed.astype(jnp.bfloat16), "voc")
        projected = quarters.transpose(1, 0, 2).reshape((tok_rows, -1))
    else:
        projected = lax.all_gather(summed.astype(jnp.bfloat16), "voc", axis=1, tiled=True)

    logits = None
    for k, piece in enumerate(table_pieces):
        cols = lax.dynamic_slice_in_dim(projected, ((t - k) % n_tok) * d_cols, d_cols, axis=1)
        part = lax.dot_general(
            cols, piece, (((1,), (1,)), ((), ())), preferred_element_type=jnp.float32
        )
        logits = part if logits is None else logits + part

    block_base = (lax.axis_index("voc") * lax.axis_size("wid") + lax.axis_index("wid")) * block_rows
    local_ids = targets - block_base
    is_target = local_ids[:, None] == lax.broadcasted_iota(jnp.int32, (tok_rows, block_rows), 1)
    picked_here = jnp.sum(jnp.where(is_target, logits, 0.0), axis=1)
    peak_here = jnp.max(logits, axis=1)
    exp_here = jnp.sum(jnp.exp(logits - peak_here[:, None]), axis=1)
    weight = valid.astype(jnp.float32)

    stats = jnp.stack([peak_here, exp_here, picked_here])
    stats = butterfly(stats, ("voc", "wid"))
    log_total = stats[0] + jnp.log(stats[1])
    picked = stats[2]
    sums = jnp.stack([jnp.sum(weight * (log_total - picked)), jnp.sum(weight)])
    sums = tree_sum(sums, "tok")

    dlogits = (
        weight[:, None] * (jnp.exp(logits - log_total[:, None]) - is_target.astype(jnp.float32))
    ).astype(jnp.bfloat16)

    n_voc, n_wid = lax.axis_size("voc"), lax.axis_size("wid")
    grad_rows_pos = None
    grad_path = (
        n_tok == 2
        and n_voc >= 2
        and is_pow2(n_voc)
        and is_pow2(n_wid)
        and tok_rows % (2 * n_wid) == 0
        and d_cols % (n_voc // 2) == 0
    )
    per_piece = 0
    if grad_path:
        per_piece = n_voc // 2
        q_cols = d_cols // per_piece
    if grad_path and per_piece == 2:
        c = lax.axis_index("voc") % 2

        def quarter_dots(sel):
            return jnp.stack(
                [
                    jnp.dot(
                        dlogits,
                        lax.dynamic_slice_in_dim(piece, sel * q_cols, q_cols, axis=1),
                        preferred_element_type=jnp.float32,
                    )
                    for piece in table_pieces
                ]
            )

        sent = quarter_dots(1 - c)
        received = lax.ppermute(sent, "voc", [(k, k ^ 1) for k in range(n_voc)])
        blocks = quarter_dots(c) + received
        voc_bits = bit_list("voc", n_voc)
        wid_bits = bit_list("wid", n_wid)
        v = lax.axis_index("voc")
        bits = {voc_bits[-1]: ((v // per_piece) % 2) ^ t}
        for key in wid_bits:
            bits[key] = (lax.axis_index("wid") // key[1]) % 2
        dims = [voc_bits[-1]] + wid_bits[::-1]
        blocks = blocks.reshape(tuple(2 for _ in dims) + (tok_rows // n_wid, q_cols))
        half = tok_rows // n_wid // 2
        rest_voc = voc_bits[1:]
        part_a = halving_steps(blocks[..., :half, :], dims, rest_voc + wid_bits, bits)
        part_b = halving_steps(blocks[..., half:, :], dims, wid_bits + rest_voc, bits)
        mine = jnp.concatenate([part_a, part_b], axis=0).astype(jnp.bfloat16)
        sums, mine = lax.optimization_barrier((sums, mine))
        grad_rows_pos = doubling_gather(mine, "wid").reshape((tok_rows, q_cols))
    elif grad_path:
        stacked = jnp.stack(
            [
                jnp.stack(
                    [
                        jnp.dot(dlogits, piece[:, i * q_cols : (i + 1) * q_cols], preferred_element_type=jnp.float32)
                        for i in range(per_piece)
                    ]
                )
                for piece in table_pieces
            ]
        )
        voc_bits = bit_list("voc", n_voc)
        wid_bits = bit_list("wid", n_wid)
        v = lax.axis_index("voc")
        bits = {key: (v // key[1]) % 2 for key in voc_bits}
        bits[voc_bits[-1]] = ((v // per_piece) % 2) ^ t
        for key in wid_bits:
            bits[key] = (lax.axis_index("wid") // key[1]) % 2
        dims = [voc_bits[-1]] + voc_bits[:-1][::-1] + wid_bits[::-1]
        blocks = stacked.reshape(tuple(2 for _ in dims) + (tok_rows // n_wid, q_cols))
        first = voc_bits[0]
        blocks = halving_steps(blocks, dims, [first], bits)
        dims = [d for d in dims if d != first]
        half = tok_rows // n_wid // 2
        rest_voc = voc_bits[1:]
        part_a = halving_steps(blocks[..., :half, :], dims, rest_voc + wid_bits, bits)
        part_b = halving_steps(blocks[..., half:, :], dims, wid_bits + rest_voc, bits)
        mine = jnp.concatenate([part_a, part_b], axis=0).astype(jnp.bfloat16)
        grad_rows_pos = doubling_gather(mine, "wid").reshape((tok_rows, q_cols))
    else:
        parts = []
        for k, piece in enumerate(table_pieces):
            parts.append(
                lax.dot_general(piece, dlogits, (((0,), (1,)), ((), ())), preferred_element_type=jnp.float32)
            )
        full_rows = jnp.zeros((d_cols * n_tok, tok_rows), jnp.float32)
        for k, part in enumerate(parts):
            full_rows = lax.dynamic_update_slice_in_dim(
                full_rows, part, ((t - k) % n_tok) * d_cols, axis=0
            )
        reduced = lax.psum_scatter(full_rows, "voc", scatter_dimension=0, tiled=True)
        grad_rows_t = lax.psum(reduced, "wid").astype(jnp.bfloat16)

    if grad_rows_pos is not None:
        grad_other = lax.ppermute(grad_rows_pos, "tok", [(0, 1), (1, 0)])
        by_pos = (((0,), (0,)), ((), ()))
        grad_proj = lax.dot_general(
            grad_rows_pos, hidden, by_pos, preferred_element_type=jnp.float32
        ) + lax.dot_general(grad_other, hidden_other, by_pos, preferred_element_type=jnp.float32)
    elif n_tok == 2:
        grad_other = lax.ppermute(grad_rows_t, "tok", [(0, 1), (1, 0)])
        first = t == 0
        grad_all = jnp.where(
            first,
            jnp.concatenate([grad_rows_t, grad_other], axis=1),
            jnp.concatenate([grad_other, grad_rows_t], axis=1),
        )
        hidden_all = jnp.where(
            first,
            jnp.concatenate([hidden, hidden_other], axis=0),
            jnp.concatenate([hidden_other, hidden], axis=0),
        )
        grad_proj = jnp.dot(grad_all, hidden_all, preferred_element_type=jnp.float32)
    else:
        grad_all = lax.all_gather(grad_rows_t, "tok", axis=1, tiled=True)
        hidden_all = lax.all_gather(hidden, "tok", axis=0, tiled=True)
        grad_proj = jnp.dot(grad_all, hidden_all, preferred_element_type=jnp.float32)
    loss = sums[0] / sums[1]
    return (grad_proj, loss)


def solution(mesh):
    return jax.shard_map(
        on_device,
        mesh=mesh,
        in_specs=(P("tok", "wid"), P("voc", "wid"), P(("voc", "wid"), "tok"), P("tok"), P("tok")),
        out_specs=(P("voc", "wid"), P()),
        check_vma=False,
    )
```

```python
import jax
import jax.numpy as jnp
from jax import lax
from jax.sharding import PartitionSpec as P


def tok_pieces(x, n_tok):
    pieces = [x]
    for k in range(1, n_tok):
        perm = [(i, (i + k) % n_tok) for i in range(n_tok)]
        pieces.append(lax.ppermute(x, "tok", perm))
    return pieces


def combine(a, b):
    peak = jnp.maximum(a[0], b[0])
    total = a[1] * jnp.exp(a[0] - peak) + b[1] * jnp.exp(b[0] - peak)
    return jnp.stack([peak, total, a[2] + b[2]])


def butterfly(stats, axes):
    for ax in axes:
        n = lax.axis_size(ax)
        if n & (n - 1):
            gathered = lax.all_gather(stats, ax)
            out = gathered[0]
            for i in range(1, n):
                out = combine(out, gathered[i])
            stats = out
            continue
        b = 1
        while b < n:
            other = lax.ppermute(stats, ax, [(i, i ^ b) for i in range(n)])
            stats = combine(stats, other)
            b *= 2
    return stats


def tree_sum(x, ax):
    n = lax.axis_size(ax)
    if n & (n - 1):
        return lax.psum(x, ax)
    b = 1
    while b < n:
        x = x + lax.ppermute(x, ax, [(i, i ^ b) for i in range(n)])
        b *= 2
    return x


def is_pow2(n):
    return n & (n - 1) == 0


def bit_list(ax, n):
    out = []
    b = 1
    while b < n:
        out.append((ax, b))
        b *= 2
    return out


def halving_steps(x, dims, order, bits=None):
    dims = list(dims)
    for ax, b in order:
        pos = dims.index((ax, b))
        n = lax.axis_size(ax)
        bit = (lax.axis_index(ax) // b) % 2 if bits is None else bits[(ax, b)]
        keep = lax.dynamic_index_in_dim(x, bit, axis=pos, keepdims=False)
        send = lax.dynamic_index_in_dim(x, 1 - bit, axis=pos, keepdims=False)
        x = keep + lax.ppermute(send, ax, [(k, k ^ b) for k in range(n)])
        dims.pop(pos)
    return x


def doubling_gather(x, ax):
    n = lax.axis_size(ax)
    i = lax.axis_index(ax)
    b = n // 2
    lead = 0
    while b >= 1:
        other = lax.ppermute(x, ax, [(k, k ^ b) for k in range(n)])
        bit = (i // b) % 2
        x = jnp.where(bit == 0, jnp.stack([x, other], axis=lead), jnp.stack([other, x], axis=lead))
        lead += 1
        b //= 2
    return x.reshape((n,) + x.shape[lead:])


def on_device(hidden, proj, table, targets, valid):
    tok_rows = hidden.shape[0]
    block_rows = table.shape[0]
    n_tok = lax.axis_size("tok")
    t = lax.axis_index("tok")
    d_cols = table.shape[1]

    table_pieces = tok_pieces(table, n_tok)
    if n_tok == 2:
        hidden_other = lax.ppermute(hidden, "tok", [(0, 1), (1, 0)])

    partial_value = lax.dot_general(
        hidden, proj, (((1,), (1,)), ((), ())), preferred_element_type=jnp.float32
    )
    summed = lax.psum(partial_value, "wid")
    if is_pow2(lax.axis_size("voc")):
        quarters = doubling_gather(summed.astype(jnp.bfloat16), "voc")
        projected = quarters.transpose(1, 0, 2).reshape((tok_rows, -1))
    else:
        projected = lax.all_gather(summed.astype(jnp.bfloat16), "voc", axis=1, tiled=True)

    logits = None
    for k, piece in enumerate(table_pieces):
        cols = lax.dynamic_slice_in_dim(projected, ((t - k) % n_tok) * d_cols, d_cols, axis=1)
        part = lax.dot_general(
            cols, piece, (((1,), (1,)), ((), ())), preferred_element_type=jnp.float32
        )
        logits = part if logits is None else logits + part

    block_base = (lax.axis_index("voc") * lax.axis_size("wid") + lax.axis_index("wid")) * block_rows
    local_ids = targets - block_base
    is_target = local_ids[:, None] == lax.broadcasted_iota(jnp.int32, (tok_rows, block_rows), 1)
    picked_here = jnp.sum(jnp.where(is_target, logits, 0.0), axis=1)
    peak_here = jnp.max(logits, axis=1)
    exp_here = jnp.sum(jnp.exp(logits - peak_here[:, None]), axis=1)
    weight = valid.astype(jnp.float32)

    stats = jnp.stack([peak_here, exp_here, picked_here])
    stats = butterfly(stats, ("voc", "wid"))
    log_total = stats[0] + jnp.log(stats[1])
    picked = stats[2]
    sums = jnp.stack([jnp.sum(weight * (log_total - picked)), jnp.sum(weight)])
    sums = tree_sum(sums, "tok")

    dlogits = (
        weight[:, None] * (jnp.exp(logits - log_total[:, None]) - is_target.astype(jnp.float32))
    ).astype(jnp.bfloat16)

    n_voc, n_wid = lax.axis_size("voc"), lax.axis_size("wid")
    grad_rows_pos = None
    grad_path = (
        n_tok == 2
        and n_voc >= 2
        and is_pow2(n_voc)
        and is_pow2(n_wid)
        and tok_rows % (2 * n_wid) == 0
        and d_cols % (n_voc // 2) == 0
    )
    per_piece = 0
    if grad_path:
        per_piece = n_voc // 2
        q_cols = d_cols // per_piece
    if grad_path and per_piece == 2:
        c = lax.axis_index("voc") % 2

        def quarter_dots(sel):
            return jnp.stack(
                [
                    jnp.dot(
                        dlogits,
                        lax.dynamic_slice_in_dim(piece, sel * q_cols, q_cols, axis=1),
                        preferred_element_type=jnp.float32,
                    )
                    for piece in table_pieces
                ]
            )

        sent = quarter_dots(1 - c)
        received = lax.ppermute(sent, "voc", [(k, k ^ 1) for k in range(n_voc)])
        blocks = quarter_dots(c) + received
        voc_bits = bit_list("voc", n_voc)
        wid_bits = bit_list("wid", n_wid)
        v = lax.axis_index("voc")
        bits = {voc_bits[-1]: ((v // per_piece) % 2) ^ t}
        for key in wid_bits:
            bits[key] = (lax.axis_index("wid") // key[1]) % 2
        dims = [voc_bits[-1]] + wid_bits[::-1]
        blocks = blocks.reshape(tuple(2 for _ in dims) + (tok_rows // n_wid, q_cols))
        half = tok_rows // n_wid // 2
        rest_voc = voc_bits[1:]
        part_a = halving_steps(blocks[..., :half, :], dims, rest_voc + wid_bits, bits)
        part_b = halving_steps(blocks[..., half:, :], dims, wid_bits + rest_voc, bits)
        mine = jnp.concatenate([part_a, part_b], axis=0).astype(jnp.bfloat16)
        grad_rows_pos = doubling_gather(mine, "wid").reshape((tok_rows, q_cols))
    elif grad_path:
        stacked = jnp.stack(
            [
                jnp.stack(
                    [
                        jnp.dot(dlogits, piece[:, i * q_cols : (i + 1) * q_cols], preferred_element_type=jnp.float32)
                        for i in range(per_piece)
                    ]
                )
                for piece in table_pieces
            ]
        )
        voc_bits = bit_list("voc", n_voc)
        wid_bits = bit_list("wid", n_wid)
        v = lax.axis_index("voc")
        bits = {key: (v // key[1]) % 2 for key in voc_bits}
        bits[voc_bits[-1]] = ((v // per_piece) % 2) ^ t
        for key in wid_bits:
            bits[key] = (lax.axis_index("wid") // key[1]) % 2
        dims = [voc_bits[-1]] + voc_bits[:-1][::-1] + wid_bits[::-1]
        blocks = stacked.reshape(tuple(2 for _ in dims) + (tok_rows // n_wid, q_cols))
        first = voc_bits[0]
        blocks = halving_steps(blocks, dims, [first], bits)
        dims = [d for d in dims if d != first]
        half = tok_rows // n_wid // 2
        rest_voc = voc_bits[1:]
        part_a = halving_steps(blocks[..., :half, :], dims, rest_voc + wid_bits, bits)
        part_b = halving_steps(blocks[..., half:, :], dims, wid_bits + rest_voc, bits)
        mine = jnp.concatenate([part_a, part_b], axis=0).astype(jnp.bfloat16)
        grad_rows_pos = doubling_gather(mine, "wid").reshape((tok_rows, q_cols))
    else:
        parts = []
        for k, piece in enumerate(table_pieces):
            parts.append(
                lax.dot_general(piece, dlogits, (((0,), (1,)), ((), ())), preferred_element_type=jnp.float32)
            )
        full_rows = jnp.zeros((d_cols * n_tok, tok_rows), jnp.float32)
        for k, part in enumerate(parts):
            full_rows = lax.dynamic_update_slice_in_dim(
                full_rows, part, ((t - k) % n_tok) * d_cols, axis=0
            )
        reduced = lax.psum_scatter(full_rows, "voc", scatter_dimension=0, tiled=True)
        grad_rows_t = lax.psum(reduced, "wid").astype(jnp.bfloat16)

    if grad_rows_pos is not None:
        grad_other = lax.ppermute(grad_rows_pos, "tok", [(0, 1), (1, 0)])
        by_pos = (((0,), (0,)), ((), ()))
        grad_proj = lax.dot_general(
            grad_rows_pos, hidden, by_pos, preferred_element_type=jnp.float32
        ) + lax.dot_general(grad_other, hidden_other, by_pos, preferred_element_type=jnp.float32)
    elif n_tok == 2:
        grad_other = lax.ppermute(grad_rows_t, "tok", [(0, 1), (1, 0)])
        first = t == 0
        grad_all = jnp.where(
            first,
            jnp.concatenate([grad_rows_t, grad_other], axis=1),
            jnp.concatenate([grad_other, grad_rows_t], axis=1),
        )
        hidden_all = jnp.where(
            first,
            jnp.concatenate([hidden, hidden_other], axis=0),
            jnp.concatenate([hidden_other, hidden], axis=0),
        )
        grad_proj = jnp.dot(grad_all, hidden_all, preferred_element_type=jnp.float32)
    else:
        grad_all = lax.all_gather(grad_rows_t, "tok", axis=1, tiled=True)
        hidden_all = lax.all_gather(hidden, "tok", axis=0, tiled=True)
        grad_proj = jnp.dot(grad_all, hidden_all, preferred_element_type=jnp.float32)
    loss = sums[0] / sums[1]
    return (grad_proj, loss)


def solution(mesh):
    return jax.shard_map(
        on_device,
        mesh=mesh,
        in_specs=(P("tok", "wid"), P("voc", "wid"), P(("voc", "wid"), "tok"), P("tok"), P("tok")),
        out_specs=(P("voc", "wid"), P()),
        check_vma=False,
    )
```

```python
import jax
import jax.numpy as jnp
from jax import lax
from jax.sharding import PartitionSpec as P


def tok_pieces(x, n_tok):
    pieces = [x]
    for k in range(1, n_tok):
        perm = [(i, (i + k) % n_tok) for i in range(n_tok)]
        pieces.append(lax.ppermute(x, "tok", perm))
    return pieces


def combine(a, b):
    peak = jnp.maximum(a[0], b[0])
    total = a[1] * jnp.exp(a[0] - peak) + b[1] * jnp.exp(b[0] - peak)
    return jnp.stack([peak, total, a[2] + b[2]])


def butterfly(stats, axes):
    for ax in axes:
        n = lax.axis_size(ax)
        if n & (n - 1):
            gathered = lax.all_gather(stats, ax)
            out = gathered[0]
            for i in range(1, n):
                out = combine(out, gathered[i])
            stats = out
            continue
        b = 1
        while b < n:
            other = lax.ppermute(stats, ax, [(i, i ^ b) for i in range(n)])
            stats = combine(stats, other)
            b *= 2
    return stats


def shift_gather(x, axes):
    sizes = [lax.axis_size(ax) for ax in axes]
    n = 1
    lin = 0
    for ax, size in zip(axes, sizes):
        n *= size
        lin = lin * size + lax.axis_index(ax)
    got = [x]
    for sh in range(1, n):
        got.append(lax.ppermute(x, tuple(axes), [(k, (k + sh) % n) for k in range(n)]))
    rev = jnp.stack([got[(-j) % n] for j in range(n)])
    return jnp.roll(rev, lin, axis=0)


def gather_combine(stats, axes):
    for ax in axes:
        g = shift_gather(stats, (ax,))
        out = g[0]
        for k in range(1, g.shape[0]):
            out = combine(out, g[k])
        stats = out
    return stats


def tree_sum(x, ax):
    n = lax.axis_size(ax)
    if n & (n - 1):
        return lax.psum(x, ax)
    b = 1
    while b < n:
        x = x + lax.ppermute(x, ax, [(i, i ^ b) for i in range(n)])
        b *= 2
    return x


def is_pow2(n):
    return n & (n - 1) == 0


def bit_list(ax, n):
    out = []
    b = 1
    while b < n:
        out.append((ax, b))
        b *= 2
    return out


def halving_steps(x, dims, order, bits=None):
    dims = list(dims)
    for ax, b in order:
        pos = dims.index((ax, b))
        n = lax.axis_size(ax)
        bit = (lax.axis_index(ax) // b) % 2 if bits is None else bits[(ax, b)]
        keep = lax.dynamic_index_in_dim(x, bit, axis=pos, keepdims=False)
        send = lax.dynamic_index_in_dim(x, 1 - bit, axis=pos, keepdims=False)
        x = keep + lax.ppermute(send, ax, [(k, k ^ b) for k in range(n)])
        dims.pop(pos)
    return x


def doubling_gather(x, ax):
    n = lax.axis_size(ax)
    i = lax.axis_index(ax)
    b = n // 2
    lead = 0
    while b >= 1:
        other = lax.ppermute(x, ax, [(k, k ^ b) for k in range(n)])
        bit = (i // b) % 2
        x = jnp.where(bit == 0, jnp.stack([x, other], axis=lead), jnp.stack([other, x], axis=lead))
        lead += 1
        b //= 2
    return x.reshape((n,) + x.shape[lead:])


def on_device(hidden, proj, table, targets, valid):
    tok_rows = hidden.shape[0]
    block_rows = table.shape[0]
    n_tok = lax.axis_size("tok")
    t = lax.axis_index("tok")
    d_cols = table.shape[1]

    table_pieces = tok_pieces(table, n_tok)
    if n_tok == 2:
        hidden_other = lax.ppermute(hidden, "tok", [(0, 1), (1, 0)])

    partial_value = lax.dot_general(
        hidden, proj, (((1,), (1,)), ((), ())), preferred_element_type=jnp.float32
    )
    summed = lax.psum(partial_value, "wid")
    if is_pow2(lax.axis_size("voc")):
        quarters = doubling_gather(summed.astype(jnp.bfloat16), "voc")
        projected = quarters.transpose(1, 0, 2).reshape((tok_rows, -1))
    else:
        projected = lax.all_gather(summed.astype(jnp.bfloat16), "voc", axis=1, tiled=True)

    logits = None
    for k, piece in enumerate(table_pieces):
        cols = lax.dynamic_slice_in_dim(projected, ((t - k) % n_tok) * d_cols, d_cols, axis=1)
        part = lax.dot_general(
            cols, piece, (((1,), (1,)), ((), ())), preferred_element_type=jnp.float32
        )
        logits = part if logits is None else logits + part

    block_base = (lax.axis_index("voc") * lax.axis_size("wid") + lax.axis_index("wid")) * block_rows
    local_ids = targets - block_base
    is_target = local_ids[:, None] == lax.broadcasted_iota(jnp.int32, (tok_rows, block_rows), 1)
    picked_here = jnp.sum(jnp.where(is_target, logits, 0.0), axis=1)
    peak_here = jnp.max(logits, axis=1)
    exp_here = jnp.sum(jnp.exp(logits - peak_here[:, None]), axis=1)
    weight = valid.astype(jnp.float32)

    stats = jnp.stack([peak_here, exp_here, picked_here])
    stats = gather_combine(stats, ("voc", "wid"))
    log_total = stats[0] + jnp.log(stats[1])
    picked = stats[2]
    sums = jnp.stack([jnp.sum(weight * (log_total - picked)), jnp.sum(weight)])
    sums = tree_sum(sums, "tok")

    dlogits = (
        weight[:, None] * (jnp.exp(logits - log_total[:, None]) - is_target.astype(jnp.float32))
    ).astype(jnp.bfloat16)

    n_voc, n_wid = lax.axis_size("voc"), lax.axis_size("wid")
    grad_rows_pos = None
    grad_all = None
    grad_path = (
        n_tok == 2
        and n_voc >= 2
        and is_pow2(n_voc)
        and is_pow2(n_wid)
        and tok_rows % (2 * n_wid) == 0
        and d_cols % (n_voc // 2) == 0
    )
    per_piece = 0
    if grad_path:
        per_piece = n_voc // 2
        q_cols = d_cols // per_piece
    if grad_path and per_piece == 2:
        c = lax.axis_index("voc") % 2

        def quarter_dots(sel):
            return jnp.stack(
                [
                    jnp.dot(
                        dlogits,
                        lax.dynamic_slice_in_dim(piece, sel * q_cols, q_cols, axis=1),
                        preferred_element_type=jnp.float32,
                    )
                    for piece in table_pieces
                ]
            )

        sent = quarter_dots(1 - c)
        received = lax.ppermute(sent, "voc", [(k, k ^ 1) for k in range(n_voc)])
        blocks = quarter_dots(c) + received
        voc_bits = bit_list("voc", n_voc)
        wid_bits = bit_list("wid", n_wid)
        v = lax.axis_index("voc")
        bits = {voc_bits[-1]: ((v // per_piece) % 2) ^ t}
        for key in wid_bits:
            bits[key] = (lax.axis_index("wid") // key[1]) % 2
        dims = [voc_bits[-1]] + wid_bits[::-1]
        blocks = blocks.reshape(tuple(2 for _ in dims) + (tok_rows // n_wid, q_cols))
        half = tok_rows // n_wid // 2
        rest_voc = voc_bits[1:]
        part_a = halving_steps(blocks[..., :half, :], dims, rest_voc + wid_bits, bits)
        part_b = halving_steps(blocks[..., half:, :], dims, wid_bits + rest_voc, bits)
        mine = jnp.concatenate([part_a, part_b], axis=0).astype(jnp.bfloat16)
        grad_all = shift_gather(mine, ("tok", "wid")).reshape((n_tok * tok_rows, q_cols))
    elif grad_path:
        stacked = jnp.stack(
            [
                jnp.stack(
                    [
                        jnp.dot(dlogits, piece[:, i * q_cols : (i + 1) * q_cols], preferred_element_type=jnp.float32)
                        for i in range(per_piece)
                    ]
                )
                for piece in table_pieces
            ]
        )
        voc_bits = bit_list("voc", n_voc)
        wid_bits = bit_list("wid", n_wid)
        v = lax.axis_index("voc")
        bits = {key: (v // key[1]) % 2 for key in voc_bits}
        bits[voc_bits[-1]] = ((v // per_piece) % 2) ^ t
        for key in wid_bits:
            bits[key] = (lax.axis_index("wid") // key[1]) % 2
        dims = [voc_bits[-1]] + voc_bits[:-1][::-1] + wid_bits[::-1]
        blocks = stacked.reshape(tuple(2 for _ in dims) + (tok_rows // n_wid, q_cols))
        first = voc_bits[0]
        blocks = halving_steps(blocks, dims, [first], bits)
        dims = [d for d in dims if d != first]
        half = tok_rows // n_wid // 2
        rest_voc = voc_bits[1:]
        part_a = halving_steps(blocks[..., :half, :], dims, rest_voc + wid_bits, bits)
        part_b = halving_steps(blocks[..., half:, :], dims, wid_bits + rest_voc, bits)
        mine = jnp.concatenate([part_a, part_b], axis=0).astype(jnp.bfloat16)
        grad_rows_pos = doubling_gather(mine, "wid").reshape((tok_rows, q_cols))
    else:
        parts = []
        for k, piece in enumerate(table_pieces):
            parts.append(
                lax.dot_general(piece, dlogits, (((0,), (1,)), ((), ())), preferred_element_type=jnp.float32)
            )
        full_rows = jnp.zeros((d_cols * n_tok, tok_rows), jnp.float32)
        for k, part in enumerate(parts):
            full_rows = lax.dynamic_update_slice_in_dim(
                full_rows, part, ((t - k) % n_tok) * d_cols, axis=0
            )
        reduced = lax.psum_scatter(full_rows, "voc", scatter_dimension=0, tiled=True)
        grad_rows_t = lax.psum(reduced, "wid").astype(jnp.bfloat16)

    if grad_all is not None:
        hidden_all = jnp.where(
            t == 0,
            jnp.concatenate([hidden, hidden_other], axis=0),
            jnp.concatenate([hidden_other, hidden], axis=0),
        )
        grad_proj = lax.dot_general(
            grad_all, hidden_all, (((0,), (0,)), ((), ())), preferred_element_type=jnp.float32
        )
    elif grad_rows_pos is not None:
        grad_other = lax.ppermute(grad_rows_pos, "tok", [(0, 1), (1, 0)])
        by_pos = (((0,), (0,)), ((), ()))
        grad_proj = lax.dot_general(
            grad_rows_pos, hidden, by_pos, preferred_element_type=jnp.float32
        ) + lax.dot_general(grad_other, hidden_other, by_pos, preferred_element_type=jnp.float32)
    elif n_tok == 2:
        grad_other = lax.ppermute(grad_rows_t, "tok", [(0, 1), (1, 0)])
        first = t == 0
        grad_all = jnp.where(
            first,
            jnp.concatenate([grad_rows_t, grad_other], axis=1),
            jnp.concatenate([grad_other, grad_rows_t], axis=1),
        )
        hidden_all = jnp.where(
            first,
            jnp.concatenate([hidden, hidden_other], axis=0),
            jnp.concatenate([hidden_other, hidden], axis=0),
        )
        grad_proj = jnp.dot(grad_all, hidden_all, preferred_element_type=jnp.float32)
    else:
        grad_all = lax.all_gather(grad_rows_t, "tok", axis=1, tiled=True)
        hidden_all = lax.all_gather(hidden, "tok", axis=0, tiled=True)
        grad_proj = jnp.dot(grad_all, hidden_all, preferred_element_type=jnp.float32)
    loss = sums[0] / sums[1]
    return (grad_proj, loss)


def solution(mesh):
    return jax.shard_map(
        on_device,
        mesh=mesh,
        in_specs=(P("tok", "wid"), P("voc", "wid"), P(("voc", "wid"), "tok"), P("tok"), P("tok")),
        out_specs=(P("voc", "wid"), P()),
        check_vma=False,
    )
```

```python
import jax
import jax.numpy as jnp
from jax import lax
from jax.sharding import PartitionSpec as P


def tok_pieces(x, n_tok):
    pieces = [x]
    for k in range(1, n_tok):
        perm = [(i, (i + k) % n_tok) for i in range(n_tok)]
        pieces.append(lax.ppermute(x, "tok", perm))
    return pieces


def combine(a, b):
    peak = jnp.maximum(a[0], b[0])
    total = a[1] * jnp.exp(a[0] - peak) + b[1] * jnp.exp(b[0] - peak)
    return jnp.stack([peak, total, a[2] + b[2]])


def butterfly(stats, axes):
    for ax in axes:
        n = lax.axis_size(ax)
        if n & (n - 1):
            gathered = lax.all_gather(stats, ax)
            out = gathered[0]
            for i in range(1, n):
                out = combine(out, gathered[i])
            stats = out
            continue
        b = 1
        while b < n:
            other = lax.ppermute(stats, ax, [(i, i ^ b) for i in range(n)])
            stats = combine(stats, other)
            b *= 2
    return stats


def tree_sum(x, ax):
    n = lax.axis_size(ax)
    if n & (n - 1):
        return lax.psum(x, ax)
    b = 1
    while b < n:
        x = x + lax.ppermute(x, ax, [(i, i ^ b) for i in range(n)])
        b *= 2
    return x


def is_pow2(n):
    return n & (n - 1) == 0


def bit_list(ax, n):
    out = []
    b = 1
    while b < n:
        out.append((ax, b))
        b *= 2
    return out


def halving_steps(x, dims, order, bits=None):
    dims = list(dims)
    for ax, b in order:
        pos = dims.index((ax, b))
        n = lax.axis_size(ax)
        bit = (lax.axis_index(ax) // b) % 2 if bits is None else bits[(ax, b)]
        keep = lax.dynamic_index_in_dim(x, bit, axis=pos, keepdims=False)
        send = lax.dynamic_index_in_dim(x, 1 - bit, axis=pos, keepdims=False)
        x = keep + lax.ppermute(send, ax, [(k, k ^ b) for k in range(n)])
        dims.pop(pos)
    return x


def doubling_gather(x, ax):
    n = lax.axis_size(ax)
    i = lax.axis_index(ax)
    b = n // 2
    lead = 0
    while b >= 1:
        other = lax.ppermute(x, ax, [(k, k ^ b) for k in range(n)])
        bit = (i // b) % 2
        x = jnp.where(bit == 0, jnp.stack([x, other], axis=lead), jnp.stack([other, x], axis=lead))
        lead += 1
        b //= 2
    return x.reshape((n,) + x.shape[lead:])


def on_device(hidden, proj, table, targets, valid):
    tok_rows = hidden.shape[0]
    block_rows = table.shape[0]
    n_tok = lax.axis_size("tok")
    t = lax.axis_index("tok")
    d_cols = table.shape[1]

    table_pieces = tok_pieces(table, n_tok)
    if n_tok == 2:
        hidden_other = lax.ppermute(hidden, "tok", [(0, 1), (1, 0)])

    partial_value = lax.dot_general(
        hidden, proj, (((1,), (1,)), ((), ())), preferred_element_type=jnp.float32
    )
    summed = lax.psum(partial_value, "wid")
    if is_pow2(lax.axis_size("voc")):
        quarters = doubling_gather(summed.astype(jnp.bfloat16), "voc")
        projected = quarters.transpose(1, 0, 2).reshape((tok_rows, -1))
    else:
        projected = lax.all_gather(summed.astype(jnp.bfloat16), "voc", axis=1, tiled=True)

    logits = None
    for k, piece in enumerate(table_pieces):
        cols = lax.dynamic_slice_in_dim(projected, ((t - k) % n_tok) * d_cols, d_cols, axis=1)
        part = lax.dot_general(
            cols, piece, (((1,), (1,)), ((), ())), preferred_element_type=jnp.float32
        )
        logits = part if logits is None else logits + part

    block_base = (lax.axis_index("voc") * lax.axis_size("wid") + lax.axis_index("wid")) * block_rows
    local_ids = targets - block_base
    is_target = local_ids[:, None] == lax.broadcasted_iota(jnp.int32, (tok_rows, block_rows), 1)
    picked_here = jnp.sum(jnp.where(is_target, logits, 0.0), axis=1)
    peak_here = jnp.max(logits, axis=1)
    exp_here = jnp.sum(jnp.exp(logits - peak_here[:, None]), axis=1)
    weight = valid.astype(jnp.float32)

    stats = jnp.stack([peak_here, exp_here, picked_here])
    stats = butterfly(stats, ("voc", "wid"))
    log_total = stats[0] + jnp.log(stats[1])
    picked = stats[2]
    sums = jnp.stack([jnp.sum(weight * (log_total - picked)), jnp.sum(weight)])
    sums = tree_sum(sums, "tok")

    dlogits = (
        weight[:, None] * (jnp.exp(logits - log_total[:, None]) - is_target.astype(jnp.float32))
    ).astype(jnp.bfloat16)

    n_voc, n_wid = lax.axis_size("voc"), lax.axis_size("wid")
    grad_rows_pos = None
    grad_path = (
        n_tok == 2
        and n_voc >= 2
        and is_pow2(n_voc)
        and is_pow2(n_wid)
        and tok_rows % (2 * n_wid) == 0
        and d_cols % (n_voc // 2) == 0
    )
    per_piece = 0
    if grad_path:
        per_piece = n_voc // 2
        q_cols = d_cols // per_piece
    if grad_path and per_piece == 2:
        c = lax.axis_index("voc") % 2

        def quarter_dots(sel):
            return jnp.stack(
                [
                    jnp.dot(
                        dlogits,
                        lax.dynamic_slice_in_dim(piece, sel * q_cols, q_cols, axis=1),
                        preferred_element_type=jnp.float32,
                    )
                    for piece in table_pieces
                ]
            )

        sent = quarter_dots(1 - c)
        received = lax.ppermute(sent, "voc", [(k, k ^ 1) for k in range(n_voc)])
        blocks = quarter_dots(c) + received
        voc_bits = bit_list("voc", n_voc)
        wid_bits = bit_list("wid", n_wid)
        v = lax.axis_index("voc")
        bits = {voc_bits[-1]: ((v // per_piece) % 2) ^ t}
        for key in wid_bits:
            bits[key] = (lax.axis_index("wid") // key[1]) % 2
        dims = [voc_bits[-1]] + wid_bits[::-1]
        blocks = blocks.reshape(tuple(2 for _ in dims) + (tok_rows // n_wid, q_cols))
        half = tok_rows // n_wid // 2
        rest_voc = voc_bits[1:]
        part_a = halving_steps(blocks[..., :half, :], dims, rest_voc + wid_bits, bits)
        part_b = halving_steps(blocks[..., half:, :], dims, wid_bits[:1] + rest_voc + wid_bits[1:], bits)
        mine = jnp.concatenate([part_a, part_b], axis=0).astype(jnp.bfloat16)
        grad_rows_pos = doubling_gather(mine, "wid").reshape((tok_rows, q_cols))
    elif grad_path:
        stacked = jnp.stack(
            [
                jnp.stack(
                    [
                        jnp.dot(dlogits, piece[:, i * q_cols : (i + 1) * q_cols], preferred_element_type=jnp.float32)
                        for i in range(per_piece)
                    ]
                )
                for piece in table_pieces
            ]
        )
        voc_bits = bit_list("voc", n_voc)
        wid_bits = bit_list("wid", n_wid)
        v = lax.axis_index("voc")
        bits = {key: (v // key[1]) % 2 for key in voc_bits}
        bits[voc_bits[-1]] = ((v // per_piece) % 2) ^ t
        for key in wid_bits:
            bits[key] = (lax.axis_index("wid") // key[1]) % 2
        dims = [voc_bits[-1]] + voc_bits[:-1][::-1] + wid_bits[::-1]
        blocks = stacked.reshape(tuple(2 for _ in dims) + (tok_rows // n_wid, q_cols))
        first = voc_bits[0]
        blocks = halving_steps(blocks, dims, [first], bits)
        dims = [d for d in dims if d != first]
        half = tok_rows // n_wid // 2
        rest_voc = voc_bits[1:]
        part_a = halving_steps(blocks[..., :half, :], dims, rest_voc + wid_bits, bits)
        part_b = halving_steps(blocks[..., half:, :], dims, wid_bits + rest_voc, bits)
        mine = jnp.concatenate([part_a, part_b], axis=0).astype(jnp.bfloat16)
        grad_rows_pos = doubling_gather(mine, "wid").reshape((tok_rows, q_cols))
    else:
        parts = []
        for k, piece in enumerate(table_pieces):
            parts.append(
                lax.dot_general(piece, dlogits, (((0,), (1,)), ((), ())), preferred_element_type=jnp.float32)
            )
        full_rows = jnp.zeros((d_cols * n_tok, tok_rows), jnp.float32)
        for k, part in enumerate(parts):
            full_rows = lax.dynamic_update_slice_in_dim(
                full_rows, part, ((t - k) % n_tok) * d_cols, axis=0
            )
        reduced = lax.psum_scatter(full_rows, "voc", scatter_dimension=0, tiled=True)
        grad_rows_t = lax.psum(reduced, "wid").astype(jnp.bfloat16)

    if grad_rows_pos is not None:
        grad_other = lax.ppermute(grad_rows_pos, "tok", [(0, 1), (1, 0)])
        by_pos = (((0,), (0,)), ((), ()))
        grad_proj = lax.dot_general(
            grad_rows_pos, hidden, by_pos, preferred_element_type=jnp.float32
        ) + lax.dot_general(grad_other, hidden_other, by_pos, preferred_element_type=jnp.float32)
    elif n_tok == 2:
        grad_other = lax.ppermute(grad_rows_t, "tok", [(0, 1), (1, 0)])
        first = t == 0
        grad_all = jnp.where(
            first,
            jnp.concatenate([grad_rows_t, grad_other], axis=1),
            jnp.concatenate([grad_other, grad_rows_t], axis=1),
        )
        hidden_all = jnp.where(
            first,
            jnp.concatenate([hidden, hidden_other], axis=0),
            jnp.concatenate([hidden_other, hidden], axis=0),
        )
        grad_proj = jnp.dot(grad_all, hidden_all, preferred_element_type=jnp.float32)
    else:
        grad_all = lax.all_gather(grad_rows_t, "tok", axis=1, tiled=True)
        hidden_all = lax.all_gather(hidden, "tok", axis=0, tiled=True)
        grad_proj = jnp.dot(grad_all, hidden_all, preferred_element_type=jnp.float32)
    loss = sums[0] / sums[1]
    return (grad_proj, loss)


def solution(mesh):
    return jax.shard_map(
        on_device,
        mesh=mesh,
        in_specs=(P("tok", "wid"), P("voc", "wid"), P(("voc", "wid"), "tok"), P("tok"), P("tok")),
        out_specs=(P("voc", "wid"), P()),
        check_vma=False,
    )
```

```python
import jax
import jax.numpy as jnp
from jax import lax
from jax.sharding import PartitionSpec as P


def tok_pieces(x, n_tok):
    pieces = [x]
    for k in range(1, n_tok):
        perm = [(i, (i + k) % n_tok) for i in range(n_tok)]
        pieces.append(lax.ppermute(x, "tok", perm))
    return pieces


def combine(a, b):
    peak = jnp.maximum(a[0], b[0])
    total = a[1] * jnp.exp(a[0] - peak) + b[1] * jnp.exp(b[0] - peak)
    return jnp.stack([peak, total, a[2] + b[2]])


def butterfly(stats, axes):
    for ax in axes:
        n = lax.axis_size(ax)
        if n & (n - 1):
            gathered = lax.all_gather(stats, ax)
            out = gathered[0]
            for i in range(1, n):
                out = combine(out, gathered[i])
            stats = out
            continue
        b = 1
        while b < n:
            other = lax.ppermute(stats, ax, [(i, i ^ b) for i in range(n)])
            stats = combine(stats, other)
            b *= 2
    return stats


def tree_sum(x, ax):
    n = lax.axis_size(ax)
    if n & (n - 1):
        return lax.psum(x, ax)
    b = 1
    while b < n:
        x = x + lax.ppermute(x, ax, [(i, i ^ b) for i in range(n)])
        b *= 2
    return x


def is_pow2(n):
    return n & (n - 1) == 0


def bit_list(ax, n):
    out = []
    b = 1
    while b < n:
        out.append((ax, b))
        b *= 2
    return out


def halving_steps(x, dims, order, bits=None):
    dims = list(dims)
    for ax, b in order:
        pos = dims.index((ax, b))
        n = lax.axis_size(ax)
        bit = (lax.axis_index(ax) // b) % 2 if bits is None else bits[(ax, b)]
        keep = lax.dynamic_index_in_dim(x, bit, axis=pos, keepdims=False)
        send = lax.dynamic_index_in_dim(x, 1 - bit, axis=pos, keepdims=False)
        x = keep + lax.ppermute(send, ax, [(k, k ^ b) for k in range(n)])
        dims.pop(pos)
    return x


def doubling_gather(x, ax):
    n = lax.axis_size(ax)
    i = lax.axis_index(ax)
    b = n // 2
    lead = 0
    while b >= 1:
        other = lax.ppermute(x, ax, [(k, k ^ b) for k in range(n)])
        bit = (i // b) % 2
        x = jnp.where(bit == 0, jnp.stack([x, other], axis=lead), jnp.stack([other, x], axis=lead))
        lead += 1
        b //= 2
    return x.reshape((n,) + x.shape[lead:])


def on_device(hidden, proj, table, targets, valid):
    tok_rows = hidden.shape[0]
    block_rows = table.shape[0]
    n_tok = lax.axis_size("tok")
    t = lax.axis_index("tok")
    d_cols = table.shape[1]

    table_pieces = tok_pieces(table, n_tok)
    if n_tok == 2:
        hidden_other = lax.ppermute(hidden, "tok", [(0, 1), (1, 0)])

    partial_value = lax.dot_general(
        hidden, proj, (((1,), (1,)), ((), ())), preferred_element_type=jnp.float32
    )
    summed = lax.psum(partial_value, "wid")
    if is_pow2(lax.axis_size("voc")):
        quarters = doubling_gather(summed.astype(jnp.bfloat16), "voc")
        projected = quarters.transpose(1, 0, 2).reshape((tok_rows, -1))
    else:
        projected = lax.all_gather(summed.astype(jnp.bfloat16), "voc", axis=1, tiled=True)

    logits = None
    for k, piece in enumerate(table_pieces):
        cols = lax.dynamic_slice_in_dim(projected, ((t - k) % n_tok) * d_cols, d_cols, axis=1)
        part = lax.dot_general(
            cols, piece, (((1,), (1,)), ((), ())), preferred_element_type=jnp.float32
        )
        logits = part if logits is None else logits + part

    block_base = (lax.axis_index("voc") * lax.axis_size("wid") + lax.axis_index("wid")) * block_rows
    local_ids = targets - block_base
    is_target = local_ids[:, None] == lax.broadcasted_iota(jnp.int32, (tok_rows, block_rows), 1)
    picked_here = jnp.sum(jnp.where(is_target, logits, 0.0), axis=1)
    peak_here = jnp.max(logits, axis=1)
    exp_here = jnp.sum(jnp.exp(logits - peak_here[:, None]), axis=1)
    weight = valid.astype(jnp.float32)

    stats = jnp.stack([peak_here, exp_here, picked_here])
    stats = butterfly(stats, ("voc", "wid"))
    log_total = stats[0] + jnp.log(stats[1])
    picked = stats[2]
    sums = jnp.stack([jnp.sum(weight * (log_total - picked)), jnp.sum(weight)])
    sums = tree_sum(lax.optimization_barrier(sums), "tok")

    dlogits = (
        weight[:, None] * (jnp.exp(logits - log_total[:, None]) - is_target.astype(jnp.float32))
    ).astype(jnp.bfloat16)

    n_voc, n_wid = lax.axis_size("voc"), lax.axis_size("wid")
    grad_rows_pos = None
    grad_path = (
        n_tok == 2
        and n_voc >= 2
        and is_pow2(n_voc)
        and is_pow2(n_wid)
        and tok_rows % (2 * n_wid) == 0
        and d_cols % (n_voc // 2) == 0
    )
    per_piece = 0
    if grad_path:
        per_piece = n_voc // 2
        q_cols = d_cols // per_piece
    if grad_path and per_piece == 2:
        c = lax.axis_index("voc") % 2

        def quarter_dots(sel):
            return jnp.stack(
                [
                    jnp.dot(
                        dlogits,
                        lax.dynamic_slice_in_dim(piece, sel * q_cols, q_cols, axis=1),
                        preferred_element_type=jnp.float32,
                    )
                    for piece in table_pieces
                ]
            )

        sent = quarter_dots(1 - c)
        received = lax.ppermute(sent, "voc", [(k, k ^ 1) for k in range(n_voc)])
        blocks = quarter_dots(c) + received
        voc_bits = bit_list("voc", n_voc)
        wid_bits = bit_list("wid", n_wid)
        v = lax.axis_index("voc")
        bits = {voc_bits[-1]: ((v // per_piece) % 2) ^ t}
        for key in wid_bits:
            bits[key] = (lax.axis_index("wid") // key[1]) % 2
        dims = [voc_bits[-1]] + wid_bits[::-1]
        blocks = blocks.reshape(tuple(2 for _ in dims) + (tok_rows // n_wid, q_cols))
        half = tok_rows // n_wid // 2
        rest_voc = voc_bits[1:]
        part_a = halving_steps(blocks[..., :half, :], dims, rest_voc + wid_bits, bits)
        part_b = halving_steps(blocks[..., half:, :], dims, wid_bits[:1] + rest_voc + wid_bits[1:], bits)
        mine = jnp.concatenate([part_a, part_b], axis=0).astype(jnp.bfloat16)
        grad_rows_pos = doubling_gather(mine, "wid").reshape((tok_rows, q_cols))
    elif grad_path:
        stacked = jnp.stack(
            [
                jnp.stack(
                    [
                        jnp.dot(dlogits, piece[:, i * q_cols : (i + 1) * q_cols], preferred_element_type=jnp.float32)
                        for i in range(per_piece)
                    ]
                )
                for piece in table_pieces
            ]
        )
        voc_bits = bit_list("voc", n_voc)
        wid_bits = bit_list("wid", n_wid)
        v = lax.axis_index("voc")
        bits = {key: (v // key[1]) % 2 for key in voc_bits}
        bits[voc_bits[-1]] = ((v // per_piece) % 2) ^ t
        for key in wid_bits:
            bits[key] = (lax.axis_index("wid") // key[1]) % 2
        dims = [voc_bits[-1]] + voc_bits[:-1][::-1] + wid_bits[::-1]
        blocks = stacked.reshape(tuple(2 for _ in dims) + (tok_rows // n_wid, q_cols))
        first = voc_bits[0]
        blocks = halving_steps(blocks, dims, [first], bits)
        dims = [d for d in dims if d != first]
        half = tok_rows // n_wid // 2
        rest_voc = voc_bits[1:]
        part_a = halving_steps(blocks[..., :half, :], dims, rest_voc + wid_bits, bits)
        part_b = halving_steps(blocks[..., half:, :], dims, wid_bits + rest_voc, bits)
        mine = jnp.concatenate([part_a, part_b], axis=0).astype(jnp.bfloat16)
        grad_rows_pos = doubling_gather(mine, "wid").reshape((tok_rows, q_cols))
    else:
        parts = []
        for k, piece in enumerate(table_pieces):
            parts.append(
                lax.dot_general(piece, dlogits, (((0,), (1,)), ((), ())), preferred_element_type=jnp.float32)
            )
        full_rows = jnp.zeros((d_cols * n_tok, tok_rows), jnp.float32)
        for k, part in enumerate(parts):
            full_rows = lax.dynamic_update_slice_in_dim(
                full_rows, part, ((t - k) % n_tok) * d_cols, axis=0
            )
        reduced = lax.psum_scatter(full_rows, "voc", scatter_dimension=0, tiled=True)
        grad_rows_t = lax.psum(reduced, "wid").astype(jnp.bfloat16)

    if grad_rows_pos is not None:
        grad_other = lax.ppermute(grad_rows_pos, "tok", [(0, 1), (1, 0)])
        by_pos = (((0,), (0,)), ((), ()))
        grad_proj = lax.dot_general(
            grad_rows_pos, hidden, by_pos, preferred_element_type=jnp.float32
        ) + lax.dot_general(grad_other, hidden_other, by_pos, preferred_element_type=jnp.float32)
    elif n_tok == 2:
        grad_other = lax.ppermute(grad_rows_t, "tok", [(0, 1), (1, 0)])
        first = t == 0
        grad_all = jnp.where(
            first,
            jnp.concatenate([grad_rows_t, grad_other], axis=1),
            jnp.concatenate([grad_other, grad_rows_t], axis=1),
        )
        hidden_all = jnp.where(
            first,
            jnp.concatenate([hidden, hidden_other], axis=0),
            jnp.concatenate([hidden_other, hidden], axis=0),
        )
        grad_proj = jnp.dot(grad_all, hidden_all, preferred_element_type=jnp.float32)
    else:
        grad_all = lax.all_gather(grad_rows_t, "tok", axis=1, tiled=True)
        hidden_all = lax.all_gather(hidden, "tok", axis=0, tiled=True)
        grad_proj = jnp.dot(grad_all, hidden_all, preferred_element_type=jnp.float32)
    loss = sums[0] / sums[1]
    return (grad_proj, loss)


def solution(mesh):
    return jax.shard_map(
        on_device,
        mesh=mesh,
        in_specs=(P("tok", "wid"), P("voc", "wid"), P(("voc", "wid"), "tok"), P("tok"), P("tok")),
        out_specs=(P("voc", "wid"), P()),
        check_vma=False,
    )
```

```python
import jax
import jax.numpy as jnp
from jax import lax
from jax.sharding import PartitionSpec as P


def tok_pieces(x, n_tok):
    pieces = [x]
    for k in range(1, n_tok):
        perm = [(i, (i + k) % n_tok) for i in range(n_tok)]
        pieces.append(lax.ppermute(x, "tok", perm))
    return pieces


def combine(a, b):
    peak = jnp.maximum(a[0], b[0])
    total = a[1] * jnp.exp(a[0] - peak) + b[1] * jnp.exp(b[0] - peak)
    return jnp.stack([peak, total, a[2] + b[2]])


def butterfly(stats, axes):
    for ax in axes:
        n = lax.axis_size(ax)
        if n & (n - 1):
            gathered = lax.all_gather(stats, ax)
            out = gathered[0]
            for i in range(1, n):
                out = combine(out, gathered[i])
            stats = out
            continue
        b = 1
        while b < n:
            other = lax.ppermute(stats, ax, [(i, i ^ b) for i in range(n)])
            stats = combine(stats, other)
            b *= 2
    return stats


def tree_sum(x, ax):
    n = lax.axis_size(ax)
    if n & (n - 1):
        return lax.psum(x, ax)
    b = 1
    while b < n:
        x = x + lax.ppermute(x, ax, [(i, i ^ b) for i in range(n)])
        b *= 2
    return x


def is_pow2(n):
    return n & (n - 1) == 0


def bit_list(ax, n):
    out = []
    b = 1
    while b < n:
        out.append((ax, b))
        b *= 2
    return out


def halving_steps(x, dims, order, bits=None):
    dims = list(dims)
    for ax, b in order:
        pos = dims.index((ax, b))
        n = lax.axis_size(ax)
        bit = (lax.axis_index(ax) // b) % 2 if bits is None else bits[(ax, b)]
        keep = lax.dynamic_index_in_dim(x, bit, axis=pos, keepdims=False)
        send = lax.dynamic_index_in_dim(x, 1 - bit, axis=pos, keepdims=False)
        x = keep + lax.ppermute(send, ax, [(k, k ^ b) for k in range(n)])
        dims.pop(pos)
    return x


def doubling_gather(x, ax):
    n = lax.axis_size(ax)
    i = lax.axis_index(ax)
    b = n // 2
    lead = 0
    while b >= 1:
        other = lax.ppermute(x, ax, [(k, k ^ b) for k in range(n)])
        bit = (i // b) % 2
        x = jnp.where(bit == 0, jnp.stack([x, other], axis=lead), jnp.stack([other, x], axis=lead))
        lead += 1
        b //= 2
    return x.reshape((n,) + x.shape[lead:])


def on_device(hidden, proj, table, targets, valid):
    tok_rows = hidden.shape[0]
    block_rows = table.shape[0]
    n_tok = lax.axis_size("tok")
    t = lax.axis_index("tok")
    d_cols = table.shape[1]

    table_pieces = tok_pieces(table, n_tok)
    if n_tok == 2:
        hidden_other = lax.ppermute(hidden, "tok", [(0, 1), (1, 0)])

    partial_value = lax.dot_general(
        hidden, proj, (((1,), (1,)), ((), ())), preferred_element_type=jnp.float32
    )
    summed = lax.psum(partial_value, "wid")
    if is_pow2(lax.axis_size("voc")):
        quarters = doubling_gather(summed.astype(jnp.bfloat16), "voc")
        projected = quarters.transpose(1, 0, 2).reshape((tok_rows, -1))
    else:
        projected = lax.all_gather(summed.astype(jnp.bfloat16), "voc", axis=1, tiled=True)

    logits = None
    for k, piece in enumerate(table_pieces):
        cols = lax.dynamic_slice_in_dim(projected, ((t - k) % n_tok) * d_cols, d_cols, axis=1)
        part = lax.dot_general(
            cols, piece, (((1,), (1,)), ((), ())), preferred_element_type=jnp.float32
        )
        logits = part if logits is None else logits + part

    block_base = (lax.axis_index("voc") * lax.axis_size("wid") + lax.axis_index("wid")) * block_rows
    local_ids = targets - block_base
    is_target = local_ids[:, None] == lax.broadcasted_iota(jnp.int32, (tok_rows, block_rows), 1)
    picked_here = jnp.sum(jnp.where(is_target, logits, 0.0), axis=1)
    peak_here = jnp.max(logits, axis=1)
    exp_here = jnp.sum(jnp.exp(logits - peak_here[:, None]), axis=1)
    weight = valid.astype(jnp.float32)

    stats = jnp.stack([peak_here, exp_here, picked_here])
    stats = butterfly(stats, ("voc", "wid"))
    log_total = stats[0] + jnp.log(stats[1])
    picked = stats[2]
    sums = jnp.stack([jnp.sum(weight * (log_total - picked)), jnp.sum(weight)])
    sums = tree_sum(sums, "tok")

    dlogits = (
        weight[:, None] * (jnp.exp(logits - log_total[:, None]) - is_target.astype(jnp.float32))
    ).astype(jnp.bfloat16)

    n_voc, n_wid = lax.axis_size("voc"), lax.axis_size("wid")
    grad_rows_pos = None
    grad_path = (
        n_tok == 2
        and n_voc >= 2
        and is_pow2(n_voc)
        and is_pow2(n_wid)
        and tok_rows % (2 * n_wid) == 0
        and d_cols % (n_voc // 2) == 0
    )
    per_piece = 0
    if grad_path:
        per_piece = n_voc // 2
        q_cols = d_cols // per_piece
    if grad_path and per_piece == 2:
        c = lax.axis_index("voc") % 2

        def quarter_dots(sel):
            return jnp.stack(
                [
                    jnp.dot(
                        dlogits,
                        lax.dynamic_slice_in_dim(piece, sel * q_cols, q_cols, axis=1),
                        preferred_element_type=jnp.float32,
                    )
                    for piece in table_pieces
                ]
            )

        sent = quarter_dots(1 - c)
        received = lax.ppermute(sent, "voc", [(k, k ^ 1) for k in range(n_voc)])
        blocks = quarter_dots(c) + received
        voc_bits = bit_list("voc", n_voc)
        wid_bits = bit_list("wid", n_wid)
        v = lax.axis_index("voc")
        bits = {voc_bits[-1]: ((v // per_piece) % 2) ^ t}
        for key in wid_bits:
            bits[key] = (lax.axis_index("wid") // key[1]) % 2
        dims = [voc_bits[-1]] + wid_bits[::-1]
        blocks = blocks.reshape(tuple(2 for _ in dims) + (tok_rows // n_wid, q_cols))
        half = tok_rows // n_wid // 2
        rest_voc = voc_bits[1:]
        part_a = halving_steps(blocks[..., :half, :], dims, rest_voc + wid_bits, bits)
        part_b = halving_steps(blocks[..., half:, :], dims, wid_bits[:1] + rest_voc + wid_bits[1:], bits)
        mine = jnp.concatenate([part_a, part_b], axis=0).astype(jnp.bfloat16)
        grad_rows_pos = doubling_gather(mine, "wid").reshape((tok_rows, q_cols))
    elif grad_path:
        stacked = jnp.stack(
            [
                jnp.stack(
                    [
                        jnp.dot(dlogits, piece[:, i * q_cols : (i + 1) * q_cols], preferred_element_type=jnp.float32)
                        for i in range(per_piece)
                    ]
                )
                for piece in table_pieces
            ]
        )
        voc_bits = bit_list("voc", n_voc)
        wid_bits = bit_list("wid", n_wid)
        v = lax.axis_index("voc")
        bits = {key: (v // key[1]) % 2 for key in voc_bits}
        bits[voc_bits[-1]] = ((v // per_piece) % 2) ^ t
        for key in wid_bits:
            bits[key] = (lax.axis_index("wid") // key[1]) % 2
        dims = [voc_bits[-1]] + voc_bits[:-1][::-1] + wid_bits[::-1]
        blocks = stacked.reshape(tuple(2 for _ in dims) + (tok_rows // n_wid, q_cols))
        first = voc_bits[0]
        blocks = halving_steps(blocks, dims, [first], bits)
        dims = [d for d in dims if d != first]
        half = tok_rows // n_wid // 2
        rest_voc = voc_bits[1:]
        part_a = halving_steps(blocks[..., :half, :], dims, rest_voc + wid_bits, bits)
        part_b = halving_steps(blocks[..., half:, :], dims, wid_bits + rest_voc, bits)
        mine = jnp.concatenate([part_a, part_b], axis=0).astype(jnp.bfloat16)
        grad_rows_pos = doubling_gather(mine, "wid").reshape((tok_rows, q_cols))
    else:
        parts = []
        for k, piece in enumerate(table_pieces):
            parts.append(
                lax.dot_general(piece, dlogits, (((0,), (1,)), ((), ())), preferred_element_type=jnp.float32)
            )
        full_rows = jnp.zeros((d_cols * n_tok, tok_rows), jnp.float32)
        for k, part in enumerate(parts):
            full_rows = lax.dynamic_update_slice_in_dim(
                full_rows, part, ((t - k) % n_tok) * d_cols, axis=0
            )
        reduced = lax.psum_scatter(full_rows, "voc", scatter_dimension=0, tiled=True)
        grad_rows_t = lax.psum(reduced, "wid").astype(jnp.bfloat16)

    if grad_rows_pos is not None:
        half_rows = tok_rows // 2
        by_pos = (((0,), (0,)), ((), ()))
        sums_of = []
        for rows, hid in ((grad_rows_pos, hidden), (None, hidden_other)):
            if rows is None:
                rows = [
                    lax.ppermute(grad_rows_pos[i * half_rows : (i + 1) * half_rows], "tok", [(0, 1), (1, 0)])
                    for i in range(2)
                ]
            else:
                rows = [rows[i * half_rows : (i + 1) * half_rows] for i in range(2)]
            dots = [
                lax.dot_general(rows[i], hid[i * half_rows : (i + 1) * half_rows], by_pos, preferred_element_type=jnp.float32)
                for i in range(2)
            ]
            sums_of.append(dots[0] + dots[1])
        grad_proj = sums_of[0] + sums_of[1]
    elif n_tok == 2:
        grad_other = lax.ppermute(grad_rows_t, "tok", [(0, 1), (1, 0)])
        first = t == 0
        grad_all = jnp.where(
            first,
            jnp.concatenate([grad_rows_t, grad_other], axis=1),
            jnp.concatenate([grad_other, grad_rows_t], axis=1),
        )
        hidden_all = jnp.where(
            first,
            jnp.concatenate([hidden, hidden_other], axis=0),
            jnp.concatenate([hidden_other, hidden], axis=0),
        )
        grad_proj = jnp.dot(grad_all, hidden_all, preferred_element_type=jnp.float32)
    else:
        grad_all = lax.all_gather(grad_rows_t, "tok", axis=1, tiled=True)
        hidden_all = lax.all_gather(hidden, "tok", axis=0, tiled=True)
        grad_proj = jnp.dot(grad_all, hidden_all, preferred_element_type=jnp.float32)
    loss = sums[0] / sums[1]
    return (grad_proj, loss)


def solution(mesh):
    return jax.shard_map(
        on_device,
        mesh=mesh,
        in_specs=(P("tok", "wid"), P("voc", "wid"), P(("voc", "wid"), "tok"), P("tok"), P("tok")),
        out_specs=(P("voc", "wid"), P()),
        check_vma=False,
    )
```

```python
import jax
import jax.numpy as jnp
from jax import lax
from jax.sharding import PartitionSpec as P


def tok_pieces(x, n_tok):
    pieces = [x]
    for k in range(1, n_tok):
        perm = [(i, (i + k) % n_tok) for i in range(n_tok)]
        pieces.append(lax.ppermute(x, "tok", perm))
    return pieces


def combine(a, b):
    peak = jnp.maximum(a[0], b[0])
    total = a[1] * jnp.exp(a[0] - peak) + b[1] * jnp.exp(b[0] - peak)
    return jnp.stack([peak, total, a[2] + b[2]])


def butterfly(stats, axes):
    for ax in axes:
        n = lax.axis_size(ax)
        if n & (n - 1):
            gathered = lax.all_gather(stats, ax)
            out = gathered[0]
            for i in range(1, n):
                out = combine(out, gathered[i])
            stats = out
            continue
        b = 1
        while b < n:
            other = lax.ppermute(stats, ax, [(i, i ^ b) for i in range(n)])
            stats = combine(stats, other)
            b *= 2
    return stats


def shift_gather(x, ax):
    n = lax.axis_size(ax)
    got = [x] + [lax.ppermute(x, ax, [(k, (k + sh) % n) for k in range(n)]) for sh in range(1, n)]
    rev = jnp.stack([got[(-j) % n] for j in range(n)])
    return jnp.roll(rev, lax.axis_index(ax), axis=0)


def gather_combine(stats, axes):
    for ax in axes:
        g = shift_gather(stats, ax)
        out = g[0]
        for k in range(1, g.shape[0]):
            out = combine(out, g[k])
        stats = out
    return stats


def tree_sum(x, ax):
    n = lax.axis_size(ax)
    if n & (n - 1):
        return lax.psum(x, ax)
    b = 1
    while b < n:
        x = x + lax.ppermute(x, ax, [(i, i ^ b) for i in range(n)])
        b *= 2
    return x


def is_pow2(n):
    return n & (n - 1) == 0


def bit_list(ax, n):
    out = []
    b = 1
    while b < n:
        out.append((ax, b))
        b *= 2
    return out


def halving_steps(x, dims, order, bits=None):
    dims = list(dims)
    for ax, b in order:
        pos = dims.index((ax, b))
        n = lax.axis_size(ax)
        bit = (lax.axis_index(ax) // b) % 2 if bits is None else bits[(ax, b)]
        keep = lax.dynamic_index_in_dim(x, bit, axis=pos, keepdims=False)
        send = lax.dynamic_index_in_dim(x, 1 - bit, axis=pos, keepdims=False)
        x = keep + lax.ppermute(send, ax, [(k, k ^ b) for k in range(n)])
        dims.pop(pos)
    return x


def doubling_gather(x, ax):
    n = lax.axis_size(ax)
    i = lax.axis_index(ax)
    b = n // 2
    lead = 0
    while b >= 1:
        other = lax.ppermute(x, ax, [(k, k ^ b) for k in range(n)])
        bit = (i // b) % 2
        x = jnp.where(bit == 0, jnp.stack([x, other], axis=lead), jnp.stack([other, x], axis=lead))
        lead += 1
        b //= 2
    return x.reshape((n,) + x.shape[lead:])


def on_device(hidden, proj, table, targets, valid):
    tok_rows = hidden.shape[0]
    block_rows = table.shape[0]
    n_tok = lax.axis_size("tok")
    t = lax.axis_index("tok")
    d_cols = table.shape[1]

    table_pieces = tok_pieces(table, n_tok)
    if n_tok == 2:
        hidden_other = lax.ppermute(hidden, "tok", [(0, 1), (1, 0)])

    partial_value = lax.dot_general(
        hidden, proj, (((1,), (1,)), ((), ())), preferred_element_type=jnp.float32
    )
    summed = lax.psum(partial_value, "wid")
    if is_pow2(lax.axis_size("voc")):
        quarters = doubling_gather(summed.astype(jnp.bfloat16), "voc")
        projected = quarters.transpose(1, 0, 2).reshape((tok_rows, -1))
    else:
        projected = lax.all_gather(summed.astype(jnp.bfloat16), "voc", axis=1, tiled=True)

    logits = None
    for k, piece in enumerate(table_pieces):
        cols = lax.dynamic_slice_in_dim(projected, ((t - k) % n_tok) * d_cols, d_cols, axis=1)
        part = lax.dot_general(
            cols, piece, (((1,), (1,)), ((), ())), preferred_element_type=jnp.float32
        )
        logits = part if logits is None else logits + part

    block_base = (lax.axis_index("voc") * lax.axis_size("wid") + lax.axis_index("wid")) * block_rows
    local_ids = targets - block_base
    is_target = local_ids[:, None] == lax.broadcasted_iota(jnp.int32, (tok_rows, block_rows), 1)
    picked_here = jnp.sum(jnp.where(is_target, logits, 0.0), axis=1)
    peak_here = jnp.max(logits, axis=1)
    exp_here = jnp.sum(jnp.exp(logits - peak_here[:, None]), axis=1)
    weight = valid.astype(jnp.float32)

    stats = jnp.stack([peak_here, exp_here, picked_here])
    stats = gather_combine(stats, ("voc", "wid"))
    log_total = stats[0] + jnp.log(stats[1])
    picked = stats[2]
    sums = jnp.stack([jnp.sum(weight * (log_total - picked)), jnp.sum(weight)])
    sums = tree_sum(sums, "tok")

    dlogits = (
        weight[:, None] * (jnp.exp(logits - log_total[:, None]) - is_target.astype(jnp.float32))
    ).astype(jnp.bfloat16)

    n_voc, n_wid = lax.axis_size("voc"), lax.axis_size("wid")
    grad_rows_pos = None
    grad_path = (
        n_tok == 2
        and n_voc >= 2
        and is_pow2(n_voc)
        and is_pow2(n_wid)
        and tok_rows % (2 * n_wid) == 0
        and d_cols % (n_voc // 2) == 0
    )
    per_piece = 0
    if grad_path:
        per_piece = n_voc // 2
        q_cols = d_cols // per_piece
    if grad_path and per_piece == 2:
        c = lax.axis_index("voc") % 2

        def quarter_dots(sel):
            return jnp.stack(
                [
                    jnp.dot(
                        dlogits,
                        lax.dynamic_slice_in_dim(piece, sel * q_cols, q_cols, axis=1),
                        preferred_element_type=jnp.float32,
                    )
                    for piece in table_pieces
                ]
            )

        sent = quarter_dots(1 - c)
        received = lax.ppermute(sent, "voc", [(k, k ^ 1) for k in range(n_voc)])
        blocks = quarter_dots(c) + received
        voc_bits = bit_list("voc", n_voc)
        wid_bits = bit_list("wid", n_wid)
        v = lax.axis_index("voc")
        bits = {voc_bits[-1]: ((v // per_piece) % 2) ^ t}
        for key in wid_bits:
            bits[key] = (lax.axis_index("wid") // key[1]) % 2
        dims = [voc_bits[-1]] + wid_bits[::-1]
        blocks = blocks.reshape(tuple(2 for _ in dims) + (tok_rows // n_wid, q_cols))
        half = tok_rows // n_wid // 2
        rest_voc = voc_bits[1:]
        part_a = halving_steps(blocks[..., :half, :], dims, rest_voc + wid_bits, bits)
        part_b = halving_steps(blocks[..., half:, :], dims, wid_bits[:1] + rest_voc + wid_bits[1:], bits)
        mine = jnp.concatenate([part_a, part_b], axis=0).astype(jnp.bfloat16)
        grad_rows_pos = doubling_gather(mine, "wid").reshape((tok_rows, q_cols))
    elif grad_path:
        stacked = jnp.stack(
            [
                jnp.stack(
                    [
                        jnp.dot(dlogits, piece[:, i * q_cols : (i + 1) * q_cols], preferred_element_type=jnp.float32)
                        for i in range(per_piece)
                    ]
                )
                for piece in table_pieces
            ]
        )
        voc_bits = bit_list("voc", n_voc)
        wid_bits = bit_list("wid", n_wid)
        v = lax.axis_index("voc")
        bits = {key: (v // key[1]) % 2 for key in voc_bits}
        bits[voc_bits[-1]] = ((v // per_piece) % 2) ^ t
        for key in wid_bits:
            bits[key] = (lax.axis_index("wid") // key[1]) % 2
        dims = [voc_bits[-1]] + voc_bits[:-1][::-1] + wid_bits[::-1]
        blocks = stacked.reshape(tuple(2 for _ in dims) + (tok_rows // n_wid, q_cols))
        first = voc_bits[0]
        blocks = halving_steps(blocks, dims, [first], bits)
        dims = [d for d in dims if d != first]
        half = tok_rows // n_wid // 2
        rest_voc = voc_bits[1:]
        part_a = halving_steps(blocks[..., :half, :], dims, rest_voc + wid_bits, bits)
        part_b = halving_steps(blocks[..., half:, :], dims, wid_bits + rest_voc, bits)
        mine = jnp.concatenate([part_a, part_b], axis=0).astype(jnp.bfloat16)
        grad_rows_pos = doubling_gather(mine, "wid").reshape((tok_rows, q_cols))
    else:
        parts = []
        for k, piece in enumerate(table_pieces):
            parts.append(
                lax.dot_general(piece, dlogits, (((0,), (1,)), ((), ())), preferred_element_type=jnp.float32)
            )
        full_rows = jnp.zeros((d_cols * n_tok, tok_rows), jnp.float32)
        for k, part in enumerate(parts):
            full_rows = lax.dynamic_update_slice_in_dim(
                full_rows, part, ((t - k) % n_tok) * d_cols, axis=0
            )
        reduced = lax.psum_scatter(full_rows, "voc", scatter_dimension=0, tiled=True)
        grad_rows_t = lax.psum(reduced, "wid").astype(jnp.bfloat16)

    if grad_rows_pos is not None:
        half_rows = tok_rows // 2
        by_pos = (((0,), (0,)), ((), ()))
        sums_of = []
        for rows, hid in ((grad_rows_pos, hidden), (None, hidden_other)):
            if rows is None:
                rows = [
                    lax.ppermute(grad_rows_pos[i * half_rows : (i + 1) * half_rows], "tok", [(0, 1), (1, 0)])
                    for i in range(2)
                ]
            else:
                rows = [rows[i * half_rows : (i + 1) * half_rows] for i in range(2)]
            dots = [
                lax.dot_general(rows[i], hid[i * half_rows : (i + 1) * half_rows], by_pos, preferred_element_type=jnp.float32)
                for i in range(2)
            ]
            sums_of.append(dots[0] + dots[1])
        grad_proj = sums_of[0] + sums_of[1]
    elif n_tok == 2:
        grad_other = lax.ppermute(grad_rows_t, "tok", [(0, 1), (1, 0)])
        first = t == 0
        grad_all = jnp.where(
            first,
            jnp.concatenate([grad_rows_t, grad_other], axis=1),
            jnp.concatenate([grad_other, grad_rows_t], axis=1),
        )
        hidden_all = jnp.where(
            first,
            jnp.concatenate([hidden, hidden_other], axis=0),
            jnp.concatenate([hidden_other, hidden], axis=0),
        )
        grad_proj = jnp.dot(grad_all, hidden_all, preferred_element_type=jnp.float32)
    else:
        grad_all = lax.all_gather(grad_rows_t, "tok", axis=1, tiled=True)
        hidden_all = lax.all_gather(hidden, "tok", axis=0, tiled=True)
        grad_proj = jnp.dot(grad_all, hidden_all, preferred_element_type=jnp.float32)
    loss = sums[0] / sums[1]
    return (grad_proj, loss)


def solution(mesh):
    return jax.shard_map(
        on_device,
        mesh=mesh,
        in_specs=(P("tok", "wid"), P("voc", "wid"), P(("voc", "wid"), "tok"), P("tok"), P("tok")),
        out_specs=(P("voc", "wid"), P()),
        check_vma=False,
    )
```

```python
import jax
import jax.numpy as jnp
from jax import lax
from jax.sharding import PartitionSpec as P


def tok_pieces(x, n_tok):
    pieces = [x]
    for k in range(1, n_tok):
        perm = [(i, (i + k) % n_tok) for i in range(n_tok)]
        pieces.append(lax.ppermute(x, "tok", perm))
    return pieces


def combine(a, b):
    peak = jnp.maximum(a[0], b[0])
    total = a[1] * jnp.exp(a[0] - peak) + b[1] * jnp.exp(b[0] - peak)
    return jnp.stack([peak, total, a[2] + b[2]])


def butterfly(stats, axes):
    for ax in axes:
        n = lax.axis_size(ax)
        if n & (n - 1):
            gathered = lax.all_gather(stats, ax)
            out = gathered[0]
            for i in range(1, n):
                out = combine(out, gathered[i])
            stats = out
            continue
        b = 1
        while b < n:
            other = lax.ppermute(stats, ax, [(i, i ^ b) for i in range(n)])
            stats = combine(stats, other)
            b *= 2
    return stats


def tree_sum(x, ax):
    n = lax.axis_size(ax)
    if n & (n - 1):
        return lax.psum(x, ax)
    b = 1
    while b < n:
        x = x + lax.ppermute(x, ax, [(i, i ^ b) for i in range(n)])
        b *= 2
    return x


def is_pow2(n):
    return n & (n - 1) == 0


def bit_list(ax, n):
    out = []
    b = 1
    while b < n:
        out.append((ax, b))
        b *= 2
    return out


def halving_steps(x, dims, order, bits=None):
    dims = list(dims)
    for ax, b in order:
        pos = dims.index((ax, b))
        n = lax.axis_size(ax)
        bit = (lax.axis_index(ax) // b) % 2 if bits is None else bits[(ax, b)]
        keep = lax.dynamic_index_in_dim(x, bit, axis=pos, keepdims=False)
        send = lax.dynamic_index_in_dim(x, 1 - bit, axis=pos, keepdims=False)
        x = keep + lax.ppermute(send, ax, [(k, k ^ b) for k in range(n)])
        dims.pop(pos)
    return x


def doubling_gather(x, ax):
    n = lax.axis_size(ax)
    i = lax.axis_index(ax)
    b = n // 2
    lead = 0
    while b >= 1:
        other = lax.ppermute(x, ax, [(k, k ^ b) for k in range(n)])
        bit = (i // b) % 2
        x = jnp.where(bit == 0, jnp.stack([x, other], axis=lead), jnp.stack([other, x], axis=lead))
        lead += 1
        b //= 2
    return x.reshape((n,) + x.shape[lead:])


def on_device(hidden, proj, table, targets, valid):
    tok_rows = hidden.shape[0]
    block_rows = table.shape[0]
    n_tok = lax.axis_size("tok")
    t = lax.axis_index("tok")
    d_cols = table.shape[1]

    table_pieces = tok_pieces(table, n_tok)
    if n_tok == 2:
        hidden_other = lax.ppermute(hidden, "tok", [(0, 1), (1, 0)])

    partial_value = lax.dot_general(
        hidden, proj, (((1,), (1,)), ((), ())), preferred_element_type=jnp.float32
    )
    summed = lax.psum(partial_value, "wid")
    if is_pow2(lax.axis_size("voc")):
        quarters = doubling_gather(summed.astype(jnp.bfloat16), "voc")
        projected = quarters.transpose(1, 0, 2).reshape((tok_rows, -1))
    else:
        projected = lax.all_gather(summed.astype(jnp.bfloat16), "voc", axis=1, tiled=True)

    logits = None
    for k, piece in enumerate(table_pieces):
        cols = lax.dynamic_slice_in_dim(projected, ((t - k) % n_tok) * d_cols, d_cols, axis=1)
        part = lax.dot_general(
            piece, cols, (((1,), (1,)), ((), ())), preferred_element_type=jnp.float32
        )
        logits = part if logits is None else logits + part

    block_base = (lax.axis_index("voc") * lax.axis_size("wid") + lax.axis_index("wid")) * block_rows
    local_ids = targets - block_base
    is_target = local_ids[None, :] == lax.broadcasted_iota(jnp.int32, (block_rows, tok_rows), 0)
    picked_here = jnp.sum(jnp.where(is_target, logits, 0.0), axis=0)
    peak_here = jnp.max(logits, axis=0)
    exp_here = jnp.sum(jnp.exp(logits - peak_here[None, :]), axis=0)
    weight = valid.astype(jnp.float32)

    stats = jnp.stack([peak_here, exp_here, picked_here])
    stats = butterfly(stats, ("voc", "wid"))
    log_total = stats[0] + jnp.log(stats[1])
    picked = stats[2]
    sums = jnp.stack([jnp.sum(weight * (log_total - picked)), jnp.sum(weight)])
    sums = tree_sum(sums, "tok")

    dlogits = (
        (weight[None, :] * (jnp.exp(logits - log_total[None, :]) - is_target.astype(jnp.float32)))
        .astype(jnp.bfloat16)
        .T
    )

    n_voc, n_wid = lax.axis_size("voc"), lax.axis_size("wid")
    grad_rows_pos = None
    grad_path = (
        n_tok == 2
        and n_voc >= 2
        and is_pow2(n_voc)
        and is_pow2(n_wid)
        and tok_rows % (2 * n_wid) == 0
        and d_cols % (n_voc // 2) == 0
    )
    per_piece = 0
    if grad_path:
        per_piece = n_voc // 2
        q_cols = d_cols // per_piece
    if grad_path and per_piece == 2:
        c = lax.axis_index("voc") % 2

        def quarter_dots(sel):
            return jnp.stack(
                [
                    jnp.dot(
                        dlogits,
                        lax.dynamic_slice_in_dim(piece, sel * q_cols, q_cols, axis=1),
                        preferred_element_type=jnp.float32,
                    )
                    for piece in table_pieces
                ]
            )

        sent = quarter_dots(1 - c)
        received = lax.ppermute(sent, "voc", [(k, k ^ 1) for k in range(n_voc)])
        blocks = quarter_dots(c) + received
        voc_bits = bit_list("voc", n_voc)
        wid_bits = bit_list("wid", n_wid)
        v = lax.axis_index("voc")
        bits = {voc_bits[-1]: ((v // per_piece) % 2) ^ t}
        for key in wid_bits:
            bits[key] = (lax.axis_index("wid") // key[1]) % 2
        dims = [voc_bits[-1]] + wid_bits[::-1]
        blocks = blocks.reshape(tuple(2 for _ in dims) + (tok_rows // n_wid, q_cols))
        half = tok_rows // n_wid // 2
        rest_voc = voc_bits[1:]
        part_a = halving_steps(blocks[..., :half, :], dims, rest_voc + wid_bits, bits)
        part_b = halving_steps(blocks[..., half:, :], dims, wid_bits[:1] + rest_voc + wid_bits[1:], bits)
        mine = jnp.concatenate([part_a, part_b], axis=0).astype(jnp.bfloat16)
        grad_rows_pos = doubling_gather(mine, "wid").reshape((tok_rows, q_cols))
    elif grad_path:
        stacked = jnp.stack(
            [
                jnp.stack(
                    [
                        jnp.dot(dlogits, piece[:, i * q_cols : (i + 1) * q_cols], preferred_element_type=jnp.float32)
                        for i in range(per_piece)
                    ]
                )
                for piece in table_pieces
            ]
        )
        voc_bits = bit_list("voc", n_voc)
        wid_bits = bit_list("wid", n_wid)
        v = lax.axis_index("voc")
        bits = {key: (v // key[1]) % 2 for key in voc_bits}
        bits[voc_bits[-1]] = ((v // per_piece) % 2) ^ t
        for key in wid_bits:
            bits[key] = (lax.axis_index("wid") // key[1]) % 2
        dims = [voc_bits[-1]] + voc_bits[:-1][::-1] + wid_bits[::-1]
        blocks = stacked.reshape(tuple(2 for _ in dims) + (tok_rows // n_wid, q_cols))
        first = voc_bits[0]
        blocks = halving_steps(blocks, dims, [first], bits)
        dims = [d for d in dims if d != first]
        half = tok_rows // n_wid // 2
        rest_voc = voc_bits[1:]
        part_a = halving_steps(blocks[..., :half, :], dims, rest_voc + wid_bits, bits)
        part_b = halving_steps(blocks[..., half:, :], dims, wid_bits + rest_voc, bits)
        mine = jnp.concatenate([part_a, part_b], axis=0).astype(jnp.bfloat16)
        grad_rows_pos = doubling_gather(mine, "wid").reshape((tok_rows, q_cols))
    else:
        parts = []
        for k, piece in enumerate(table_pieces):
            parts.append(
                lax.dot_general(piece, dlogits, (((0,), (1,)), ((), ())), preferred_element_type=jnp.float32)
            )
        full_rows = jnp.zeros((d_cols * n_tok, tok_rows), jnp.float32)
        for k, part in enumerate(parts):
            full_rows = lax.dynamic_update_slice_in_dim(
                full_rows, part, ((t - k) % n_tok) * d_cols, axis=0
            )
        reduced = lax.psum_scatter(full_rows, "voc", scatter_dimension=0, tiled=True)
        grad_rows_t = lax.psum(reduced, "wid").astype(jnp.bfloat16)

    if grad_rows_pos is not None:
        half_rows = tok_rows // 2
        by_pos = (((0,), (0,)), ((), ()))
        sums_of = []
        for rows, hid in ((grad_rows_pos, hidden), (None, hidden_other)):
            if rows is None:
                rows = [
                    lax.ppermute(grad_rows_pos[i * half_rows : (i + 1) * half_rows], "tok", [(0, 1), (1, 0)])
                    for i in range(2)
                ]
            else:
                rows = [rows[i * half_rows : (i + 1) * half_rows] for i in range(2)]
            dots = [
                lax.dot_general(rows[i], hid[i * half_rows : (i + 1) * half_rows], by_pos, preferred_element_type=jnp.float32)
                for i in range(2)
            ]
            sums_of.append(dots[0] + dots[1])
        grad_proj = sums_of[0] + sums_of[1]
    elif n_tok == 2:
        grad_other = lax.ppermute(grad_rows_t, "tok", [(0, 1), (1, 0)])
        first = t == 0
        grad_all = jnp.where(
            first,
            jnp.concatenate([grad_rows_t, grad_other], axis=1),
            jnp.concatenate([grad_other, grad_rows_t], axis=1),
        )
        hidden_all = jnp.where(
            first,
            jnp.concatenate([hidden, hidden_other], axis=0),
            jnp.concatenate([hidden_other, hidden], axis=0),
        )
        grad_proj = jnp.dot(grad_all, hidden_all, preferred_element_type=jnp.float32)
    else:
        grad_all = lax.all_gather(grad_rows_t, "tok", axis=1, tiled=True)
        hidden_all = lax.all_gather(hidden, "tok", axis=0, tiled=True)
        grad_proj = jnp.dot(grad_all, hidden_all, preferred_element_type=jnp.float32)
    loss = sums[0] / sums[1]
    return (grad_proj, loss)


def solution(mesh):
    return jax.shard_map(
        on_device,
        mesh=mesh,
        in_specs=(P("tok", "wid"), P("voc", "wid"), P(("voc", "wid"), "tok"), P("tok"), P("tok")),
        out_specs=(P("voc", "wid"), P()),
        check_vma=False,
    )
```

```python
import jax
import jax.numpy as jnp
from jax import lax
from jax.sharding import PartitionSpec as P


def tok_pieces(x, n_tok):
    pieces = [x]
    for k in range(1, n_tok):
        perm = [(i, (i + k) % n_tok) for i in range(n_tok)]
        pieces.append(lax.ppermute(x, "tok", perm))
    return pieces


def combine(a, b):
    peak = jnp.maximum(a[0], b[0])
    total = a[1] * jnp.exp(a[0] - peak) + b[1] * jnp.exp(b[0] - peak)
    return jnp.stack([peak, total, a[2] + b[2]])


def butterfly(stats, axes):
    for ax in axes:
        n = lax.axis_size(ax)
        if n & (n - 1):
            gathered = lax.all_gather(stats, ax)
            out = gathered[0]
            for i in range(1, n):
                out = combine(out, gathered[i])
            stats = out
            continue
        b = 1
        while b < n:
            other = lax.ppermute(stats, ax, [(i, i ^ b) for i in range(n)])
            stats = combine(stats, other)
            b *= 2
    return stats


def tree_sum(x, ax):
    n = lax.axis_size(ax)
    if n & (n - 1):
        return lax.psum(x, ax)
    b = 1
    while b < n:
        x = x + lax.ppermute(x, ax, [(i, i ^ b) for i in range(n)])
        b *= 2
    return x


def is_pow2(n):
    return n & (n - 1) == 0


def bit_list(ax, n):
    out = []
    b = 1
    while b < n:
        out.append((ax, b))
        b *= 2
    return out


def halving_steps(x, dims, order, bits=None):
    dims = list(dims)
    for ax, b in order:
        pos = dims.index((ax, b))
        n = lax.axis_size(ax)
        bit = (lax.axis_index(ax) // b) % 2 if bits is None else bits[(ax, b)]
        keep = lax.dynamic_index_in_dim(x, bit, axis=pos, keepdims=False)
        send = lax.dynamic_index_in_dim(x, 1 - bit, axis=pos, keepdims=False)
        x = keep + lax.ppermute(send, ax, [(k, k ^ b) for k in range(n)])
        dims.pop(pos)
    return x


def doubling_gather(x, ax):
    n = lax.axis_size(ax)
    i = lax.axis_index(ax)
    b = n // 2
    lead = 0
    while b >= 1:
        other = lax.ppermute(x, ax, [(k, k ^ b) for k in range(n)])
        bit = (i // b) % 2
        x = jnp.where(bit == 0, jnp.stack([x, other], axis=lead), jnp.stack([other, x], axis=lead))
        lead += 1
        b //= 2
    return x.reshape((n,) + x.shape[lead:])


def on_device(hidden, proj, table, targets, valid):
    tok_rows = hidden.shape[0]
    block_rows = table.shape[0]
    n_tok = lax.axis_size("tok")
    t = lax.axis_index("tok")
    d_cols = table.shape[1]

    n_wid_early = lax.axis_size("wid")
    chunked = (
        n_tok == 2
        and block_rows % 32 == 0
        and lax.axis_size("voc") == 4
        and is_pow2(n_wid_early)
        and tok_rows % (2 * n_wid_early) == 0
        and d_cols % 2 == 0
    )
    if chunked:
        r1 = block_rows // 2
        swap = [(0, 1), (1, 0)]
        other_chunks = [lax.ppermute(table[:r1], "tok", swap), lax.ppermute(table[r1:], "tok", swap)]
        table_pieces = [table]
    else:
        table_pieces = tok_pieces(table, n_tok)
    if n_tok == 2:
        hidden_other = lax.ppermute(hidden, "tok", [(0, 1), (1, 0)])

    partial_value = lax.dot_general(
        hidden, proj, (((1,), (1,)), ((), ())), preferred_element_type=jnp.float32
    )
    summed = lax.psum(partial_value, "wid")
    if is_pow2(lax.axis_size("voc")):
        quarters = doubling_gather(summed.astype(jnp.bfloat16), "voc")
        projected = quarters.transpose(1, 0, 2).reshape((tok_rows, -1))
    else:
        projected = lax.all_gather(summed.astype(jnp.bfloat16), "voc", axis=1, tiled=True)

    logits = None
    for k, piece in enumerate(table_pieces):
        cols = lax.dynamic_slice_in_dim(projected, ((t - k) % n_tok) * d_cols, d_cols, axis=1)
        part = lax.dot_general(
            piece, cols, (((1,), (1,)), ((), ())), preferred_element_type=jnp.float32
        )
        logits = part if logits is None else logits + part
    if chunked:
        cols = lax.dynamic_slice_in_dim(projected, (1 - t) * d_cols, d_cols, axis=1)
        logits = logits + jnp.concatenate(
            [
                lax.dot_general(ch, cols, (((1,), (1,)), ((), ())), preferred_element_type=jnp.float32)
                for ch in other_chunks
            ],
            axis=0,
        )

    block_base = (lax.axis_index("voc") * lax.axis_size("wid") + lax.axis_index("wid")) * block_rows
    local_ids = targets - block_base
    is_target = local_ids[None, :] == lax.broadcasted_iota(jnp.int32, (block_rows, tok_rows), 0)
    picked_here = jnp.sum(jnp.where(is_target, logits, 0.0), axis=0)
    peak_here = jnp.max(logits, axis=0)
    exp_here = jnp.sum(jnp.exp(logits - peak_here[None, :]), axis=0)
    weight = valid.astype(jnp.float32)

    stats = jnp.stack([peak_here, exp_here, picked_here])
    stats = butterfly(stats, ("voc", "wid"))
    log_total = stats[0] + jnp.log(stats[1])
    picked = stats[2]
    sums = jnp.stack([jnp.sum(weight * (log_total - picked)), jnp.sum(weight)])
    sums = tree_sum(sums, "tok")

    dlogits = (
        (weight[None, :] * (jnp.exp(logits - log_total[None, :]) - is_target.astype(jnp.float32)))
        .astype(jnp.bfloat16)
        .T
    )

    n_voc, n_wid = lax.axis_size("voc"), lax.axis_size("wid")
    grad_rows_pos = None
    grad_path = (
        n_tok == 2
        and n_voc >= 2
        and is_pow2(n_voc)
        and is_pow2(n_wid)
        and tok_rows % (2 * n_wid) == 0
        and d_cols % (n_voc // 2) == 0
    )
    per_piece = 0
    if grad_path:
        per_piece = n_voc // 2
        q_cols = d_cols // per_piece
    if grad_path and per_piece == 2:
        c = lax.axis_index("voc") % 2

        def quarter_dots(sel):
            def qdot(rows, piece):
                return jnp.dot(
                    rows,
                    lax.dynamic_slice_in_dim(piece, sel * q_cols, q_cols, axis=1),
                    preferred_element_type=jnp.float32,
                )

            if not chunked:
                return jnp.stack([qdot(dlogits, piece) for piece in table_pieces])
            own = qdot(dlogits, table)
            other = qdot(dlogits[:, :r1], other_chunks[0]) + qdot(dlogits[:, r1:], other_chunks[1])
            return jnp.stack([own, other])

        sent = quarter_dots(1 - c)
        received = lax.ppermute(sent, "voc", [(k, k ^ 1) for k in range(n_voc)])
        blocks = quarter_dots(c) + received
        voc_bits = bit_list("voc", n_voc)
        wid_bits = bit_list("wid", n_wid)
        v = lax.axis_index("voc")
        bits = {voc_bits[-1]: ((v // per_piece) % 2) ^ t}
        for key in wid_bits:
            bits[key] = (lax.axis_index("wid") // key[1]) % 2
        dims = [voc_bits[-1]] + wid_bits[::-1]
        blocks = blocks.reshape(tuple(2 for _ in dims) + (tok_rows // n_wid, q_cols))
        half = tok_rows // n_wid // 2
        rest_voc = voc_bits[1:]
        part_a = halving_steps(blocks[..., :half, :], dims, rest_voc + wid_bits, bits)
        part_b = halving_steps(blocks[..., half:, :], dims, wid_bits[:1] + rest_voc + wid_bits[1:], bits)
        mine = jnp.concatenate([part_a, part_b], axis=0).astype(jnp.bfloat16)
        grad_rows_pos = doubling_gather(mine, "wid").reshape((tok_rows, q_cols))
    elif grad_path:
        stacked = jnp.stack(
            [
                jnp.stack(
                    [
                        jnp.dot(dlogits, piece[:, i * q_cols : (i + 1) * q_cols], preferred_element_type=jnp.float32)
                        for i in range(per_piece)
                    ]
                )
                for piece in table_pieces
            ]
        )
        voc_bits = bit_list("voc", n_voc)
        wid_bits = bit_list("wid", n_wid)
        v = lax.axis_index("voc")
        bits = {key: (v // key[1]) % 2 for key in voc_bits}
        bits[voc_bits[-1]] = ((v // per_piece) % 2) ^ t
        for key in wid_bits:
            bits[key] = (lax.axis_index("wid") // key[1]) % 2
        dims = [voc_bits[-1]] + voc_bits[:-1][::-1] + wid_bits[::-1]
        blocks = stacked.reshape(tuple(2 for _ in dims) + (tok_rows // n_wid, q_cols))
        first = voc_bits[0]
        blocks = halving_steps(blocks, dims, [first], bits)
        dims = [d for d in dims if d != first]
        half = tok_rows // n_wid // 2
        rest_voc = voc_bits[1:]
        part_a = halving_steps(blocks[..., :half, :], dims, rest_voc + wid_bits, bits)
        part_b = halving_steps(blocks[..., half:, :], dims, wid_bits + rest_voc, bits)
        mine = jnp.concatenate([part_a, part_b], axis=0).astype(jnp.bfloat16)
        grad_rows_pos = doubling_gather(mine, "wid").reshape((tok_rows, q_cols))
    else:
        parts = []
        for k, piece in enumerate(table_pieces):
            parts.append(
                lax.dot_general(piece, dlogits, (((0,), (1,)), ((), ())), preferred_element_type=jnp.float32)
            )
        full_rows = jnp.zeros((d_cols * n_tok, tok_rows), jnp.float32)
        for k, part in enumerate(parts):
            full_rows = lax.dynamic_update_slice_in_dim(
                full_rows, part, ((t - k) % n_tok) * d_cols, axis=0
            )
        reduced = lax.psum_scatter(full_rows, "voc", scatter_dimension=0, tiled=True)
        grad_rows_t = lax.psum(reduced, "wid").astype(jnp.bfloat16)

    if grad_rows_pos is not None:
        half_rows = tok_rows // 2
        by_pos = (((0,), (0,)), ((), ()))
        sums_of = []
        for rows, hid in ((grad_rows_pos, hidden), (None, hidden_other)):
            if rows is None:
                rows = [
                    lax.ppermute(grad_rows_pos[i * half_rows : (i + 1) * half_rows], "tok", [(0, 1), (1, 0)])
                    for i in range(2)
                ]
            else:
                rows = [rows[i * half_rows : (i + 1) * half_rows] for i in range(2)]
            dots = [
                lax.dot_general(rows[i], hid[i * half_rows : (i + 1) * half_rows], by_pos, preferred_element_type=jnp.float32)
                for i in range(2)
            ]
            sums_of.append(dots[0] + dots[1])
        grad_proj = sums_of[0] + sums_of[1]
    elif n_tok == 2:
        grad_other = lax.ppermute(grad_rows_t, "tok", [(0, 1), (1, 0)])
        first = t == 0
        grad_all = jnp.where(
            first,
            jnp.concatenate([grad_rows_t, grad_other], axis=1),
            jnp.concatenate([grad_other, grad_rows_t], axis=1),
        )
        hidden_all = jnp.where(
            first,
            jnp.concatenate([hidden, hidden_other], axis=0),
            jnp.concatenate([hidden_other, hidden], axis=0),
        )
        grad_proj = jnp.dot(grad_all, hidden_all, preferred_element_type=jnp.float32)
    else:
        grad_all = lax.all_gather(grad_rows_t, "tok", axis=1, tiled=True)
        hidden_all = lax.all_gather(hidden, "tok", axis=0, tiled=True)
        grad_proj = jnp.dot(grad_all, hidden_all, preferred_element_type=jnp.float32)
    loss = sums[0] / sums[1]
    return (grad_proj, loss)


def solution(mesh):
    return jax.shard_map(
        on_device,
        mesh=mesh,
        in_specs=(P("tok", "wid"), P("voc", "wid"), P(("voc", "wid"), "tok"), P("tok"), P("tok")),
        out_specs=(P("voc", "wid"), P()),
        check_vma=False,
    )
```

```python
import jax
import jax.numpy as jnp
from jax import lax
from jax.sharding import PartitionSpec as P


def tok_pieces(x, n_tok):
    pieces = [x]
    for k in range(1, n_tok):
        perm = [(i, (i + k) % n_tok) for i in range(n_tok)]
        pieces.append(lax.ppermute(x, "tok", perm))
    return pieces


def combine(a, b):
    peak = jnp.maximum(a[0], b[0])
    total = a[1] * jnp.exp(a[0] - peak) + b[1] * jnp.exp(b[0] - peak)
    return jnp.stack([peak, total, a[2] + b[2]])


def butterfly(stats, axes):
    for ax in axes:
        n = lax.axis_size(ax)
        if n & (n - 1):
            gathered = lax.all_gather(stats, ax)
            out = gathered[0]
            for i in range(1, n):
                out = combine(out, gathered[i])
            stats = out
            continue
        b = 1
        while b < n:
            other = lax.ppermute(stats, ax, [(i, i ^ b) for i in range(n)])
            stats = combine(stats, other)
            b *= 2
    return stats


def tree_sum(x, ax):
    n = lax.axis_size(ax)
    if n & (n - 1):
        return lax.psum(x, ax)
    b = 1
    while b < n:
        x = x + lax.ppermute(x, ax, [(i, i ^ b) for i in range(n)])
        b *= 2
    return x


def is_pow2(n):
    return n & (n - 1) == 0


def bit_list(ax, n):
    out = []
    b = 1
    while b < n:
        out.append((ax, b))
        b *= 2
    return out


def halving_steps(x, dims, order, bits=None):
    dims = list(dims)
    for ax, b in order:
        pos = dims.index((ax, b))
        n = lax.axis_size(ax)
        bit = (lax.axis_index(ax) // b) % 2 if bits is None else bits[(ax, b)]
        keep = lax.dynamic_index_in_dim(x, bit, axis=pos, keepdims=False)
        send = lax.dynamic_index_in_dim(x, 1 - bit, axis=pos, keepdims=False)
        x = keep + lax.ppermute(send, ax, [(k, k ^ b) for k in range(n)])
        dims.pop(pos)
    return x


def doubling_gather(x, ax):
    n = lax.axis_size(ax)
    i = lax.axis_index(ax)
    b = n // 2
    lead = 0
    while b >= 1:
        other = lax.ppermute(x, ax, [(k, k ^ b) for k in range(n)])
        bit = (i // b) % 2
        x = jnp.where(bit == 0, jnp.stack([x, other], axis=lead), jnp.stack([other, x], axis=lead))
        lead += 1
        b //= 2
    return x.reshape((n,) + x.shape[lead:])


def on_device(hidden, proj, table, targets, valid):
    tok_rows = hidden.shape[0]
    block_rows = table.shape[0]
    n_tok = lax.axis_size("tok")
    t = lax.axis_index("tok")
    d_cols = table.shape[1]

    table_pieces = tok_pieces(table, n_tok)
    if n_tok == 2:
        hidden_other = lax.ppermute(hidden, "tok", [(0, 1), (1, 0)])

    partial_value = lax.dot_general(
        hidden, proj, (((1,), (1,)), ((), ())), preferred_element_type=jnp.float32
    )
    summed = lax.psum(partial_value, "wid")
    if is_pow2(lax.axis_size("voc")):
        quarters = doubling_gather(summed.astype(jnp.bfloat16), "voc")
        projected = quarters.transpose(1, 0, 2).reshape((tok_rows, -1))
    else:
        projected = lax.all_gather(summed.astype(jnp.bfloat16), "voc", axis=1, tiled=True)

    logits = None
    for k, piece in enumerate(table_pieces):
        cols = lax.dynamic_slice_in_dim(projected, ((t - k) % n_tok) * d_cols, d_cols, axis=1)
        part = lax.dot_general(
            piece, cols, (((1,), (1,)), ((), ())), preferred_element_type=jnp.float32
        )
        logits = part if logits is None else logits + part

    block_base = (lax.axis_index("voc") * lax.axis_size("wid") + lax.axis_index("wid")) * block_rows
    local_ids = targets - block_base
    is_target = local_ids[None, :] == lax.broadcasted_iota(jnp.int32, (block_rows, tok_rows), 0)
    picked_here = jnp.sum(jnp.where(is_target, logits, 0.0), axis=0)
    peak_here = jnp.max(logits, axis=0)
    exp_here = jnp.sum(jnp.exp(logits - peak_here[None, :]), axis=0)
    weight = valid.astype(jnp.float32)

    stats = jnp.stack([peak_here, exp_here, picked_here])
    stats = butterfly(stats, ("voc", "wid"))
    log_total = stats[0] + jnp.log(stats[1])
    picked = stats[2]
    sums = jnp.dot(
        jnp.stack([weight * (log_total - picked), weight]),
        jnp.ones((tok_rows,), jnp.float32),
        precision=lax.Precision.HIGHEST,
    )
    sums = tree_sum(sums, "tok")

    dlogits = (
        (weight[None, :] * (jnp.exp(logits - log_total[None, :]) - is_target.astype(jnp.float32)))
        .astype(jnp.bfloat16)
        .T
    )

    n_voc, n_wid = lax.axis_size("voc"), lax.axis_size("wid")
    grad_rows_pos = None
    grad_path = (
        n_tok == 2
        and n_voc >= 2
        and is_pow2(n_voc)
        and is_pow2(n_wid)
        and tok_rows % (2 * n_wid) == 0
        and d_cols % (n_voc // 2) == 0
    )
    per_piece = 0
    if grad_path:
        per_piece = n_voc // 2
        q_cols = d_cols // per_piece
    if grad_path and per_piece == 2:
        c = lax.axis_index("voc") % 2

        def quarter_dots(sel):
            return jnp.stack(
                [
                    jnp.dot(
                        dlogits,
                        lax.dynamic_slice_in_dim(piece, sel * q_cols, q_cols, axis=1),
                        preferred_element_type=jnp.float32,
                    )
                    for piece in table_pieces
                ]
            )

        sent = quarter_dots(1 - c)
        received = lax.ppermute(sent, "voc", [(k, k ^ 1) for k in range(n_voc)])
        blocks = quarter_dots(c) + received
        voc_bits = bit_list("voc", n_voc)
        wid_bits = bit_list("wid", n_wid)
        v = lax.axis_index("voc")
        bits = {voc_bits[-1]: ((v // per_piece) % 2) ^ t}
        for key in wid_bits:
            bits[key] = (lax.axis_index("wid") // key[1]) % 2
        dims = [voc_bits[-1]] + wid_bits[::-1]
        blocks = blocks.reshape(tuple(2 for _ in dims) + (tok_rows // n_wid, q_cols))
        half = tok_rows // n_wid // 2
        rest_voc = voc_bits[1:]
        part_a = halving_steps(blocks[..., :half, :], dims, rest_voc + wid_bits, bits)
        part_b = halving_steps(blocks[..., half:, :], dims, wid_bits[:1] + rest_voc + wid_bits[1:], bits)
        mine = jnp.concatenate([part_a, part_b], axis=0).astype(jnp.bfloat16)
        grad_rows_pos = doubling_gather(mine, "wid").reshape((tok_rows, q_cols))
    elif grad_path:
        stacked = jnp.stack(
            [
                jnp.stack(
                    [
                        jnp.dot(dlogits, piece[:, i * q_cols : (i + 1) * q_cols], preferred_element_type=jnp.float32)
                        for i in range(per_piece)
                    ]
                )
                for piece in table_pieces
            ]
        )
        voc_bits = bit_list("voc", n_voc)
        wid_bits = bit_list("wid", n_wid)
        v = lax.axis_index("voc")
        bits = {key: (v // key[1]) % 2 for key in voc_bits}
        bits[voc_bits[-1]] = ((v // per_piece) % 2) ^ t
        for key in wid_bits:
            bits[key] = (lax.axis_index("wid") // key[1]) % 2
        dims = [voc_bits[-1]] + voc_bits[:-1][::-1] + wid_bits[::-1]
        blocks = stacked.reshape(tuple(2 for _ in dims) + (tok_rows // n_wid, q_cols))
        first = voc_bits[0]
        blocks = halving_steps(blocks, dims, [first], bits)
        dims = [d for d in dims if d != first]
        half = tok_rows // n_wid // 2
        rest_voc = voc_bits[1:]
        part_a = halving_steps(blocks[..., :half, :], dims, rest_voc + wid_bits, bits)
        part_b = halving_steps(blocks[..., half:, :], dims, wid_bits + rest_voc, bits)
        mine = jnp.concatenate([part_a, part_b], axis=0).astype(jnp.bfloat16)
        grad_rows_pos = doubling_gather(mine, "wid").reshape((tok_rows, q_cols))
    else:
        parts = []
        for k, piece in enumerate(table_pieces):
            parts.append(
                lax.dot_general(piece, dlogits, (((0,), (1,)), ((), ())), preferred_element_type=jnp.float32)
            )
        full_rows = jnp.zeros((d_cols * n_tok, tok_rows), jnp.float32)
        for k, part in enumerate(parts):
            full_rows = lax.dynamic_update_slice_in_dim(
                full_rows, part, ((t - k) % n_tok) * d_cols, axis=0
            )
        reduced = lax.psum_scatter(full_rows, "voc", scatter_dimension=0, tiled=True)
        grad_rows_t = lax.psum(reduced, "wid").astype(jnp.bfloat16)

    if grad_rows_pos is not None:
        half_rows = tok_rows // 2
        by_pos = (((0,), (0,)), ((), ()))
        sums_of = []
        for rows, hid in ((grad_rows_pos, hidden), (None, hidden_other)):
            if rows is None:
                rows = [
                    lax.ppermute(grad_rows_pos[i * half_rows : (i + 1) * half_rows], "tok", [(0, 1), (1, 0)])
                    for i in range(2)
                ]
            else:
                rows = [rows[i * half_rows : (i + 1) * half_rows] for i in range(2)]
            dots = [
                lax.dot_general(rows[i], hid[i * half_rows : (i + 1) * half_rows], by_pos, preferred_element_type=jnp.float32)
                for i in range(2)
            ]
            sums_of.append(dots[0] + dots[1])
        grad_proj = sums_of[0] + sums_of[1]
    elif n_tok == 2:
        grad_other = lax.ppermute(grad_rows_t, "tok", [(0, 1), (1, 0)])
        first = t == 0
        grad_all = jnp.where(
            first,
            jnp.concatenate([grad_rows_t, grad_other], axis=1),
            jnp.concatenate([grad_other, grad_rows_t], axis=1),
        )
        hidden_all = jnp.where(
            first,
            jnp.concatenate([hidden, hidden_other], axis=0),
            jnp.concatenate([hidden_other, hidden], axis=0),
        )
        grad_proj = jnp.dot(grad_all, hidden_all, preferred_element_type=jnp.float32)
    else:
        grad_all = lax.all_gather(grad_rows_t, "tok", axis=1, tiled=True)
        hidden_all = lax.all_gather(hidden, "tok", axis=0, tiled=True)
        grad_proj = jnp.dot(grad_all, hidden_all, preferred_element_type=jnp.float32)
    loss = sums[0] / sums[1]
    return (grad_proj, loss)


def solution(mesh):
    return jax.shard_map(
        on_device,
        mesh=mesh,
        in_specs=(P("tok", "wid"), P("voc", "wid"), P(("voc", "wid"), "tok"), P("tok"), P("tok")),
        out_specs=(P("voc", "wid"), P()),
        check_vma=False,
    )
```

```python
import jax
import jax.numpy as jnp
from jax import lax
from jax.sharding import PartitionSpec as P


def tok_pieces(x, n_tok):
    pieces = [x]
    for k in range(1, n_tok):
        perm = [(i, (i + k) % n_tok) for i in range(n_tok)]
        pieces.append(lax.ppermute(x, "tok", perm))
    return pieces


def combine(a, b):
    peak = jnp.maximum(a[0], b[0])
    total = a[1] * jnp.exp(a[0] - peak) + b[1] * jnp.exp(b[0] - peak)
    return jnp.stack([peak, total, a[2] + b[2]])


def butterfly(stats, axes):
    for ax in axes:
        n = lax.axis_size(ax)
        if n & (n - 1):
            gathered = lax.all_gather(stats, ax)
            out = gathered[0]
            for i in range(1, n):
                out = combine(out, gathered[i])
            stats = out
            continue
        b = 1
        while b < n:
            other = lax.ppermute(stats, ax, [(i, i ^ b) for i in range(n)])
            stats = combine(stats, other)
            b *= 2
    return stats


def tree_sum(x, ax):
    n = lax.axis_size(ax)
    if n & (n - 1):
        return lax.psum(x, ax)
    b = 1
    while b < n:
        x = x + lax.ppermute(x, ax, [(i, i ^ b) for i in range(n)])
        b *= 2
    return x


def is_pow2(n):
    return n & (n - 1) == 0


def bit_list(ax, n):
    out = []
    b = 1
    while b < n:
        out.append((ax, b))
        b *= 2
    return out


def halving_steps(x, dims, order, bits=None):
    dims = list(dims)
    for ax, b in order:
        pos = dims.index((ax, b))
        n = lax.axis_size(ax)
        bit = (lax.axis_index(ax) // b) % 2 if bits is None else bits[(ax, b)]
        terms = x if isinstance(x, tuple) else (x,)
        keep = sum(lax.dynamic_index_in_dim(y, bit, axis=pos, keepdims=False) for y in terms)
        send = sum(lax.dynamic_index_in_dim(y, 1 - bit, axis=pos, keepdims=False) for y in terms)
        x = keep + lax.ppermute(send, ax, [(k, k ^ b) for k in range(n)])
        dims.pop(pos)
    return x


def doubling_gather(x, ax):
    n = lax.axis_size(ax)
    i = lax.axis_index(ax)
    b = n // 2
    lead = 0
    while b >= 1:
        other = lax.ppermute(x, ax, [(k, k ^ b) for k in range(n)])
        bit = (i // b) % 2
        x = jnp.where(bit == 0, jnp.stack([x, other], axis=lead), jnp.stack([other, x], axis=lead))
        lead += 1
        b //= 2
    return x.reshape((n,) + x.shape[lead:])


def on_device(hidden, proj, table, targets, valid):
    tok_rows = hidden.shape[0]
    block_rows = table.shape[0]
    n_tok = lax.axis_size("tok")
    t = lax.axis_index("tok")
    d_cols = table.shape[1]

    table_pieces = tok_pieces(table, n_tok)
    if n_tok == 2:
        hidden_other = lax.ppermute(hidden, "tok", [(0, 1), (1, 0)])

    partial_value = lax.dot_general(
        hidden, proj, (((1,), (1,)), ((), ())), preferred_element_type=jnp.float32
    )
    summed = lax.psum(partial_value, "wid")
    if is_pow2(lax.axis_size("voc")):
        quarters = doubling_gather(summed.astype(jnp.bfloat16), "voc")
        projected = quarters.transpose(1, 0, 2).reshape((tok_rows, -1))
    else:
        projected = lax.all_gather(summed.astype(jnp.bfloat16), "voc", axis=1, tiled=True)

    logits = None
    for k, piece in enumerate(table_pieces):
        cols = lax.dynamic_slice_in_dim(projected, ((t - k) % n_tok) * d_cols, d_cols, axis=1)
        part = lax.dot_general(
            piece, cols, (((1,), (1,)), ((), ())), preferred_element_type=jnp.float32
        )
        logits = part if logits is None else logits + part

    block_base = (lax.axis_index("voc") * lax.axis_size("wid") + lax.axis_index("wid")) * block_rows
    local_ids = targets - block_base
    is_target = local_ids[None, :] == lax.broadcasted_iota(jnp.int32, (block_rows, tok_rows), 0)
    picked_here = jnp.sum(jnp.where(is_target, logits, 0.0), axis=0)
    peak_here = jnp.max(logits, axis=0)
    exp_here = jnp.sum(jnp.exp(logits - peak_here[None, :]), axis=0)
    weight = valid.astype(jnp.float32)

    stats = jnp.stack([peak_here, exp_here, picked_here])
    stats = butterfly(stats, ("voc", "wid"))
    log_total = stats[0] + jnp.log(stats[1])
    picked = stats[2]
    sums = jnp.stack([jnp.sum(weight * (log_total - picked)), jnp.sum(weight)])
    sums = tree_sum(sums, "tok")

    dlogits = (
        (weight[None, :] * (jnp.exp(logits - log_total[None, :]) - is_target.astype(jnp.float32)))
        .astype(jnp.bfloat16)
        .T
    )

    n_voc, n_wid = lax.axis_size("voc"), lax.axis_size("wid")
    grad_rows_pos = None
    grad_path = (
        n_tok == 2
        and n_voc >= 2
        and is_pow2(n_voc)
        and is_pow2(n_wid)
        and tok_rows % (2 * n_wid) == 0
        and d_cols % (n_voc // 2) == 0
    )
    per_piece = 0
    if grad_path:
        per_piece = n_voc // 2
        q_cols = d_cols // per_piece
    if grad_path and per_piece == 2:
        c = lax.axis_index("voc") % 2

        def quarter_dots(sel):
            return jnp.stack(
                [
                    jnp.dot(
                        dlogits,
                        lax.dynamic_slice_in_dim(piece, sel * q_cols, q_cols, axis=1),
                        preferred_element_type=jnp.float32,
                    )
                    for piece in table_pieces
                ]
            )

        sent = quarter_dots(1 - c)
        received = lax.ppermute(sent, "voc", [(k, k ^ 1) for k in range(n_voc)])
        kept = quarter_dots(c)
        voc_bits = bit_list("voc", n_voc)
        wid_bits = bit_list("wid", n_wid)
        v = lax.axis_index("voc")
        bits = {voc_bits[-1]: ((v // per_piece) % 2) ^ t}
        for key in wid_bits:
            bits[key] = (lax.axis_index("wid") // key[1]) % 2
        dims = [voc_bits[-1]] + wid_bits[::-1]
        shape = tuple(2 for _ in dims) + (tok_rows // n_wid, q_cols)
        kept = kept.reshape(shape)
        received = received.reshape(shape)
        half = tok_rows // n_wid // 2
        rest_voc = voc_bits[1:]
        part_a = halving_steps(
            (kept[..., :half, :], received[..., :half, :]), dims, rest_voc + wid_bits, bits
        )
        part_b = halving_steps(
            (kept[..., half:, :], received[..., half:, :]), dims, wid_bits[:1] + rest_voc + wid_bits[1:], bits
        )
        mine = jnp.concatenate([part_a, part_b], axis=0).astype(jnp.bfloat16)
        grad_rows_pos = doubling_gather(mine, "wid").reshape((tok_rows, q_cols))
    elif grad_path:
        stacked = jnp.stack(
            [
                jnp.stack(
                    [
                        jnp.dot(dlogits, piece[:, i * q_cols : (i + 1) * q_cols], preferred_element_type=jnp.float32)
                        for i in range(per_piece)
                    ]
                )
                for piece in table_pieces
            ]
        )
        voc_bits = bit_list("voc", n_voc)
        wid_bits = bit_list("wid", n_wid)
        v = lax.axis_index("voc")
        bits = {key: (v // key[1]) % 2 for key in voc_bits}
        bits[voc_bits[-1]] = ((v // per_piece) % 2) ^ t
        for key in wid_bits:
            bits[key] = (lax.axis_index("wid") // key[1]) % 2
        dims = [voc_bits[-1]] + voc_bits[:-1][::-1] + wid_bits[::-1]
        blocks = stacked.reshape(tuple(2 for _ in dims) + (tok_rows // n_wid, q_cols))
        first = voc_bits[0]
        blocks = halving_steps(blocks, dims, [first], bits)
        dims = [d for d in dims if d != first]
        half = tok_rows // n_wid // 2
        rest_voc = voc_bits[1:]
        part_a = halving_steps(blocks[..., :half, :], dims, rest_voc + wid_bits, bits)
        part_b = halving_steps(blocks[..., half:, :], dims, wid_bits + rest_voc, bits)
        mine = jnp.concatenate([part_a, part_b], axis=0).astype(jnp.bfloat16)
        grad_rows_pos = doubling_gather(mine, "wid").reshape((tok_rows, q_cols))
    else:
        parts = []
        for k, piece in enumerate(table_pieces):
            parts.append(
                lax.dot_general(piece, dlogits, (((0,), (1,)), ((), ())), preferred_element_type=jnp.float32)
            )
        full_rows = jnp.zeros((d_cols * n_tok, tok_rows), jnp.float32)
        for k, part in enumerate(parts):
            full_rows = lax.dynamic_update_slice_in_dim(
                full_rows, part, ((t - k) % n_tok) * d_cols, axis=0
            )
        reduced = lax.psum_scatter(full_rows, "voc", scatter_dimension=0, tiled=True)
        grad_rows_t = lax.psum(reduced, "wid").astype(jnp.bfloat16)

    if grad_rows_pos is not None:
        half_rows = tok_rows // 2
        by_pos = (((0,), (0,)), ((), ()))
        sums_of = []
        for rows, hid in ((grad_rows_pos, hidden), (None, hidden_other)):
            if rows is None:
                rows = [
                    lax.ppermute(grad_rows_pos[i * half_rows : (i + 1) * half_rows], "tok", [(0, 1), (1, 0)])
                    for i in range(2)
                ]
            else:
                rows = [rows[i * half_rows : (i + 1) * half_rows] for i in range(2)]
            dots = [
                lax.dot_general(rows[i], hid[i * half_rows : (i + 1) * half_rows], by_pos, preferred_element_type=jnp.float32)
                for i in range(2)
            ]
            sums_of.append(dots[0] + dots[1])
        grad_proj = sums_of[0] + sums_of[1]
    elif n_tok == 2:
        grad_other = lax.ppermute(grad_rows_t, "tok", [(0, 1), (1, 0)])
        first = t == 0
        grad_all = jnp.where(
            first,
            jnp.concatenate([grad_rows_t, grad_other], axis=1),
            jnp.concatenate([grad_other, grad_rows_t], axis=1),
        )
        hidden_all = jnp.where(
            first,
            jnp.concatenate([hidden, hidden_other], axis=0),
            jnp.concatenate([hidden_other, hidden], axis=0),
        )
        grad_proj = jnp.dot(grad_all, hidden_all, preferred_element_type=jnp.float32)
    else:
        grad_all = lax.all_gather(grad_rows_t, "tok", axis=1, tiled=True)
        hidden_all = lax.all_gather(hidden, "tok", axis=0, tiled=True)
        grad_proj = jnp.dot(grad_all, hidden_all, preferred_element_type=jnp.float32)
    loss = sums[0] / sums[1]
    return (grad_proj, loss)


def solution(mesh):
    return jax.shard_map(
        on_device,
        mesh=mesh,
        in_specs=(P("tok", "wid"), P("voc", "wid"), P(("voc", "wid"), "tok"), P("tok"), P("tok")),
        out_specs=(P("voc", "wid"), P()),
        check_vma=False,
    )
```

```python
import jax
import jax.numpy as jnp
from jax import lax
from jax.sharding import PartitionSpec as P


def tok_pieces(x, n_tok):
    pieces = [x]
    for k in range(1, n_tok):
        perm = [(i, (i + k) % n_tok) for i in range(n_tok)]
        pieces.append(lax.ppermute(x, "tok", perm))
    return pieces


def combine(a, b):
    peak = jnp.maximum(a[0], b[0])
    total = a[1] * jnp.exp(a[0] - peak) + b[1] * jnp.exp(b[0] - peak)
    return jnp.stack([peak, total, a[2] + b[2]])


def butterfly(stats, axes):
    for ax in axes:
        n = lax.axis_size(ax)
        if n & (n - 1):
            gathered = lax.all_gather(stats, ax)
            out = gathered[0]
            for i in range(1, n):
                out = combine(out, gathered[i])
            stats = out
            continue
        b = 1
        while b < n:
            other = lax.ppermute(stats, ax, [(i, i ^ b) for i in range(n)])
            stats = combine(stats, other)
            b *= 2
    return stats


def tree_sum(x, ax):
    n = lax.axis_size(ax)
    if n & (n - 1):
        return lax.psum(x, ax)
    b = 1
    while b < n:
        x = x + lax.ppermute(x, ax, [(i, i ^ b) for i in range(n)])
        b *= 2
    return x


def is_pow2(n):
    return n & (n - 1) == 0


def bit_list(ax, n):
    out = []
    b = 1
    while b < n:
        out.append((ax, b))
        b *= 2
    return out


def halving_steps(x, dims, order, bits=None):
    dims = list(dims)
    for ax, b in order:
        pos = dims.index((ax, b))
        n = lax.axis_size(ax)
        bit = (lax.axis_index(ax) // b) % 2 if bits is None else bits[(ax, b)]
        terms = x if isinstance(x, tuple) else (x,)
        keep = sum(lax.dynamic_index_in_dim(y, bit, axis=pos, keepdims=False) for y in terms)
        send = sum(lax.dynamic_index_in_dim(y, 1 - bit, axis=pos, keepdims=False) for y in terms)
        x = keep + lax.ppermute(send, ax, [(k, k ^ b) for k in range(n)])
        dims.pop(pos)
    return x


def doubling_gather(x, ax):
    n = lax.axis_size(ax)
    i = lax.axis_index(ax)
    b = n // 2
    lead = 0
    while b >= 1:
        other = lax.ppermute(x, ax, [(k, k ^ b) for k in range(n)])
        bit = (i // b) % 2
        x = jnp.where(bit == 0, jnp.stack([x, other], axis=lead), jnp.stack([other, x], axis=lead))
        lead += 1
        b //= 2
    return x.reshape((n,) + x.shape[lead:])


def on_device(hidden, proj, table, targets, valid):
    tok_rows = hidden.shape[0]
    block_rows = table.shape[0]
    n_tok = lax.axis_size("tok")
    t = lax.axis_index("tok")
    d_cols = table.shape[1]

    table_pieces = tok_pieces(table, n_tok)
    if n_tok == 2:
        hidden_other = lax.ppermute(hidden, "tok", [(0, 1), (1, 0)])

    partial_value = lax.dot_general(
        hidden, proj, (((1,), (1,)), ((), ())), preferred_element_type=jnp.float32
    )
    summed = lax.psum(partial_value, "wid")
    if is_pow2(lax.axis_size("voc")):
        quarters = doubling_gather(summed.astype(jnp.bfloat16), "voc")
        projected = quarters.transpose(1, 0, 2).reshape((tok_rows, -1))
    else:
        projected = lax.all_gather(summed.astype(jnp.bfloat16), "voc", axis=1, tiled=True)

    logits = None
    for k, piece in enumerate(table_pieces):
        cols = lax.dynamic_slice_in_dim(projected, ((t - k) % n_tok) * d_cols, d_cols, axis=1)
        part = lax.dot_general(
            piece, cols, (((1,), (1,)), ((), ())), preferred_element_type=jnp.float32
        )
        logits = part if logits is None else logits + part

    block_base = (lax.axis_index("voc") * lax.axis_size("wid") + lax.axis_index("wid")) * block_rows
    local_ids = targets - block_base
    is_target = local_ids[None, :] == lax.broadcasted_iota(jnp.int32, (block_rows, tok_rows), 0)
    picked_here = jnp.sum(jnp.where(is_target, logits, 0.0), axis=0)
    peak_here = jnp.max(logits, axis=0)
    exp_here = jnp.sum(jnp.exp(logits - peak_here[None, :]), axis=0)
    weight = valid.astype(jnp.float32)

    stats = jnp.stack([peak_here, exp_here, picked_here])
    stats = butterfly(stats, ("voc", "wid"))
    log_total = stats[0] + jnp.log(stats[1])
    picked = stats[2]
    sums = jnp.stack([jnp.sum(weight * (log_total - picked)), jnp.sum(weight)])
    sums = tree_sum(sums, "tok")

    dlogits = (
        (weight[None, :] * (jnp.exp(logits - log_total[None, :]) - is_target.astype(jnp.float32)))
        .astype(jnp.bfloat16)
        .T
    )

    n_voc, n_wid = lax.axis_size("voc"), lax.axis_size("wid")
    grad_rows_pos = None
    grad_path = (
        n_tok == 2
        and n_voc >= 2
        and is_pow2(n_voc)
        and is_pow2(n_wid)
        and tok_rows % (2 * n_wid) == 0
        and d_cols % (n_voc // 2) == 0
    )
    per_piece = 0
    if grad_path:
        per_piece = n_voc // 2
        q_cols = d_cols // per_piece
    if grad_path and per_piece == 2:
        c = lax.axis_index("voc") % 2

        def quarter_dots(sel):
            return jnp.stack(
                [
                    jnp.dot(
                        dlogits,
                        lax.dynamic_slice_in_dim(piece, sel * q_cols, q_cols, axis=1),
                        preferred_element_type=jnp.float32,
                    )
                    for piece in table_pieces
                ]
            )

        sent = quarter_dots(1 - c)
        received = lax.ppermute(sent, "voc", [(k, k ^ 1) for k in range(n_voc)])
        kept = quarter_dots(c)
        voc_bits = bit_list("voc", n_voc)
        wid_bits = bit_list("wid", n_wid)
        v = lax.axis_index("voc")
        bits = {voc_bits[-1]: ((v // per_piece) % 2) ^ t}
        for key in wid_bits:
            bits[key] = (lax.axis_index("wid") // key[1]) % 2
        dims = [voc_bits[-1]] + wid_bits[::-1]
        shape = tuple(2 for _ in dims) + (tok_rows // n_wid, q_cols)
        kept = kept.reshape(shape)
        received = received.reshape(shape)
        half = tok_rows // n_wid // 2
        rest_voc = voc_bits[1:]
        part_a = halving_steps(
            (kept[..., :half, :], received[..., :half, :]), dims, rest_voc + wid_bits, bits
        )
        part_b = halving_steps(
            (kept[..., half:, :], received[..., half:, :]), dims, wid_bits[:1] + rest_voc + wid_bits[1:], bits
        )
        mine = jnp.concatenate([part_a, part_b], axis=0).astype(jnp.bfloat16)
        grad_rows_pos = doubling_gather(mine, "wid").reshape((tok_rows, q_cols))
    elif grad_path:
        stacked = jnp.stack(
            [
                jnp.stack(
                    [
                        jnp.dot(dlogits, piece[:, i * q_cols : (i + 1) * q_cols], preferred_element_type=jnp.float32)
                        for i in range(per_piece)
                    ]
                )
                for piece in table_pieces
            ]
        )
        voc_bits = bit_list("voc", n_voc)
        wid_bits = bit_list("wid", n_wid)
        v = lax.axis_index("voc")
        bits = {key: (v // key[1]) % 2 for key in voc_bits}
        bits[voc_bits[-1]] = ((v // per_piece) % 2) ^ t
        for key in wid_bits:
            bits[key] = (lax.axis_index("wid") // key[1]) % 2
        dims = [voc_bits[-1]] + voc_bits[:-1][::-1] + wid_bits[::-1]
        blocks = stacked.reshape(tuple(2 for _ in dims) + (tok_rows // n_wid, q_cols))
        first = voc_bits[0]
        blocks = halving_steps(blocks, dims, [first], bits)
        dims = [d for d in dims if d != first]
        half = tok_rows // n_wid // 2
        rest_voc = voc_bits[1:]
        part_a = halving_steps(blocks[..., :half, :], dims, rest_voc + wid_bits, bits)
        part_b = halving_steps(blocks[..., half:, :], dims, wid_bits + rest_voc, bits)
        mine = jnp.concatenate([part_a, part_b], axis=0).astype(jnp.bfloat16)
        grad_rows_pos = doubling_gather(mine, "wid").reshape((tok_rows, q_cols))
    else:
        parts = []
        for k, piece in enumerate(table_pieces):
            parts.append(
                lax.dot_general(piece, dlogits, (((0,), (1,)), ((), ())), preferred_element_type=jnp.float32)
            )
        full_rows = jnp.zeros((d_cols * n_tok, tok_rows), jnp.float32)
        for k, part in enumerate(parts):
            full_rows = lax.dynamic_update_slice_in_dim(
                full_rows, part, ((t - k) % n_tok) * d_cols, axis=0
            )
        reduced = lax.psum_scatter(full_rows, "voc", scatter_dimension=0, tiled=True)
        grad_rows_t = lax.psum(reduced, "wid").astype(jnp.bfloat16)

    if grad_rows_pos is not None:
        half_rows = tok_rows // 2
        by_pos = (((0,), (0,)), ((), ()))
        sums_of = []
        for rows, hid in ((grad_rows_pos, hidden), (None, hidden_other)):
            if rows is None:
                rows = [
                    lax.ppermute(grad_rows_pos[i * half_rows : (i + 1) * half_rows], "tok", [(0, 1), (1, 0)])
                    for i in range(2)
                ]
            else:
                rows = [rows[i * half_rows : (i + 1) * half_rows] for i in range(2)]
            dots = [
                lax.dot_general(rows[i], hid[i * half_rows : (i + 1) * half_rows], by_pos, preferred_element_type=jnp.float32)
                for i in range(2)
            ]
            tok_sum = dots[0] + dots[1]
            if not sums_of:
                tok_sum = lax.optimization_barrier(tok_sum)
            sums_of.append(tok_sum)
        grad_proj = sums_of[0] + sums_of[1]
    elif n_tok == 2:
        grad_other = lax.ppermute(grad_rows_t, "tok", [(0, 1), (1, 0)])
        first = t == 0
        grad_all = jnp.where(
            first,
            jnp.concatenate([grad_rows_t, grad_other], axis=1),
            jnp.concatenate([grad_other, grad_rows_t], axis=1),
        )
        hidden_all = jnp.where(
            first,
            jnp.concatenate([hidden, hidden_other], axis=0),
            jnp.concatenate([hidden_other, hidden], axis=0),
        )
        grad_proj = jnp.dot(grad_all, hidden_all, preferred_element_type=jnp.float32)
    else:
        grad_all = lax.all_gather(grad_rows_t, "tok", axis=1, tiled=True)
        hidden_all = lax.all_gather(hidden, "tok", axis=0, tiled=True)
        grad_proj = jnp.dot(grad_all, hidden_all, preferred_element_type=jnp.float32)
    loss = sums[0] / sums[1]
    return (grad_proj, loss)


def solution(mesh):
    return jax.shard_map(
        on_device,
        mesh=mesh,
        in_specs=(P("tok", "wid"), P("voc", "wid"), P(("voc", "wid"), "tok"), P("tok"), P("tok")),
        out_specs=(P("voc", "wid"), P()),
        check_vma=False,
    )
```

```python
import jax
import jax.numpy as jnp
from jax import lax
from jax.sharding import PartitionSpec as P


def tok_pieces(x, n_tok):
    pieces = [x]
    for k in range(1, n_tok):
        perm = [(i, (i + k) % n_tok) for i in range(n_tok)]
        pieces.append(lax.ppermute(x, "tok", perm))
    return pieces


def combine(a, b):
    peak = jnp.maximum(a[0], b[0])
    total = a[1] * jnp.exp(a[0] - peak) + b[1] * jnp.exp(b[0] - peak)
    return jnp.stack([peak, total, a[2] + b[2]])


def butterfly(stats, axes):
    for ax in axes:
        n = lax.axis_size(ax)
        if n & (n - 1):
            gathered = lax.all_gather(stats, ax)
            out = gathered[0]
            for i in range(1, n):
                out = combine(out, gathered[i])
            stats = out
            continue
        b = 1
        while b < n:
            other = lax.ppermute(stats, ax, [(i, i ^ b) for i in range(n)])
            stats = combine(stats, other)
            b *= 2
    return stats


def tree_sum(x, ax):
    n = lax.axis_size(ax)
    if n & (n - 1):
        return lax.psum(x, ax)
    b = 1
    while b < n:
        x = x + lax.ppermute(x, ax, [(i, i ^ b) for i in range(n)])
        b *= 2
    return x


def is_pow2(n):
    return n & (n - 1) == 0


def bit_list(ax, n):
    out = []
    b = 1
    while b < n:
        out.append((ax, b))
        b *= 2
    return out


def halving_steps(x, dims, order, bits=None):
    dims = list(dims)
    for ax, b in order:
        pos = dims.index((ax, b))
        n = lax.axis_size(ax)
        bit = (lax.axis_index(ax) // b) % 2 if bits is None else bits[(ax, b)]
        terms = x if isinstance(x, tuple) else (x,)
        keep = sum(lax.dynamic_index_in_dim(y, bit, axis=pos, keepdims=False) for y in terms)
        send = sum(lax.dynamic_index_in_dim(y, 1 - bit, axis=pos, keepdims=False) for y in terms)
        x = keep + lax.ppermute(send, ax, [(k, k ^ b) for k in range(n)])
        dims.pop(pos)
    return x


def doubling_gather(x, ax):
    n = lax.axis_size(ax)
    i = lax.axis_index(ax)
    b = n // 2
    lead = 0
    while b >= 1:
        other = lax.ppermute(x, ax, [(k, k ^ b) for k in range(n)])
        bit = (i // b) % 2
        x = jnp.where(bit == 0, jnp.stack([x, other], axis=lead), jnp.stack([other, x], axis=lead))
        lead += 1
        b //= 2
    return x.reshape((n,) + x.shape[lead:])


def on_device(hidden, proj, table, targets, valid):
    tok_rows = hidden.shape[0]
    block_rows = table.shape[0]
    n_tok = lax.axis_size("tok")
    t = lax.axis_index("tok")
    d_cols = table.shape[1]

    table_pieces = tok_pieces(table, n_tok)
    early_hidden = n_tok == 2 and not (
        lax.axis_size("voc") == 4
        and is_pow2(lax.axis_size("wid"))
        and tok_rows % (2 * lax.axis_size("wid")) == 0
        and d_cols % 2 == 0
    )
    if early_hidden:
        hidden_other = lax.ppermute(hidden, "tok", [(0, 1), (1, 0)])

    partial_value = lax.dot_general(
        hidden, proj, (((1,), (1,)), ((), ())), preferred_element_type=jnp.float32
    )
    summed = lax.psum(partial_value, "wid")
    if is_pow2(lax.axis_size("voc")):
        quarters = doubling_gather(summed.astype(jnp.bfloat16), "voc")
        projected = quarters.transpose(1, 0, 2).reshape((tok_rows, -1))
    else:
        projected = lax.all_gather(summed.astype(jnp.bfloat16), "voc", axis=1, tiled=True)

    logits = None
    for k, piece in enumerate(table_pieces):
        cols = lax.dynamic_slice_in_dim(projected, ((t - k) % n_tok) * d_cols, d_cols, axis=1)
        part = lax.dot_general(
            piece, cols, (((1,), (1,)), ((), ())), preferred_element_type=jnp.float32
        )
        logits = part if logits is None else logits + part

    block_base = (lax.axis_index("voc") * lax.axis_size("wid") + lax.axis_index("wid")) * block_rows
    local_ids = targets - block_base
    is_target = local_ids[None, :] == lax.broadcasted_iota(jnp.int32, (block_rows, tok_rows), 0)
    picked_here = jnp.sum(jnp.where(is_target, logits, 0.0), axis=0)
    peak_here = jnp.max(logits, axis=0)
    exp_here = jnp.sum(jnp.exp(logits - peak_here[None, :]), axis=0)
    weight = valid.astype(jnp.float32)

    stats = jnp.stack([peak_here, exp_here, picked_here])
    stats = butterfly(stats, ("voc", "wid"))
    log_total = stats[0] + jnp.log(stats[1])
    picked = stats[2]
    sums = jnp.stack([jnp.sum(weight * (log_total - picked)), jnp.sum(weight)])
    sums = tree_sum(sums, "tok")

    dlogits = (
        (weight[None, :] * (jnp.exp(logits - log_total[None, :]) - is_target.astype(jnp.float32)))
        .astype(jnp.bfloat16)
        .T
    )

    n_voc, n_wid = lax.axis_size("voc"), lax.axis_size("wid")
    grad_rows_pos = None
    grad_path = (
        n_tok == 2
        and n_voc >= 2
        and is_pow2(n_voc)
        and is_pow2(n_wid)
        and tok_rows % (2 * n_wid) == 0
        and d_cols % (n_voc // 2) == 0
    )
    per_piece = 0
    if grad_path:
        per_piece = n_voc // 2
        q_cols = d_cols // per_piece
    if grad_path and per_piece == 2:
        c = lax.axis_index("voc") % 2

        def quarter_dots(sel):
            return jnp.stack(
                [
                    jnp.dot(
                        dlogits,
                        lax.dynamic_slice_in_dim(piece, sel * q_cols, q_cols, axis=1),
                        preferred_element_type=jnp.float32,
                    )
                    for piece in table_pieces
                ]
            )

        sent = quarter_dots(1 - c)
        received = lax.ppermute(sent, "voc", [(k, k ^ 1) for k in range(n_voc)])
        kept = quarter_dots(c)
        hidden_send, kept = lax.optimization_barrier((hidden, kept))
        hidden_other = lax.ppermute(hidden_send, "tok", [(0, 1), (1, 0)])
        voc_bits = bit_list("voc", n_voc)
        wid_bits = bit_list("wid", n_wid)
        v = lax.axis_index("voc")
        bits = {voc_bits[-1]: ((v // per_piece) % 2) ^ t}
        for key in wid_bits:
            bits[key] = (lax.axis_index("wid") // key[1]) % 2
        dims = [voc_bits[-1]] + wid_bits[::-1]
        shape = tuple(2 for _ in dims) + (tok_rows // n_wid, q_cols)
        kept = kept.reshape(shape)
        received = received.reshape(shape)
        half = tok_rows // n_wid // 2
        rest_voc = voc_bits[1:]
        part_a = halving_steps(
            (kept[..., :half, :], received[..., :half, :]), dims, rest_voc + wid_bits, bits
        )
        part_b = halving_steps(
            (kept[..., half:, :], received[..., half:, :]), dims, wid_bits[:1] + rest_voc + wid_bits[1:], bits
        )
        mine = jnp.concatenate([part_a, part_b], axis=0).astype(jnp.bfloat16)
        grad_rows_pos = doubling_gather(mine, "wid").reshape((tok_rows, q_cols))
    elif grad_path:
        stacked = jnp.stack(
            [
                jnp.stack(
                    [
                        jnp.dot(dlogits, piece[:, i * q_cols : (i + 1) * q_cols], preferred_element_type=jnp.float32)
                        for i in range(per_piece)
                    ]
                )
                for piece in table_pieces
            ]
        )
        voc_bits = bit_list("voc", n_voc)
        wid_bits = bit_list("wid", n_wid)
        v = lax.axis_index("voc")
        bits = {key: (v // key[1]) % 2 for key in voc_bits}
        bits[voc_bits[-1]] = ((v // per_piece) % 2) ^ t
        for key in wid_bits:
            bits[key] = (lax.axis_index("wid") // key[1]) % 2
        dims = [voc_bits[-1]] + voc_bits[:-1][::-1] + wid_bits[::-1]
        blocks = stacked.reshape(tuple(2 for _ in dims) + (tok_rows // n_wid, q_cols))
        first = voc_bits[0]
        blocks = halving_steps(blocks, dims, [first], bits)
        dims = [d for d in dims if d != first]
        half = tok_rows // n_wid // 2
        rest_voc = voc_bits[1:]
        part_a = halving_steps(blocks[..., :half, :], dims, rest_voc + wid_bits, bits)
        part_b = halving_steps(blocks[..., half:, :], dims, wid_bits + rest_voc, bits)
        mine = jnp.concatenate([part_a, part_b], axis=0).astype(jnp.bfloat16)
        grad_rows_pos = doubling_gather(mine, "wid").reshape((tok_rows, q_cols))
    else:
        parts = []
        for k, piece in enumerate(table_pieces):
            parts.append(
                lax.dot_general(piece, dlogits, (((0,), (1,)), ((), ())), preferred_element_type=jnp.float32)
            )
        full_rows = jnp.zeros((d_cols * n_tok, tok_rows), jnp.float32)
        for k, part in enumerate(parts):
            full_rows = lax.dynamic_update_slice_in_dim(
                full_rows, part, ((t - k) % n_tok) * d_cols, axis=0
            )
        reduced = lax.psum_scatter(full_rows, "voc", scatter_dimension=0, tiled=True)
        grad_rows_t = lax.psum(reduced, "wid").astype(jnp.bfloat16)

    if grad_rows_pos is not None:
        half_rows = tok_rows // 2
        by_pos = (((0,), (0,)), ((), ()))
        sums_of = []
        for rows, hid in ((grad_rows_pos, hidden), (None, hidden_other)):
            if rows is None:
                rows = [
                    lax.ppermute(grad_rows_pos[i * half_rows : (i + 1) * half_rows], "tok", [(0, 1), (1, 0)])
                    for i in range(2)
                ]
            else:
                rows = [rows[i * half_rows : (i + 1) * half_rows] for i in range(2)]
            dots = [
                lax.dot_general(rows[i], hid[i * half_rows : (i + 1) * half_rows], by_pos, preferred_element_type=jnp.float32)
                for i in range(2)
            ]
            sums_of.append(dots[0] + dots[1])
        grad_proj = sums_of[0] + sums_of[1]
    elif n_tok == 2:
        grad_other = lax.ppermute(grad_rows_t, "tok", [(0, 1), (1, 0)])
        first = t == 0
        grad_all = jnp.where(
            first,
            jnp.concatenate([grad_rows_t, grad_other], axis=1),
            jnp.concatenate([grad_other, grad_rows_t], axis=1),
        )
        hidden_all = jnp.where(
            first,
            jnp.concatenate([hidden, hidden_other], axis=0),
            jnp.concatenate([hidden_other, hidden], axis=0),
        )
        grad_proj = jnp.dot(grad_all, hidden_all, preferred_element_type=jnp.float32)
    else:
        grad_all = lax.all_gather(grad_rows_t, "tok", axis=1, tiled=True)
        hidden_all = lax.all_gather(hidden, "tok", axis=0, tiled=True)
        grad_proj = jnp.dot(grad_all, hidden_all, preferred_element_type=jnp.float32)
    loss = sums[0] / sums[1]
    return (grad_proj, loss)


def solution(mesh):
    return jax.shard_map(
        on_device,
        mesh=mesh,
        in_specs=(P("tok", "wid"), P("voc", "wid"), P(("voc", "wid"), "tok"), P("tok"), P("tok")),
        out_specs=(P("voc", "wid"), P()),
        check_vma=False,
    )
```
